32 devices in a mesh: src: 8 (over z, core), rcv: 4 (over y, x).
Axes of the slice: x: 2, y: 2, z: 4, core: 2. Of those that a mesh axis runs over, the one named last changes fastest.
Arguments:
- spectra: bfloat16 [128, 4, 2, 2048], P(('src', 'rcv')), may hold values from -50 to 50
- valid: int32 [128, 4], P(('src', 'rcv')), may hold values 0 or 1
Outputs:
- correlations: bfloat16 [128, 128, 512], P('src', 'rcv')
The draws below stay inside these ranges and needn't reach their ends.
All inputs are finite; a program needn't handle non-finite values. No bound on the sum of `valid` on one device may be relied on, other than what follows from the above.
Results may differ from the reference program's by a relative error of at most 0.0065.
Values may be sent and summed in bfloat16 or wider, within the bound.
No kernel may reach another device: no remote copies, remote signals or barrier semaphores. Data moves between devices by JAX's collectives and lax.ppermute only.
A program may use at most 64 MiB of HBM per device.

```python
import math
import jax
import jax.numpy as jnp
from jax import lax

CH_DEV = 4
WINDOWS = 4
FREQS = 2048
LAGS = 512
BAND = 32
NSAMP = 7500
SRC_COUNT = 8
RCV_COUNT = 4
CHANNELS = 128


def draw_spectra(key, part):
    first_key, second_key = jax.random.split(key)
    shape = (CHANNELS, WINDOWS, 2, FREQS)
    base = jnp.clip(jax.random.normal(first_key, shape, jnp.float32), -5.0, 5.0)
    exponent = jax.random.uniform(second_key, (CHANNELS, WINDOWS, 1, FREQS // BAND), jnp.float32)
    factor = jnp.repeat(jnp.exp(exponent * math.log(10.0)), BAND, axis=3)
    return (base * factor).astype(jnp.bfloat16)


def place_ends(values, key, least, top_value):
    longest = values.shape.index(max(values.shape))
    spots = []
    for shift in (0, 1):
        where = [jax.random.randint(jax.random.fold_in(key, axis), (), 0, length) for axis, length in enumerate(values.shape)]
        where[longest] = (where[longest] + shift) % values.shape[longest]
        spots.append(tuple(where))
    return values.at[spots[0]].set(least).at[spots[1]].set(top_value)


def setup_inputs(seed: int = 0) -> dict:
    arg_keys = jax.random.split(jax.random.key(seed), 3)
    return {
        "spectra": draw_spectra(jax.random.fold_in(arg_keys[2], 71), 0),
        "valid": place_ends((jax.random.randint(arg_keys[1], (CHANNELS, WINDOWS), 0, 4) < 3).astype(jnp.int32), jax.random.fold_in(arg_keys[1], 1), 0, 1),
    }


epsilon = 1e-06

def whiten_spectra(spectra):
    values = spectra.astype(jnp.float32)
    squares = values[:, :, 0] ** 2 + values[:, :, 1] ** 2
    banded = squares.reshape(squares.shape[0], squares.shape[1], squares.shape[2] // BAND, BAND)
    power = lax.optimization_barrier(jnp.sum(banded, axis=3)) / (2.0 * BAND)
    factor = jnp.repeat(1.0 / jnp.sqrt(power + epsilon), BAND, axis=2)
    return (values * factor[:, :, None, :]).astype(jnp.bfloat16)

def lag_table(freq_count, lag_count):
    bins_index = jnp.arange(freq_count, dtype=jnp.int32)
    shifts = jnp.arange(lag_count, dtype=jnp.int32) - lag_count // 2
    phase = jnp.mod(bins_index[:, None] * shifts[None, :], NSAMP)
    angle = phase.astype(jnp.float32) * (2.0 * math.pi / NSAMP)
    factor = 1.0 / math.sqrt(2.0 * freq_count)
    cosines = (jnp.cos(angle) * factor).astype(jnp.bfloat16)
    sines = (-jnp.sin(angle) * factor).astype(jnp.bfloat16)
    return jnp.concatenate([cosines, sines], axis=0)

def correlate_block(rec_spec, rec_mask, src_spec, src_mask, table):
    rec_vals = rec_spec.astype(jnp.float32)
    src_vals = src_spec.astype(jnp.float32)
    counts = jnp.einsum('iw,qw->iq', rec_mask, src_mask)
    weights = rec_mask[:, None, :] * src_mask[None, :, :] / jnp.maximum(counts, 1.0)[:, :, None]
    real_part = jnp.einsum('iqw,iwf,qwf->iqf', weights, rec_vals[:, :, 0], src_vals[:, :, 0])
    real_part = real_part + jnp.einsum('iqw,iwf,qwf->iqf', weights, rec_vals[:, :, 1], src_vals[:, :, 1])
    imag_part = jnp.einsum('iqw,iwf,qwf->iqf', weights, rec_vals[:, :, 0], src_vals[:, :, 1])
    imag_part = imag_part - jnp.einsum('iqw,iwf,qwf->iqf', weights, rec_vals[:, :, 1], src_vals[:, :, 0])
    stacked = jnp.concatenate([real_part.astype(jnp.bfloat16), imag_part.astype(jnp.bfloat16)], axis=2)
    return jnp.einsum('iqk,kl->iql', stacked.astype(jnp.float32), table.astype(jnp.float32))

def reference(spectra, valid):
    whitened = whiten_spectra(spectra)
    masks = valid.astype(jnp.float32)
    src_spec = whitened.reshape(SRC_COUNT, RCV_COUNT, CH_DEV, WINDOWS, 2, FREQS)
    src_spec = src_spec.transpose(1, 0, 2, 3, 4, 5).reshape(CHANNELS, WINDOWS, 2, FREQS)
    src_mask = masks.reshape(SRC_COUNT, RCV_COUNT, CH_DEV, WINDOWS).transpose(1, 0, 2, 3).reshape(CHANNELS, WINDOWS)
    table = lag_table(FREQS, LAGS)

    def one_group(group):
        return correlate_block(group[0], group[1], src_spec, src_mask, table).astype(jnp.bfloat16)
    grouped = (whitened.reshape(CHANNELS // 8, 8, WINDOWS, 2, FREQS), masks.reshape(CHANNELS // 8, 8, WINDOWS))
    result = lax.map(one_group, grouped)
    return result.reshape(CHANNELS, CHANNELS, LAGS)
```

```python
import math

import jax
import jax.numpy as jnp
from jax import lax
from jax.sharding import PartitionSpec as P

LAGS = 512
BAND = 32
NSAMP = 7500
PAD = 128

epsilon = 1e-06


def whiten_spectra(spectra):
    values = spectra.astype(jnp.float32)
    squares = values[:, :, 0] ** 2 + values[:, :, 1] ** 2
    banded = squares.reshape(squares.shape[0], squares.shape[1], squares.shape[2] // BAND, BAND)
    power = jnp.sum(banded, axis=3) / (2.0 * BAND)
    factor = jnp.repeat(1.0 / jnp.sqrt(power + epsilon), BAND, axis=2)
    return (values * factor[:, :, None, :]).astype(jnp.bfloat16)


def lag_table(freq_count, lag_count):
    step = 64
    shifts = jnp.arange(lag_count, dtype=jnp.int32) - lag_count // 2
    hi = jnp.arange(freq_count // step, dtype=jnp.int32) * step
    lo = jnp.arange(step, dtype=jnp.int32)
    scale = 2.0 * math.pi / NSAMP
    angle_hi = jnp.mod(hi[:, None] * shifts[None, :], NSAMP).astype(jnp.float32) * scale
    angle_lo = jnp.mod(lo[:, None] * shifts[None, :], NSAMP).astype(jnp.float32) * scale
    cos_hi, sin_hi = jnp.cos(angle_hi)[:, None, :], jnp.sin(angle_hi)[:, None, :]
    cos_lo, sin_lo = jnp.cos(angle_lo)[None, :, :], jnp.sin(angle_lo)[None, :, :]
    factor = 1.0 / math.sqrt(2.0 * freq_count)
    cosines = (cos_hi * cos_lo - sin_hi * sin_lo) * factor
    sines = (sin_hi * cos_lo + cos_hi * sin_lo) * (-factor)
    cosines = cosines.reshape(freq_count, lag_count).astype(jnp.bfloat16)
    sines = sines.reshape(freq_count, lag_count).astype(jnp.bfloat16)
    return jnp.stack([cosines, sines], axis=0)


def pack(whitened, mask):
    channels = whitened.shape[0]
    flat = whitened.reshape(channels, -1)
    tail = jnp.zeros((channels, PAD), jnp.bfloat16).at[:, : mask.shape[1]].set(mask)
    return jnp.concatenate([flat, tail], axis=1)


def unpack(packed, windows, freqs):
    channels = packed.shape[0]
    body = packed[:, : windows * 2 * freqs].reshape(channels, windows, 2, freqs)
    mask = packed[:, windows * 2 * freqs : windows * 2 * freqs + windows].astype(jnp.float32)
    return body, mask


def local(spectra, valid):
    channels, windows, _, freqs = spectra.shape
    table = lag_table(freqs, LAGS)
    mask_wire = valid.astype(jnp.bfloat16)
    whitened = whiten_spectra(spectra)
    packed = pack(whitened, mask_wire)
    rec_packed = lax.all_gather(packed, "rcv", axis=0, tiled=True)
    src_packed = lax.all_gather(packed, "src", axis=0, tiled=True)
    rec_spec, rec_mask = unpack(rec_packed, windows, freqs)
    src_spec, src_mask = unpack(src_packed, windows, freqs)

    counts = jnp.dot(rec_mask, src_mask.T, preferred_element_type=jnp.float32)
    inverse = 1.0 / jnp.maximum(counts, 1.0)
    rec = rec_spec.astype(jnp.float32) * rec_mask[:, :, None, None]
    src = src_spec.astype(jnp.float32) * src_mask[:, :, None, None]
    ra, rb = rec[:, :, 0][:, None], rec[:, :, 1][:, None]
    sa, sb = src[:, :, 0][None], src[:, :, 1][None]
    real_part = jnp.sum(sa * ra + sb * rb, axis=2) * inverse[:, :, None]
    imag_part = jnp.sum(sb * ra - sa * rb, axis=2) * inverse[:, :, None]
    stacked = jnp.stack(
        [real_part.astype(jnp.bfloat16), imag_part.astype(jnp.bfloat16)], axis=2
    )
    out = jnp.einsum("iqpf,pfl->iql", stacked, table, preferred_element_type=jnp.float32)
    return out.astype(jnp.bfloat16)


def solution(mesh):
    return jax.shard_map(
        local,
        mesh=mesh,
        in_specs=(P(("src", "rcv"), None, None, None), P(("src", "rcv"), None)),
        out_specs=P("src", "rcv", None),
        check_vma=False,
    )
```

```python
import functools
import math

import jax
import jax.numpy as jnp
from jax import lax
from jax.experimental import pallas as pl
from jax.experimental.pallas import tpu as pltpu
from jax.sharding import PartitionSpec as P

LAGS = 512
BAND = 32
NSAMP = 7500
PAD = 128

epsilon = 1e-06


def whiten_spectra(spectra):
    values = spectra.astype(jnp.float32)
    squares = values[:, :, 0] ** 2 + values[:, :, 1] ** 2
    banded = squares.reshape(squares.shape[0], squares.shape[1], squares.shape[2] // BAND, BAND)
    power = jnp.sum(banded, axis=3) / (2.0 * BAND)
    factor = jnp.repeat(1.0 / jnp.sqrt(power + epsilon), BAND, axis=2)
    return (values * factor[:, :, None, :]).astype(jnp.bfloat16)


def lag_table(freq_count, lag_count):
    step = 64
    shifts = jnp.arange(lag_count, dtype=jnp.int32) - lag_count // 2
    hi = jnp.arange(freq_count // step, dtype=jnp.int32) * step
    lo = jnp.arange(step, dtype=jnp.int32)
    scale = 2.0 * math.pi / NSAMP
    angle_hi = jnp.mod(hi[:, None] * shifts[None, :], NSAMP).astype(jnp.float32) * scale
    angle_lo = jnp.mod(lo[:, None] * shifts[None, :], NSAMP).astype(jnp.float32) * scale
    cos_hi, sin_hi = jnp.cos(angle_hi)[:, None, :], jnp.sin(angle_hi)[:, None, :]
    cos_lo, sin_lo = jnp.cos(angle_lo)[None, :, :], jnp.sin(angle_lo)[None, :, :]
    factor = 1.0 / math.sqrt(2.0 * freq_count)
    cosines = (cos_hi * cos_lo - sin_hi * sin_lo) * factor
    sines = (sin_hi * cos_lo + cos_hi * sin_lo) * (-factor)
    cosines = cosines.reshape(freq_count, lag_count).astype(jnp.bfloat16)
    sines = sines.reshape(freq_count, lag_count).astype(jnp.bfloat16)
    return jnp.stack([cosines, sines], axis=0)


def pack(whitened, mask):
    channels = whitened.shape[0]
    flat = whitened.reshape(channels, -1)
    tail = jnp.zeros((channels, PAD), jnp.bfloat16).at[:, : mask.shape[1]].set(mask)
    return jnp.concatenate([flat, tail], axis=1)


def cross_kernel(rec_ref, src_ref, tab_ref, out_ref, srcf, recf, rtails, cross, *, windows, freqs, group, chunk):
    step = pl.program_id(0)
    nsrc = src_ref.shape[0]
    body = windows * 2 * freqs
    width = 2 * freqs

    @pl.when(step == 0)
    def _():
        smask = src_ref[:, body : body + PAD].astype(jnp.float32)
        rmask = rec_ref[:, body : body + PAD].astype(jnp.float32)
        rtails[...] = rmask
        for w in range(windows):
            cols = slice(w * width, (w + 1) * width)
            srcf[:, cols] = src_ref[:, cols].astype(jnp.float32) * smask[:, w : w + 1]
            recf[:, cols] = rec_ref[:, cols].astype(jnp.float32) * rmask[:, w : w + 1]

    smask = src_ref[:, body : body + PAD].astype(jnp.float32)

    def per_receiver(j, carry):
        i = step * group + j
        rtail = rtails[pl.ds(i, 1), :]
        count = jnp.sum(smask * rtail, axis=1, keepdims=True)
        inverse = 1.0 / jnp.maximum(count, 1.0)
        rows = pl.ds(pl.multiple_of(j * nsrc, nsrc), nsrc)
        for c in range(freqs // chunk):
            real = jnp.zeros((nsrc, chunk), jnp.float32)
            imag = jnp.zeros((nsrc, chunk), jnp.float32)
            for w in range(windows):
                a0 = w * width + c * chunk
                b0 = a0 + freqs
                sa = srcf[:, a0 : a0 + chunk]
                sb = srcf[:, b0 : b0 + chunk]
                ra = recf[pl.ds(i, 1), a0 : a0 + chunk]
                rb = recf[pl.ds(i, 1), b0 : b0 + chunk]
                real = real + (sa * ra + sb * rb)
                imag = imag + (sb * ra - sa * rb)
            cross[rows, c * chunk : (c + 1) * chunk] = (real * inverse).astype(jnp.bfloat16)
            cross[rows, freqs + c * chunk : freqs + (c + 1) * chunk] = (imag * inverse).astype(
                jnp.bfloat16
            )
        return carry

    lax.fori_loop(0, group, per_receiver, 0)
    out_ref[...] = jnp.dot(
        cross[...], tab_ref[...], preferred_element_type=jnp.float32
    ).astype(jnp.bfloat16)


def correlate(rec_packed, src_packed, table, windows, freqs):
    nrec, width = rec_packed.shape
    nsrc = src_packed.shape[0]
    lags = table.shape[1]
    group = 8
    kernel = functools.partial(
        cross_kernel, windows=windows, freqs=freqs, group=group, chunk=256
    )
    out = pl.pallas_call(
        kernel,
        grid=(nrec // group,),
        in_specs=[
            pl.BlockSpec((nrec, width), lambda g: (0, 0)),
            pl.BlockSpec((nsrc, width), lambda g: (0, 0)),
            pl.BlockSpec(table.shape, lambda g: (0, 0)),
        ],
        out_specs=pl.BlockSpec((group * nsrc, lags), lambda g: (g, 0)),
        out_shape=jax.ShapeDtypeStruct((nrec * nsrc, lags), jnp.bfloat16),
        scratch_shapes=[
            pltpu.VMEM((nsrc, windows * 2 * freqs), jnp.float32),
            pltpu.VMEM((nrec, windows * 2 * freqs), jnp.float32),
            pltpu.VMEM((nrec, PAD), jnp.float32),
            pltpu.VMEM((group * nsrc, 2 * freqs), jnp.bfloat16),
        ],
        compiler_params=pltpu.CompilerParams(dimension_semantics=("arbitrary",)),
    )(rec_packed, src_packed, table)
    return out.reshape(nrec, nsrc, lags)


def local(spectra, valid):
    channels, windows, _, freqs = spectra.shape
    table = lag_table(freqs, LAGS).reshape(2 * freqs, LAGS)
    mask_wire = valid.astype(jnp.bfloat16)
    whitened = whiten_spectra(spectra)
    packed = pack(whitened, mask_wire)
    rec_packed = lax.all_gather(packed, "rcv", axis=0, tiled=True)
    src_packed = lax.all_gather(packed, "src", axis=0, tiled=True)
    return correlate(rec_packed, src_packed, table, windows, freqs)


def solution(mesh):
    return jax.shard_map(
        local,
        mesh=mesh,
        in_specs=(P(("src", "rcv"), None, None, None), P(("src", "rcv"), None)),
        out_specs=P("src", "rcv", None),
        check_vma=False,
    )
```

```python
import functools
import math

import jax
import jax.numpy as jnp
from jax import lax
from jax.experimental import pallas as pl
from jax.experimental.pallas import tpu as pltpu
from jax.sharding import PartitionSpec as P

LAGS = 512
BAND = 32
NSAMP = 7500
PAD = 128

epsilon = 1e-06


def whiten_spectra(spectra):
    values = spectra.astype(jnp.float32)
    squares = values[:, :, 0] ** 2 + values[:, :, 1] ** 2
    banded = squares.reshape(squares.shape[0], squares.shape[1], squares.shape[2] // BAND, BAND)
    power = jnp.sum(banded, axis=3) / (2.0 * BAND)
    factor = jnp.repeat(1.0 / jnp.sqrt(power + epsilon), BAND, axis=2)
    return (values * factor[:, :, None, :]).astype(jnp.bfloat16)


def lag_table(freq_count, lag_count):
    step = 64
    shifts = jnp.arange(lag_count, dtype=jnp.int32) - lag_count // 2
    hi = jnp.arange(freq_count // step, dtype=jnp.int32) * step
    lo = jnp.arange(step, dtype=jnp.int32)
    scale = 2.0 * math.pi / NSAMP
    angle_hi = jnp.mod(hi[:, None] * shifts[None, :], NSAMP).astype(jnp.float32) * scale
    angle_lo = jnp.mod(lo[:, None] * shifts[None, :], NSAMP).astype(jnp.float32) * scale
    cos_hi, sin_hi = jnp.cos(angle_hi)[:, None, :], jnp.sin(angle_hi)[:, None, :]
    cos_lo, sin_lo = jnp.cos(angle_lo)[None, :, :], jnp.sin(angle_lo)[None, :, :]
    factor = 1.0 / math.sqrt(2.0 * freq_count)
    cosines = (cos_hi * cos_lo - sin_hi * sin_lo) * factor
    sines = (sin_hi * cos_lo + cos_hi * sin_lo) * (-factor)
    cosines = cosines.reshape(freq_count, lag_count).astype(jnp.bfloat16)
    sines = sines.reshape(freq_count, lag_count).astype(jnp.bfloat16)
    return jnp.stack([cosines, sines], axis=0)


def pack(whitened, mask):
    channels = whitened.shape[0]
    flat = whitened.reshape(channels, -1)
    tail = jnp.zeros((channels, PAD), jnp.bfloat16).at[:, : mask.shape[1]].set(mask)
    return jnp.concatenate([flat, tail], axis=1)


def cross_kernel(rec_ref, src_ref, tab_ref, out_ref, srcf, recf, rtails, cross, *, windows, freqs, group, chunk):
    step = pl.program_id(0)
    nsrc = src_ref.shape[0]
    body = windows * 2 * freqs
    width = 2 * freqs

    @pl.when(step == 0)
    def _():
        smask = src_ref[:, body : body + PAD].astype(jnp.float32)
        rmask = rec_ref[:, body : body + PAD].astype(jnp.float32)
        rtails[...] = rmask
        for w in range(windows):
            cols = slice(w * width, (w + 1) * width)
            srcf[:, cols] = src_ref[:, cols].astype(jnp.float32) * smask[:, w : w + 1]
            recf[:, cols] = rec_ref[:, cols].astype(jnp.float32) * rmask[:, w : w + 1]

    smask = src_ref[:, body : body + PAD].astype(jnp.float32)

    def per_receiver(j, carry):
        i = step * group + j
        rtail = rtails[pl.ds(i, 1), :]
        count = jnp.sum(smask * rtail, axis=1, keepdims=True)
        inverse = 1.0 / jnp.maximum(count, 1.0)
        rows = pl.ds(pl.multiple_of(j * nsrc, nsrc), nsrc)
        for c in range(freqs // chunk):
            real = jnp.zeros((nsrc, chunk), jnp.float32)
            imag = jnp.zeros((nsrc, chunk), jnp.float32)
            for w in range(windows):
                a0 = w * width + c * chunk
                b0 = a0 + freqs
                sa = srcf[:, a0 : a0 + chunk]
                sb = srcf[:, b0 : b0 + chunk]
                ra = recf[pl.ds(i, 1), a0 : a0 + chunk]
                rb = recf[pl.ds(i, 1), b0 : b0 + chunk]
                real = real + (sa * ra + sb * rb)
                imag = imag + (sb * ra - sa * rb)
            cross[rows, c * chunk : (c + 1) * chunk] = (real * inverse).astype(jnp.bfloat16)
            cross[rows, freqs + c * chunk : freqs + (c + 1) * chunk] = (imag * inverse).astype(
                jnp.bfloat16
            )
        return carry

    lax.fori_loop(0, group, per_receiver, 0)
    out_ref[...] = jnp.dot(
        cross[...], tab_ref[...], preferred_element_type=jnp.float32
    ).astype(jnp.bfloat16)


def correlate(rec_packed, src_packed, table, windows, freqs):
    nrec, width = rec_packed.shape
    nsrc = src_packed.shape[0]
    lags = table.shape[1]
    group = 8
    kernel = functools.partial(
        cross_kernel, windows=windows, freqs=freqs, group=group, chunk=256
    )
    out = pl.pallas_call(
        kernel,
        grid=(nrec // group,),
        in_specs=[
            pl.BlockSpec((nrec, width), lambda g: (0, 0)),
            pl.BlockSpec((nsrc, width), lambda g: (0, 0)),
            pl.BlockSpec(table.shape, lambda g: (0, 0)),
        ],
        out_specs=pl.BlockSpec((group * nsrc, lags), lambda g: (g, 0)),
        out_shape=jax.ShapeDtypeStruct((nrec * nsrc, lags), jnp.bfloat16),
        scratch_shapes=[
            pltpu.VMEM((nsrc, windows * 2 * freqs), jnp.float32),
            pltpu.VMEM((nrec, windows * 2 * freqs), jnp.float32),
            pltpu.VMEM((nrec, PAD), jnp.float32),
            pltpu.VMEM((group * nsrc, 2 * freqs), jnp.bfloat16),
        ],
        compiler_params=pltpu.CompilerParams(dimension_semantics=("arbitrary",)),
    )(rec_packed, src_packed, table)
    return out.reshape(nrec, nsrc, lags)


def permute_gather(x, axis, count):
    index = lax.axis_index(axis)
    parts = [x]
    for shift in range(1, count):
        pairs = [(j, (j + shift) % count) for j in range(count)]
        parts.append(lax.ppermute(x, axis, perm=pairs))
    backward = jnp.stack(parts[::-1])
    doubled = jnp.concatenate([backward, backward], axis=0)
    ordered = lax.dynamic_slice_in_dim(doubled, count - 1 - index, count, axis=0)
    return ordered.reshape((count * x.shape[0],) + x.shape[1:])


def local(spectra, valid, rcv_count):
    channels, windows, _, freqs = spectra.shape
    table = lag_table(freqs, LAGS).reshape(2 * freqs, LAGS)
    mask_wire = valid.astype(jnp.bfloat16)
    whitened = whiten_spectra(spectra)
    packed = pack(whitened, mask_wire)
    rec_packed = permute_gather(packed, "rcv", rcv_count)
    src_packed = lax.all_gather(packed, "src", axis=0, tiled=True)
    return correlate(rec_packed, src_packed, table, windows, freqs)


def solution(mesh):
    return jax.shard_map(
        functools.partial(local, rcv_count=mesh.shape["rcv"]),
        mesh=mesh,
        in_specs=(P(("src", "rcv"), None, None, None), P(("src", "rcv"), None)),
        out_specs=P("src", "rcv", None),
        check_vma=False,
    )
```

```python
import functools
import math

import jax
import jax.numpy as jnp
from jax import lax
from jax.experimental import pallas as pl
from jax.experimental.pallas import tpu as pltpu
from jax.sharding import PartitionSpec as P

LAGS = 512
BAND = 32
NSAMP = 7500
PAD = 128

epsilon = 1e-06


def whiten_spectra(spectra):
    values = spectra.astype(jnp.float32)
    squares = values[:, :, 0] ** 2 + values[:, :, 1] ** 2
    banded = squares.reshape(squares.shape[0], squares.shape[1], squares.shape[2] // BAND, BAND)
    power = jnp.sum(banded, axis=3) / (2.0 * BAND)
    factor = jnp.repeat(1.0 / jnp.sqrt(power + epsilon), BAND, axis=2)
    return (values * factor[:, :, None, :]).astype(jnp.bfloat16)


def lag_table(freq_count, lag_count):
    step = 64
    shifts = jnp.arange(lag_count, dtype=jnp.int32) - lag_count // 2
    hi = jnp.arange(freq_count // step, dtype=jnp.int32) * step
    lo = jnp.arange(step, dtype=jnp.int32)
    scale = 2.0 * math.pi / NSAMP
    angle_hi = jnp.mod(hi[:, None] * shifts[None, :], NSAMP).astype(jnp.float32) * scale
    angle_lo = jnp.mod(lo[:, None] * shifts[None, :], NSAMP).astype(jnp.float32) * scale
    cos_hi, sin_hi = jnp.cos(angle_hi)[:, None, :], jnp.sin(angle_hi)[:, None, :]
    cos_lo, sin_lo = jnp.cos(angle_lo)[None, :, :], jnp.sin(angle_lo)[None, :, :]
    factor = 1.0 / math.sqrt(2.0 * freq_count)
    cosines = (cos_hi * cos_lo - sin_hi * sin_lo) * factor
    sines = (sin_hi * cos_lo + cos_hi * sin_lo) * (-factor)
    cosines = cosines.reshape(freq_count, lag_count).astype(jnp.bfloat16)
    sines = sines.reshape(freq_count, lag_count).astype(jnp.bfloat16)
    return jnp.stack([cosines, sines], axis=0)


def pack(whitened, mask):
    channels = whitened.shape[0]
    flat = whitened.reshape(channels, -1)
    tail = jnp.zeros((channels, PAD), jnp.bfloat16).at[:, : mask.shape[1]].set(mask)
    return jnp.concatenate([flat, tail], axis=1)


def cross_kernel(rec_ref, src_ref, tab_ref, out_ref, srcf, recf, rtails, cross, *, windows, freqs, group, chunk):
    step = pl.program_id(0)
    nsrc = src_ref.shape[0]
    body = windows * 2 * freqs
    width = 2 * freqs

    @pl.when(step == 0)
    def _():
        smask = src_ref[:, body : body + PAD].astype(jnp.float32)
        rmask = rec_ref[:, body : body + PAD].astype(jnp.float32)
        rtails[...] = rmask
        for w in range(windows):
            cols = slice(w * width, (w + 1) * width)
            srcf[:, cols] = src_ref[:, cols].astype(jnp.float32) * smask[:, w : w + 1]
            recf[:, cols] = rec_ref[:, cols].astype(jnp.float32) * rmask[:, w : w + 1]

    smask = src_ref[:, body : body + PAD].astype(jnp.float32)

    def per_receiver(j, carry):
        i = step * group + j
        rtail = rtails[pl.ds(i, 1), :]
        count = jnp.sum(smask * rtail, axis=1, keepdims=True)
        inverse = 1.0 / jnp.maximum(count, 1.0)
        rows = pl.ds(pl.multiple_of(j * nsrc, nsrc), nsrc)
        for c in range(freqs // chunk):
            real = jnp.zeros((nsrc, chunk), jnp.float32)
            imag = jnp.zeros((nsrc, chunk), jnp.float32)
            for w in range(windows):
                a0 = w * width + c * chunk
                b0 = a0 + freqs
                sa = srcf[:, a0 : a0 + chunk]
                sb = srcf[:, b0 : b0 + chunk]
                ra = recf[pl.ds(i, 1), a0 : a0 + chunk]
                rb = recf[pl.ds(i, 1), b0 : b0 + chunk]
                real = real + (sa * ra + sb * rb)
                imag = imag + (sb * ra - sa * rb)
            cross[rows, c * chunk : (c + 1) * chunk] = (real * inverse).astype(jnp.bfloat16)
            cross[rows, freqs + c * chunk : freqs + (c + 1) * chunk] = (imag * inverse).astype(
                jnp.bfloat16
            )
        return carry

    lax.fori_loop(0, group, per_receiver, 0)
    out_ref[...] = jnp.dot(
        cross[...], tab_ref[...], preferred_element_type=jnp.float32
    ).astype(jnp.bfloat16)


def correlate(rec_packed, src_packed, table, windows, freqs):
    nrec, width = rec_packed.shape
    nsrc = src_packed.shape[0]
    lags = table.shape[1]
    group = 8
    kernel = functools.partial(
        cross_kernel, windows=windows, freqs=freqs, group=group, chunk=256
    )
    out = pl.pallas_call(
        kernel,
        grid=(nrec // group,),
        in_specs=[
            pl.BlockSpec((nrec, width), lambda g: (0, 0)),
            pl.BlockSpec((nsrc, width), lambda g: (0, 0)),
            pl.BlockSpec(table.shape, lambda g: (0, 0)),
        ],
        out_specs=pl.BlockSpec((group * nsrc, lags), lambda g: (g, 0)),
        out_shape=jax.ShapeDtypeStruct((nrec * nsrc, lags), jnp.bfloat16),
        scratch_shapes=[
            pltpu.VMEM((nsrc, windows * 2 * freqs), jnp.float32),
            pltpu.VMEM((nrec, windows * 2 * freqs), jnp.float32),
            pltpu.VMEM((nrec, PAD), jnp.float32),
            pltpu.VMEM((group * nsrc, 2 * freqs), jnp.bfloat16),
        ],
        compiler_params=pltpu.CompilerParams(dimension_semantics=("arbitrary",)),
    )(rec_packed, src_packed, table)
    return out.reshape(nrec, nsrc, lags)


def permute_gather(x, axis, count):
    index = lax.axis_index(axis)
    parts = [x]
    for shift in range(1, count):
        pairs = [(j, (j + shift) % count) for j in range(count)]
        parts.append(lax.ppermute(x, axis, perm=pairs))
    backward = jnp.stack(parts[::-1])
    doubled = jnp.concatenate([backward, backward], axis=0)
    ordered = lax.dynamic_slice_in_dim(doubled, count - 1 - index, count, axis=0)
    return ordered.reshape((count * x.shape[0],) + x.shape[1:])


def chip_gather(x, axis, count):
    index = lax.axis_index(axis)
    chips = count // 2
    parts = [x]
    for shift in range(1, chips):
        pairs = [(j, (j + 2 * shift) % count) for j in range(count)]
        parts.append(lax.ppermute(x, axis, perm=pairs))
    backward = jnp.stack(parts[::-1])
    doubled = jnp.concatenate([backward, backward], axis=0)
    mine = lax.dynamic_slice_in_dim(doubled, chips - 1 - index // 2, chips, axis=0)
    sibling = lax.ppermute(mine, axis, perm=[(j, j ^ 1) for j in range(count)])
    low = index % 2 == 0
    full = jnp.stack([jnp.where(low, mine, sibling), jnp.where(low, sibling, mine)], axis=1)
    return full.reshape((count * x.shape[0],) + x.shape[1:])


def local(spectra, valid, rcv_count, src_count):
    channels, windows, _, freqs = spectra.shape
    table = lag_table(freqs, LAGS).reshape(2 * freqs, LAGS)
    mask_wire = valid.astype(jnp.bfloat16)
    whitened = whiten_spectra(spectra)
    packed = pack(whitened, mask_wire)
    rec_packed = permute_gather(packed, "rcv", rcv_count)
    src_packed = chip_gather(packed, "src", src_count)
    return correlate(rec_packed, src_packed, table, windows, freqs)


def solution(mesh):
    return jax.shard_map(
        functools.partial(local, rcv_count=mesh.shape["rcv"], src_count=mesh.shape["src"]),
        mesh=mesh,
        in_specs=(P(("src", "rcv"), None, None, None), P(("src", "rcv"), None)),
        out_specs=P("src", "rcv", None),
        check_vma=False,
    )
```

```python
import functools
import math

import jax
import jax.numpy as jnp
from jax import lax
from jax.experimental import pallas as pl
from jax.experimental.pallas import tpu as pltpu
from jax.sharding import PartitionSpec as P

LAGS = 512
BAND = 32
NSAMP = 7500
PAD = 128

epsilon = 1e-06


def whiten_spectra(spectra):
    values = spectra.astype(jnp.float32)
    squares = values[:, :, 0] ** 2 + values[:, :, 1] ** 2
    banded = squares.reshape(squares.shape[0], squares.shape[1], squares.shape[2] // BAND, BAND)
    power = jnp.sum(banded, axis=3) / (2.0 * BAND)
    factor = jnp.repeat(1.0 / jnp.sqrt(power + epsilon), BAND, axis=2)
    return (values * factor[:, :, None, :]).astype(jnp.bfloat16)


def lag_table(freq_count, lag_count):
    step = 64
    shifts = jnp.arange(lag_count, dtype=jnp.int32) - lag_count // 2
    hi = jnp.arange(freq_count // step, dtype=jnp.int32) * step
    lo = jnp.arange(step, dtype=jnp.int32)
    scale = 2.0 * math.pi / NSAMP
    angle_hi = jnp.mod(hi[:, None] * shifts[None, :], NSAMP).astype(jnp.float32) * scale
    angle_lo = jnp.mod(lo[:, None] * shifts[None, :], NSAMP).astype(jnp.float32) * scale
    cos_hi, sin_hi = jnp.cos(angle_hi)[:, None, :], jnp.sin(angle_hi)[:, None, :]
    cos_lo, sin_lo = jnp.cos(angle_lo)[None, :, :], jnp.sin(angle_lo)[None, :, :]
    factor = 1.0 / math.sqrt(2.0 * freq_count)
    cosines = (cos_hi * cos_lo - sin_hi * sin_lo) * factor
    sines = (sin_hi * cos_lo + cos_hi * sin_lo) * (-factor)
    cosines = cosines.reshape(freq_count, lag_count).astype(jnp.bfloat16)
    sines = sines.reshape(freq_count, lag_count).astype(jnp.bfloat16)
    return jnp.stack([cosines, sines], axis=0)


def pack(whitened, mask):
    channels = whitened.shape[0]
    flat = whitened.reshape(channels, -1)
    tail = jnp.pad(mask, ((0, 0), (0, PAD - mask.shape[1])))
    return jnp.concatenate([flat, tail], axis=1)


def cross_kernel(
    place_ref, rec_ref, own_ref, sib_ref, tab_ref, out_ref, srcf, recf, rtails, stails, cross,
    *, windows, freqs, group, chunk
):
    step = pl.program_id(0)
    rcv_count, per = rec_ref.shape[0], rec_ref.shape[1]
    chips = own_ref.shape[0]
    nsrc = 2 * chips * per
    body = windows * 2 * freqs
    width = 2 * freqs

    def place(block, dst, values, tails):
        rows = slice(dst * per, (dst + 1) * per)
        mask = block[:, body : body + PAD].astype(jnp.float32)
        tails[rows, :] = mask
        for w in range(windows):
            cols = slice(w * width, (w + 1) * width)
            values[rows, cols] = block[:, cols].astype(jnp.float32) * mask[:, w : w + 1]

    @pl.when(step == 0)
    def _():
        rcv_index, chip, core = place_ref[0], place_ref[1], place_ref[2]
        for dst in range(rcv_count):
            k = (rcv_index - dst + rcv_count) % rcv_count
            place(rec_ref[k], dst, recf, rtails)
        for zz in range(chips):
            k = (chip - zz + chips) % chips
            own_block = own_ref[k]
            sib_block = sib_ref[k]
            for cc in range(2):
                same = core == cc
                block = jnp.where(same, own_block, sib_block)
                place(block, zz * 2 + cc, srcf, stails)

    smask = stails[...]

    def per_receiver(j, carry):
        i = step * group + j
        rtail = rtails[pl.ds(i, 1), :]
        count = jnp.sum(smask * rtail, axis=1, keepdims=True)
        inverse = 1.0 / jnp.maximum(count, 1.0)
        rows = pl.ds(pl.multiple_of(j * nsrc, nsrc), nsrc)
        for c in range(freqs // chunk):
            real = jnp.zeros((nsrc, chunk), jnp.float32)
            imag = jnp.zeros((nsrc, chunk), jnp.float32)
            for w in range(windows):
                a0 = w * width + c * chunk
                b0 = a0 + freqs
                sa = srcf[:, a0 : a0 + chunk]
                sb = srcf[:, b0 : b0 + chunk]
                ra = recf[pl.ds(i, 1), a0 : a0 + chunk]
                rb = recf[pl.ds(i, 1), b0 : b0 + chunk]
                real = real + (sa * ra + sb * rb)
                imag = imag + (sb * ra - sa * rb)
            cross[rows, c * chunk : (c + 1) * chunk] = (real * inverse).astype(jnp.bfloat16)
            cross[rows, freqs + c * chunk : freqs + (c + 1) * chunk] = (imag * inverse).astype(
                jnp.bfloat16
            )
        return carry

    lax.fori_loop(0, group, per_receiver, 0)
    out_ref[...] = jnp.dot(
        cross[...], tab_ref[...], preferred_element_type=jnp.float32
    ).astype(jnp.bfloat16)


def correlate(place, rec_stack, own_stack, sib_stack, table, windows, freqs):
    rcv_count, per, width = rec_stack.shape
    chips = own_stack.shape[0]
    nrec = rcv_count * per
    nsrc = 2 * chips * per
    lags = table.shape[1]
    group = 8
    kernel = functools.partial(
        cross_kernel, windows=windows, freqs=freqs, group=group, chunk=256
    )
    full3 = lambda g, p: (0, 0, 0)
    out = pl.pallas_call(
        kernel,
        grid_spec=pltpu.PrefetchScalarGridSpec(
            num_scalar_prefetch=1,
            grid=(nrec // group,),
            in_specs=[
                pl.BlockSpec(rec_stack.shape, full3),
                pl.BlockSpec(own_stack.shape, full3),
                pl.BlockSpec(sib_stack.shape, full3),
                pl.BlockSpec(table.shape, lambda g, p: (0, 0)),
            ],
            out_specs=pl.BlockSpec((group * nsrc, lags), lambda g, p: (g, 0)),
            scratch_shapes=[
                pltpu.VMEM((nsrc, windows * 2 * freqs), jnp.float32),
                pltpu.VMEM((nrec, windows * 2 * freqs), jnp.float32),
                pltpu.VMEM((nrec, PAD), jnp.float32),
                pltpu.VMEM((nsrc, PAD), jnp.float32),
                pltpu.VMEM((group * nsrc, 2 * freqs), jnp.bfloat16),
            ],
        ),
        out_shape=jax.ShapeDtypeStruct((nrec * nsrc, lags), jnp.bfloat16),
        compiler_params=pltpu.CompilerParams(dimension_semantics=("arbitrary",)),
    )(place, rec_stack, own_stack, sib_stack, table)
    return out.reshape(nrec, nsrc, lags)


def shifted(x, axis, count, stride):
    parts = [x]
    for shift in range(1, count // stride):
        pairs = [(j, (j + stride * shift) % count) for j in range(count)]
        parts.append(lax.ppermute(x, axis, perm=pairs))
    return jnp.stack(parts)


def local(spectra, valid, rcv_count, src_count):
    channels, windows, _, freqs = spectra.shape
    table = lag_table(freqs, LAGS).reshape(2 * freqs, LAGS)
    mask_wire = valid.astype(jnp.bfloat16)
    whitened = whiten_spectra(spectra)
    packed = pack(whitened, mask_wire)
    rec_stack = shifted(packed, "rcv", rcv_count, 1)
    own_stack = shifted(packed, "src", src_count, 2)
    sib_stack = lax.ppermute(own_stack, "src", perm=[(j, j ^ 1) for j in range(src_count)])
    src_index = lax.axis_index("src")
    place = jnp.stack(
        [lax.axis_index("rcv"), src_index // 2, src_index % 2]
    ).astype(jnp.int32)
    return correlate(place, rec_stack, own_stack, sib_stack, table, windows, freqs)


def solution(mesh):
    return jax.shard_map(
        functools.partial(local, rcv_count=mesh.shape["rcv"], src_count=mesh.shape["src"]),
        mesh=mesh,
        in_specs=(P(("src", "rcv"), None, None, None), P(("src", "rcv"), None)),
        out_specs=P("src", "rcv", None),
        check_vma=False,
    )
```

```python
import functools
import math

import jax
import jax.numpy as jnp
from jax import lax
from jax.experimental import pallas as pl
from jax.experimental.pallas import tpu as pltpu
from jax.sharding import PartitionSpec as P

LAGS = 512
BAND = 32
NSAMP = 7500
PAD = 128

epsilon = 1e-06


def split3(x):
    hi = x.astype(jnp.bfloat16)
    rest = x - hi.astype(jnp.float32)
    mid = rest.astype(jnp.bfloat16)
    lo = (rest - mid.astype(jnp.float32)).astype(jnp.bfloat16)
    return hi, mid, lo


def exact_dot(x, ones):
    return sum(jnp.dot(part, ones, preferred_element_type=jnp.float32) for part in split3(x))


def whiten_kernel(x_ref, v_ref, out_ref, sq_ref, *, channels, windows, freqs):
    bands = freqs // BAND
    band_of = lax.broadcasted_iota(jnp.int32, (freqs, bands), 0) // BAND
    to_band = (band_of == lax.broadcasted_iota(jnp.int32, (freqs, bands), 1)).astype(jnp.bfloat16)
    band_row = lax.broadcasted_iota(jnp.int32, (bands, freqs), 1) // BAND
    from_band = (band_row == lax.broadcasted_iota(jnp.int32, (bands, freqs), 0)).astype(
        jnp.bfloat16
    )
    for c in range(channels):
        for w in range(windows):
            x = x_ref[c, w].astype(jnp.float32)
            row = c * windows + w
            sq_ref[row : row + 1, :] = x[0:1] ** 2 + x[1:2] ** 2
    power = exact_dot(sq_ref[...], to_band) / (2.0 * BAND)
    factor = exact_dot(1.0 / jnp.sqrt(power + epsilon), from_band)
    width = 2 * freqs
    for c in range(channels):
        for w in range(windows):
            x = x_ref[c, w].astype(jnp.float32)
            row = c * windows + w
            scale = factor[row : row + 1, :]
            out_ref[c : c + 1, w * width : w * width + freqs] = (x[0:1] * scale).astype(
                jnp.bfloat16
            )
            out_ref[c : c + 1, w * width + freqs : (w + 1) * width] = (x[1:2] * scale).astype(
                jnp.bfloat16
            )
    body = windows * width
    out_ref[:, body : body + PAD] = v_ref[...].astype(jnp.float32).astype(jnp.bfloat16)


def whiten_pack(spectra, valid):
    channels, windows, _, freqs = spectra.shape
    tail = jnp.pad(valid, ((0, 0), (0, PAD - windows)))
    kernel = functools.partial(whiten_kernel, channels=channels, windows=windows, freqs=freqs)
    return pl.pallas_call(
        kernel,
        out_shape=jax.ShapeDtypeStruct((channels, windows * 2 * freqs + PAD), jnp.bfloat16),
        scratch_shapes=[pltpu.VMEM((channels * windows, freqs), jnp.float32)],
    )(spectra, tail)


def table_kernel(chi_ref, shi_ref, clo_ref, slo_ref, out_ref, *, freqs, factor):
    step = clo_ref.shape[0]
    clo = clo_ref[...]
    slo = slo_ref[...]

    def body(h, carry):
        ch = chi_ref[pl.ds(h, 1), :]
        sh = shi_ref[pl.ds(h, 1), :]
        rows = pl.ds(pl.multiple_of(h * step, step), step)
        out_ref[rows, :] = ((ch * clo - sh * slo) * factor).astype(jnp.bfloat16)
        rows = pl.ds(pl.multiple_of(freqs + h * step, step), step)
        out_ref[rows, :] = ((sh * clo + ch * slo) * (-factor)).astype(jnp.bfloat16)
        return carry

    lax.fori_loop(0, chi_ref.shape[0], body, 0)


def lag_table(freq_count, lag_count):
    step = 64
    shifts = jnp.arange(lag_count, dtype=jnp.int32) - lag_count // 2
    hi = jnp.arange(freq_count // step, dtype=jnp.int32) * step
    lo = jnp.arange(step, dtype=jnp.int32)
    scale = 2.0 * math.pi / NSAMP
    angle_hi = jnp.mod(hi[:, None] * shifts[None, :], NSAMP).astype(jnp.float32) * scale
    angle_lo = jnp.mod(lo[:, None] * shifts[None, :], NSAMP).astype(jnp.float32) * scale
    factor = 1.0 / math.sqrt(2.0 * freq_count)
    kernel = functools.partial(table_kernel, freqs=freq_count, factor=factor)
    return pl.pallas_call(
        kernel,
        out_shape=jax.ShapeDtypeStruct((2 * freq_count, lag_count), jnp.bfloat16),
    )(jnp.cos(angle_hi), jnp.sin(angle_hi), jnp.cos(angle_lo), jnp.sin(angle_lo))


def cross_kernel(
    place_ref, rec_ref, own_ref, sib_ref, tab_ref, out_ref, srcf, recf, rtails, stails, cross,
    *, windows, freqs, group, chunk
):
    step = pl.program_id(0)
    rcv_count, per = rec_ref.shape[0], rec_ref.shape[1]
    chips = own_ref.shape[0]
    nsrc = 2 * chips * per
    body = windows * 2 * freqs
    width = 2 * freqs

    def place(block, dst, values, tails):
        rows = slice(dst * per, (dst + 1) * per)
        mask = block[:, body : body + PAD].astype(jnp.float32)
        tails[rows, :] = mask
        for w in range(windows):
            cols = slice(w * width, (w + 1) * width)
            values[rows, cols] = block[:, cols].astype(jnp.float32) * mask[:, w : w + 1]

    @pl.when(step == 0)
    def _():
        rcv_index, chip, core = place_ref[0], place_ref[1], place_ref[2]
        for dst in range(rcv_count):
            k = (rcv_index - dst + rcv_count) % rcv_count
            place(rec_ref[k], dst, recf, rtails)
        for zz in range(chips):
            k = (chip - zz + chips) % chips
            own_block = own_ref[k]
            sib_block = sib_ref[k]
            for cc in range(2):
                same = core == cc
                block = jnp.where(same, own_block, sib_block)
                place(block, zz * 2 + cc, srcf, stails)

    smask = stails[...]

    def per_receiver(j, carry):
        i = step * group + j
        rtail = rtails[pl.ds(i, 1), :]
        count = jnp.sum(smask * rtail, axis=1, keepdims=True)
        inverse = 1.0 / jnp.maximum(count, 1.0)
        rows = pl.ds(pl.multiple_of(j * nsrc, nsrc), nsrc)
        for c in range(freqs // chunk):
            real = jnp.zeros((nsrc, chunk), jnp.float32)
            imag = jnp.zeros((nsrc, chunk), jnp.float32)
            for w in range(windows):
                a0 = w * width + c * chunk
                b0 = a0 + freqs
                sa = srcf[:, a0 : a0 + chunk]
                sb = srcf[:, b0 : b0 + chunk]
                ra = recf[pl.ds(i, 1), a0 : a0 + chunk]
                rb = recf[pl.ds(i, 1), b0 : b0 + chunk]
                real = real + (sa * ra + sb * rb)
                imag = imag + (sb * ra - sa * rb)
            cross[rows, c * chunk : (c + 1) * chunk] = (real * inverse).astype(jnp.bfloat16)
            cross[rows, freqs + c * chunk : freqs + (c + 1) * chunk] = (imag * inverse).astype(
                jnp.bfloat16
            )
        return carry

    lax.fori_loop(0, group, per_receiver, 0)
    out_ref[...] = jnp.dot(
        cross[...], tab_ref[...], preferred_element_type=jnp.float32
    ).astype(jnp.bfloat16)


def correlate(place, rec_stack, own_stack, sib_stack, table, windows, freqs):
    rcv_count, per, width = rec_stack.shape
    chips = own_stack.shape[0]
    nrec = rcv_count * per
    nsrc = 2 * chips * per
    lags = table.shape[1]
    group = 8
    kernel = functools.partial(
        cross_kernel, windows=windows, freqs=freqs, group=group, chunk=256
    )
    full3 = lambda g, p: (0, 0, 0)
    out = pl.pallas_call(
        kernel,
        grid_spec=pltpu.PrefetchScalarGridSpec(
            num_scalar_prefetch=1,
            grid=(nrec // group,),
            in_specs=[
                pl.BlockSpec(rec_stack.shape, full3),
                pl.BlockSpec(own_stack.shape, full3),
                pl.BlockSpec(sib_stack.shape, full3),
                pl.BlockSpec(table.shape, lambda g, p: (0, 0)),
            ],
            out_specs=pl.BlockSpec((group * nsrc, lags), lambda g, p: (g, 0)),
            scratch_shapes=[
                pltpu.VMEM((nsrc, windows * 2 * freqs), jnp.float32),
                pltpu.VMEM((nrec, windows * 2 * freqs), jnp.float32),
                pltpu.VMEM((nrec, PAD), jnp.float32),
                pltpu.VMEM((nsrc, PAD), jnp.float32),
                pltpu.VMEM((group * nsrc, 2 * freqs), jnp.bfloat16),
            ],
        ),
        out_shape=jax.ShapeDtypeStruct((nrec * nsrc, lags), jnp.bfloat16),
        compiler_params=pltpu.CompilerParams(dimension_semantics=("arbitrary",)),
    )(place, rec_stack, own_stack, sib_stack, table)
    return out.reshape(nrec, nsrc, lags)


def shifted(x, axis, count, stride):
    parts = [x]
    for shift in range(1, count // stride):
        pairs = [(j, (j + stride * shift) % count) for j in range(count)]
        parts.append(lax.ppermute(x, axis, perm=pairs))
    return jnp.stack(parts)


def local(spectra, valid, rcv_count, src_count):
    channels, windows, _, freqs = spectra.shape
    table = lag_table(freqs, LAGS)
    packed = whiten_pack(spectra, valid)
    rec_stack = shifted(packed, "rcv", rcv_count, 1)
    own_stack = shifted(packed, "src", src_count, 2)
    sib_stack = lax.ppermute(own_stack, "src", perm=[(j, j ^ 1) for j in range(src_count)])
    src_index = lax.axis_index("src")
    place = jnp.stack(
        [lax.axis_index("rcv"), src_index // 2, src_index % 2]
    ).astype(jnp.int32)
    return correlate(place, rec_stack, own_stack, sib_stack, table, windows, freqs)


def solution(mesh):
    return jax.shard_map(
        functools.partial(local, rcv_count=mesh.shape["rcv"], src_count=mesh.shape["src"]),
        mesh=mesh,
        in_specs=(P(("src", "rcv"), None, None, None), P(("src", "rcv"), None)),
        out_specs=P("src", "rcv", None),
        check_vma=False,
    )
```

```python
import functools
import math

import jax
import jax.numpy as jnp
from jax import lax
from jax.experimental import pallas as pl
from jax.experimental.pallas import tpu as pltpu
from jax.sharding import PartitionSpec as P

LAGS = 512
BAND = 32
NSAMP = 7500
PAD = 128

epsilon = 1e-06


def split3(x):
    hi = x.astype(jnp.bfloat16)
    rest = x - hi.astype(jnp.float32)
    mid = rest.astype(jnp.bfloat16)
    lo = (rest - mid.astype(jnp.float32)).astype(jnp.bfloat16)
    return hi, mid, lo


def exact_dot(x, ones):
    return sum(jnp.dot(part, ones, preferred_element_type=jnp.float32) for part in split3(x))


def whiten_kernel(x_ref, v_ref, out_ref, sq_ref, *, channels, windows, freqs):
    bands = freqs // BAND
    band_of = lax.broadcasted_iota(jnp.int32, (freqs, bands), 0) // BAND
    to_band = (band_of == lax.broadcasted_iota(jnp.int32, (freqs, bands), 1)).astype(jnp.bfloat16)
    band_row = lax.broadcasted_iota(jnp.int32, (bands, freqs), 1) // BAND
    from_band = (band_row == lax.broadcasted_iota(jnp.int32, (bands, freqs), 0)).astype(
        jnp.bfloat16
    )
    for c in range(channels):
        for w in range(windows):
            x = x_ref[c, w].astype(jnp.float32)
            row = c * windows + w
            sq_ref[row : row + 1, :] = x[0:1] ** 2 + x[1:2] ** 2
    power = exact_dot(sq_ref[...], to_band) / (2.0 * BAND)
    factor = exact_dot(1.0 / jnp.sqrt(power + epsilon), from_band)
    width = 2 * freqs
    for c in range(channels):
        for w in range(windows):
            x = x_ref[c, w].astype(jnp.float32)
            row = c * windows + w
            scale = factor[row : row + 1, :]
            out_ref[c : c + 1, w * width : w * width + freqs] = (x[0:1] * scale).astype(
                jnp.bfloat16
            )
            out_ref[c : c + 1, w * width + freqs : (w + 1) * width] = (x[1:2] * scale).astype(
                jnp.bfloat16
            )
    body = windows * width
    out_ref[:, body : body + PAD] = v_ref[...].astype(jnp.float32).astype(jnp.bfloat16)


def whiten_pack(spectra, valid):
    channels, windows, _, freqs = spectra.shape
    tail = jnp.pad(valid, ((0, 0), (0, PAD - windows)))
    kernel = functools.partial(whiten_kernel, channels=channels, windows=windows, freqs=freqs)
    return pl.pallas_call(
        kernel,
        out_shape=jax.ShapeDtypeStruct((channels, windows * 2 * freqs + PAD), jnp.bfloat16),
        scratch_shapes=[pltpu.VMEM((channels * windows, freqs), jnp.float32)],
    )(spectra, tail)


def lag_table(freq_count, lag_count):
    step = 64
    shifts = jnp.arange(lag_count, dtype=jnp.int32) - lag_count // 2
    hi = jnp.arange(freq_count // step, dtype=jnp.int32) * step
    lo = jnp.arange(step, dtype=jnp.int32)
    scale = 2.0 * math.pi / NSAMP
    angle_hi = jnp.mod(hi[:, None] * shifts[None, :], NSAMP).astype(jnp.float32) * scale
    angle_lo = jnp.mod(lo[:, None] * shifts[None, :], NSAMP).astype(jnp.float32) * scale
    cos_hi, sin_hi = jnp.cos(angle_hi)[:, None, :], jnp.sin(angle_hi)[:, None, :]
    cos_lo, sin_lo = jnp.cos(angle_lo)[None, :, :], jnp.sin(angle_lo)[None, :, :]
    factor = 1.0 / math.sqrt(2.0 * freq_count)
    cosines = (cos_hi * cos_lo - sin_hi * sin_lo) * factor
    sines = (sin_hi * cos_lo + cos_hi * sin_lo) * (-factor)
    cosines = cosines.reshape(freq_count, lag_count).astype(jnp.bfloat16)
    sines = sines.reshape(freq_count, lag_count).astype(jnp.bfloat16)
    return jnp.stack([cosines, sines], axis=0).reshape(2 * freq_count, lag_count)


def cross_kernel(
    place_ref, rec_ref, own_ref, sib_ref, tab_ref, out_ref, srcf, recf, rtails, stails, cross,
    *, windows, freqs, group, chunk
):
    step = pl.program_id(0)
    rcv_count, per = rec_ref.shape[0], rec_ref.shape[1]
    chips = own_ref.shape[0]
    nsrc = 2 * chips * per
    body = windows * 2 * freqs
    width = 2 * freqs

    def place(block, dst, values, tails):
        rows = slice(dst * per, (dst + 1) * per)
        mask = block[:, body : body + PAD].astype(jnp.float32)
        tails[rows, :] = mask
        for w in range(windows):
            cols = slice(w * width, (w + 1) * width)
            values[rows, cols] = block[:, cols].astype(jnp.float32) * mask[:, w : w + 1]

    @pl.when(step == 0)
    def _():
        rcv_index, chip, core = place_ref[0], place_ref[1], place_ref[2]
        for dst in range(rcv_count):
            k = (rcv_index - dst + rcv_count) % rcv_count
            place(rec_ref[k], dst, recf, rtails)
        for zz in range(chips):
            k = (chip - zz + chips) % chips
            own_block = own_ref[k]
            sib_block = sib_ref[k]
            for cc in range(2):
                same = core == cc
                block = jnp.where(same, own_block, sib_block)
                place(block, zz * 2 + cc, srcf, stails)

    smask = stails[...]

    def per_receiver(j, carry):
        i = step * group + j
        rtail = rtails[pl.ds(i, 1), :]
        count = jnp.sum(smask * rtail, axis=1, keepdims=True)
        inverse = 1.0 / jnp.maximum(count, 1.0)
        rows = pl.ds(pl.multiple_of(j * nsrc, nsrc), nsrc)
        for c in range(freqs // chunk):
            real = jnp.zeros((nsrc, chunk), jnp.float32)
            imag = jnp.zeros((nsrc, chunk), jnp.float32)
            for w in range(windows):
                a0 = w * width + c * chunk
                b0 = a0 + freqs
                sa = srcf[:, a0 : a0 + chunk]
                sb = srcf[:, b0 : b0 + chunk]
                ra = recf[pl.ds(i, 1), a0 : a0 + chunk]
                rb = recf[pl.ds(i, 1), b0 : b0 + chunk]
                real = real + (sa * ra + sb * rb)
                imag = imag + (sb * ra - sa * rb)
            cross[rows, c * chunk : (c + 1) * chunk] = (real * inverse).astype(jnp.bfloat16)
            cross[rows, freqs + c * chunk : freqs + (c + 1) * chunk] = (imag * inverse).astype(
                jnp.bfloat16
            )
        return carry

    lax.fori_loop(0, group, per_receiver, 0)
    out_ref[...] = jnp.dot(
        cross[...], tab_ref[...], preferred_element_type=jnp.float32
    ).astype(jnp.bfloat16)


def correlate(place, rec_stack, own_stack, sib_stack, table, windows, freqs):
    rcv_count, per, width = rec_stack.shape
    chips = own_stack.shape[0]
    nrec = rcv_count * per
    nsrc = 2 * chips * per
    lags = table.shape[1]
    group = 8
    kernel = functools.partial(
        cross_kernel, windows=windows, freqs=freqs, group=group, chunk=256
    )
    full3 = lambda g, p: (0, 0, 0)
    out = pl.pallas_call(
        kernel,
        grid_spec=pltpu.PrefetchScalarGridSpec(
            num_scalar_prefetch=1,
            grid=(nrec // group,),
            in_specs=[
                pl.BlockSpec(rec_stack.shape, full3),
                pl.BlockSpec(own_stack.shape, full3),
                pl.BlockSpec(sib_stack.shape, full3),
                pl.BlockSpec(table.shape, lambda g, p: (0, 0)),
            ],
            out_specs=pl.BlockSpec((group * nsrc, lags), lambda g, p: (g, 0)),
            scratch_shapes=[
                pltpu.VMEM((nsrc, windows * 2 * freqs), jnp.float32),
                pltpu.VMEM((nrec, windows * 2 * freqs), jnp.float32),
                pltpu.VMEM((nrec, PAD), jnp.float32),
                pltpu.VMEM((nsrc, PAD), jnp.float32),
                pltpu.VMEM((group * nsrc, 2 * freqs), jnp.bfloat16),
            ],
        ),
        out_shape=jax.ShapeDtypeStruct((nrec * nsrc, lags), jnp.bfloat16),
        compiler_params=pltpu.CompilerParams(dimension_semantics=("arbitrary",)),
    )(place, rec_stack, own_stack, sib_stack, table)
    return out.reshape(nrec, nsrc, lags)


def shifted(x, axis, count, stride):
    parts = [x]
    for shift in range(1, count // stride):
        pairs = [(j, (j + stride * shift) % count) for j in range(count)]
        parts.append(lax.ppermute(x, axis, perm=pairs))
    return jnp.stack(parts)


def local(spectra, valid, rcv_count, src_count):
    channels, windows, _, freqs = spectra.shape
    table = lag_table(freqs, LAGS)
    packed = whiten_pack(spectra, valid)
    rec_stack = shifted(packed, "rcv", rcv_count, 1)
    own_stack = shifted(packed, "src", src_count, 2)
    table, rec_stack, own_stack = lax.optimization_barrier((table, rec_stack, own_stack))
    sib_stack = lax.ppermute(own_stack, "src", perm=[(j, j ^ 1) for j in range(src_count)])
    src_index = lax.axis_index("src")
    place = jnp.stack(
        [lax.axis_index("rcv"), src_index // 2, src_index % 2]
    ).astype(jnp.int32)
    return correlate(place, rec_stack, own_stack, sib_stack, table, windows, freqs)


def solution(mesh):
    return jax.shard_map(
        functools.partial(local, rcv_count=mesh.shape["rcv"], src_count=mesh.shape["src"]),
        mesh=mesh,
        in_specs=(P(("src", "rcv"), None, None, None), P(("src", "rcv"), None)),
        out_specs=P("src", "rcv", None),
        check_vma=False,
    )
```

```python
import functools
import math

import jax
import jax.numpy as jnp
from jax import lax
from jax.experimental import pallas as pl
from jax.experimental.pallas import tpu as pltpu
from jax.sharding import PartitionSpec as P

LAGS = 512
BAND = 32
NSAMP = 7500
PAD = 128

epsilon = 1e-06


def split3(x):
    hi = x.astype(jnp.bfloat16)
    rest = x - hi.astype(jnp.float32)
    mid = rest.astype(jnp.bfloat16)
    lo = (rest - mid.astype(jnp.float32)).astype(jnp.bfloat16)
    return hi, mid, lo


def exact_dot(x, ones):
    return sum(jnp.dot(part, ones, preferred_element_type=jnp.float32) for part in split3(x))


def whiten_kernel(x_ref, v_ref, out_ref, sq_ref, *, channels, windows, freqs):
    bands = freqs // BAND
    band_of = lax.broadcasted_iota(jnp.int32, (freqs, bands), 0) // BAND
    to_band = (band_of == lax.broadcasted_iota(jnp.int32, (freqs, bands), 1)).astype(jnp.bfloat16)
    band_row = lax.broadcasted_iota(jnp.int32, (bands, freqs), 1) // BAND
    from_band = (band_row == lax.broadcasted_iota(jnp.int32, (bands, freqs), 0)).astype(
        jnp.bfloat16
    )
    for c in range(channels):
        for w in range(windows):
            x = x_ref[c, w].astype(jnp.float32)
            row = c * windows + w
            sq_ref[row : row + 1, :] = x[0:1] ** 2 + x[1:2] ** 2
    power = exact_dot(sq_ref[...], to_band) / (2.0 * BAND)
    factor = exact_dot(1.0 / jnp.sqrt(power + epsilon), from_band)
    width = 2 * freqs
    for c in range(channels):
        for w in range(windows):
            x = x_ref[c, w].astype(jnp.float32)
            row = c * windows + w
            scale = factor[row : row + 1, :]
            out_ref[c : c + 1, w * width : w * width + freqs] = (x[0:1] * scale).astype(
                jnp.bfloat16
            )
            out_ref[c : c + 1, w * width + freqs : (w + 1) * width] = (x[1:2] * scale).astype(
                jnp.bfloat16
            )
    body = windows * width
    out_ref[:, body : body + PAD] = v_ref[...].astype(jnp.float32).astype(jnp.bfloat16)


def whiten_pack(spectra, valid):
    channels, windows, _, freqs = spectra.shape
    tail = jnp.pad(valid, ((0, 0), (0, PAD - windows)))
    kernel = functools.partial(whiten_kernel, channels=channels, windows=windows, freqs=freqs)
    return pl.pallas_call(
        kernel,
        out_shape=jax.ShapeDtypeStruct((channels, windows * 2 * freqs + PAD), jnp.bfloat16),
        scratch_shapes=[pltpu.VMEM((channels * windows, freqs), jnp.float32)],
    )(spectra, tail)


def lag_table(freq_count, lag_count):
    step = 64
    shifts = jnp.arange(lag_count, dtype=jnp.int32) - lag_count // 2
    hi = jnp.arange(freq_count // step, dtype=jnp.int32) * step
    lo = jnp.arange(step, dtype=jnp.int32)
    scale = 2.0 * math.pi / NSAMP
    angle_hi = jnp.mod(hi[:, None] * shifts[None, :], NSAMP).astype(jnp.float32) * scale
    angle_lo = jnp.mod(lo[:, None] * shifts[None, :], NSAMP).astype(jnp.float32) * scale
    cos_hi, sin_hi = jnp.cos(angle_hi)[:, None, :], jnp.sin(angle_hi)[:, None, :]
    cos_lo, sin_lo = jnp.cos(angle_lo)[None, :, :], jnp.sin(angle_lo)[None, :, :]
    factor = 1.0 / math.sqrt(2.0 * freq_count)
    cosines = (cos_hi * cos_lo - sin_hi * sin_lo) * factor
    sines = (sin_hi * cos_lo + cos_hi * sin_lo) * (-factor)
    cosines = cosines.reshape(freq_count, lag_count).astype(jnp.bfloat16)
    sines = sines.reshape(freq_count, lag_count).astype(jnp.bfloat16)
    return jnp.stack([cosines, sines], axis=0).reshape(2 * freq_count, lag_count)


def cross_kernel(
    place_ref, rec_ref, own_ref, sib_ref, tab_ref, out_ref, srcf, recf, rtails, stails, cross,
    *, windows, freqs, group, chunk
):
    step = pl.program_id(0)
    rcv_count, per = rec_ref.shape[0], rec_ref.shape[1]
    chips = own_ref.shape[0]
    nsrc = 2 * chips * per
    body = windows * 2 * freqs
    width = 2 * freqs

    def place(block, dst, values, tails, source_side):
        rows = slice(dst * per, (dst + 1) * per)
        mask = block[:, body : body + PAD].astype(jnp.float32)
        tails[rows, :] = mask
        for w in range(windows):
            m = mask[:, w : w + 1]
            a = block[:, w * width : w * width + freqs].astype(jnp.float32) * m
            b = block[:, w * width + freqs : (w + 1) * width].astype(jnp.float32) * m
            if source_side:
                terms = (a, b - a, a + b)
            else:
                terms = (a - b, a, b)
            for t, term in enumerate(terms):
                start = (3 * w + t) * freqs
                values[rows, start : start + freqs] = term

    @pl.when(step == 0)
    def _():
        rcv_index, chip, core = place_ref[0], place_ref[1], place_ref[2]
        for dst in range(rcv_count):
            k = (rcv_index - dst + rcv_count) % rcv_count
            place(rec_ref[k], dst, recf, rtails, False)
        for zz in range(chips):
            k = (chip - zz + chips) % chips
            own_block = own_ref[k]
            sib_block = sib_ref[k]
            for cc in range(2):
                same = core == cc
                block = jnp.where(same, own_block, sib_block)
                place(block, zz * 2 + cc, srcf, stails, True)

    smask = stails[...]

    def per_receiver(j, carry):
        i = step * group + j
        rtail = rtails[pl.ds(i, 1), :]
        count = jnp.sum(smask * rtail, axis=1, keepdims=True)
        inverse = 1.0 / jnp.maximum(count, 1.0)
        rows = pl.ds(pl.multiple_of(j * nsrc, nsrc), nsrc)
        for c in range(freqs // chunk):
            k1 = jnp.zeros((nsrc, chunk), jnp.float32)
            k2 = jnp.zeros((nsrc, chunk), jnp.float32)
            k3 = jnp.zeros((nsrc, chunk), jnp.float32)
            for w in range(windows):
                at = [(3 * w + t) * freqs + c * chunk for t in range(3)]
                sa = srcf[:, at[0] : at[0] + chunk]
                sd = srcf[:, at[1] : at[1] + chunk]
                se = srcf[:, at[2] : at[2] + chunk]
                ru = recf[pl.ds(i, 1), at[0] : at[0] + chunk]
                ra = recf[pl.ds(i, 1), at[1] : at[1] + chunk]
                rb = recf[pl.ds(i, 1), at[2] : at[2] + chunk]
                k1 = k1 + sa * ru
                k2 = k2 + ra * sd
                k3 = k3 + rb * se
            real = (k1 + k3) * inverse
            imag = (k1 + k2) * inverse
            cross[rows, c * chunk : (c + 1) * chunk] = real.astype(jnp.bfloat16)
            cross[rows, freqs + c * chunk : freqs + (c + 1) * chunk] = imag.astype(jnp.bfloat16)
        return carry

    lax.fori_loop(0, group, per_receiver, 0)
    out_ref[...] = jnp.dot(
        cross[...], tab_ref[...], preferred_element_type=jnp.float32
    ).astype(jnp.bfloat16)


def correlate(place, rec_stack, own_stack, sib_stack, table, windows, freqs):
    rcv_count, per, width = rec_stack.shape
    chips = own_stack.shape[0]
    nrec = rcv_count * per
    nsrc = 2 * chips * per
    lags = table.shape[1]
    group = 8
    kernel = functools.partial(
        cross_kernel, windows=windows, freqs=freqs, group=group, chunk=256
    )
    full3 = lambda g, p: (0, 0, 0)
    out = pl.pallas_call(
        kernel,
        grid_spec=pltpu.PrefetchScalarGridSpec(
            num_scalar_prefetch=1,
            grid=(nrec // group,),
            in_specs=[
                pl.BlockSpec(rec_stack.shape, full3),
                pl.BlockSpec(own_stack.shape, full3),
                pl.BlockSpec(sib_stack.shape, full3),
                pl.BlockSpec(table.shape, lambda g, p: (0, 0)),
            ],
            out_specs=pl.BlockSpec((group * nsrc, lags), lambda g, p: (g, 0)),
            scratch_shapes=[
                pltpu.VMEM((nsrc, windows * 3 * freqs), jnp.float32),
                pltpu.VMEM((nrec, windows * 3 * freqs), jnp.float32),
                pltpu.VMEM((nrec, PAD), jnp.float32),
                pltpu.VMEM((nsrc, PAD), jnp.float32),
                pltpu.VMEM((group * nsrc, 2 * freqs), jnp.bfloat16),
            ],
        ),
        out_shape=jax.ShapeDtypeStruct((nrec * nsrc, lags), jnp.bfloat16),
        compiler_params=pltpu.CompilerParams(dimension_semantics=("arbitrary",)),
    )(place, rec_stack, own_stack, sib_stack, table)
    return out.reshape(nrec, nsrc, lags)


def shifted(x, axis, count, stride):
    parts = [x]
    for shift in range(1, count // stride):
        pairs = [(j, (j + stride * shift) % count) for j in range(count)]
        parts.append(lax.ppermute(x, axis, perm=pairs))
    return jnp.stack(parts)


def local(spectra, valid, rcv_count, src_count):
    channels, windows, _, freqs = spectra.shape
    table = lag_table(freqs, LAGS)
    packed = whiten_pack(spectra, valid)
    rec_stack = shifted(packed, "rcv", rcv_count, 1)
    own_stack = shifted(packed, "src", src_count, 2)
    table, rec_stack, own_stack = lax.optimization_barrier((table, rec_stack, own_stack))
    sib_stack = lax.ppermute(own_stack, "src", perm=[(j, j ^ 1) for j in range(src_count)])
    src_index = lax.axis_index("src")
    place = jnp.stack(
        [lax.axis_index("rcv"), src_index // 2, src_index % 2]
    ).astype(jnp.int32)
    return correlate(place, rec_stack, own_stack, sib_stack, table, windows, freqs)


def solution(mesh):
    return jax.shard_map(
        functools.partial(local, rcv_count=mesh.shape["rcv"], src_count=mesh.shape["src"]),
        mesh=mesh,
        in_specs=(P(("src", "rcv"), None, None, None), P(("src", "rcv"), None)),
        out_specs=P("src", "rcv", None),
        check_vma=False,
    )
```

```python
import functools
import math

import jax
import jax.numpy as jnp
from jax import lax
from jax.experimental import pallas as pl
from jax.experimental.pallas import tpu as pltpu
from jax.sharding import PartitionSpec as P

LAGS = 512
BAND = 32
NSAMP = 7500
PAD = 128

epsilon = 1e-06


def split3(x):
    hi = x.astype(jnp.bfloat16)
    rest = x - hi.astype(jnp.float32)
    mid = rest.astype(jnp.bfloat16)
    lo = (rest - mid.astype(jnp.float32)).astype(jnp.bfloat16)
    return hi, mid, lo


def exact_dot(x, ones):
    return sum(jnp.dot(part, ones, preferred_element_type=jnp.float32) for part in split3(x))


def whiten_kernel(x_ref, v_ref, out_ref, sq_ref, *, channels, windows, freqs):
    bands = freqs // BAND
    band_of = lax.broadcasted_iota(jnp.int32, (freqs, bands), 0) // BAND
    to_band = (band_of == lax.broadcasted_iota(jnp.int32, (freqs, bands), 1)).astype(jnp.bfloat16)
    band_row = lax.broadcasted_iota(jnp.int32, (bands, freqs), 1) // BAND
    from_band = (band_row == lax.broadcasted_iota(jnp.int32, (bands, freqs), 0)).astype(
        jnp.bfloat16
    )
    for c in range(channels):
        for w in range(windows):
            x = x_ref[c, w].astype(jnp.float32)
            row = c * windows + w
            sq_ref[row : row + 1, :] = x[0:1] ** 2 + x[1:2] ** 2
    power = exact_dot(sq_ref[...], to_band) / (2.0 * BAND)
    factor = exact_dot(1.0 / jnp.sqrt(power + epsilon), from_band)
    width = 2 * freqs
    for c in range(channels):
        for w in range(windows):
            x = x_ref[c, w].astype(jnp.float32)
            row = c * windows + w
            scale = factor[row : row + 1, :]
            out_ref[c : c + 1, w * width : w * width + freqs] = (x[0:1] * scale).astype(
                jnp.bfloat16
            )
            out_ref[c : c + 1, w * width + freqs : (w + 1) * width] = (x[1:2] * scale).astype(
                jnp.bfloat16
            )
    body = windows * width
    valid = v_ref[...].astype(jnp.float32)
    lane = lax.broadcasted_iota(jnp.int32, (channels, PAD), 1)
    tail = jnp.zeros((channels, PAD), jnp.float32)
    for w in range(windows):
        tail = jnp.where(lane == w, valid[:, w : w + 1], tail)
    out_ref[:, body : body + PAD] = tail.astype(jnp.bfloat16)


def whiten_pack(spectra, valid):
    channels, windows, _, freqs = spectra.shape
    kernel = functools.partial(whiten_kernel, channels=channels, windows=windows, freqs=freqs)
    return pl.pallas_call(
        kernel,
        out_shape=jax.ShapeDtypeStruct((channels, windows * 2 * freqs + PAD), jnp.bfloat16),
        scratch_shapes=[pltpu.VMEM((channels * windows, freqs), jnp.float32)],
    )(spectra, valid)


def lag_table(freq_count, lag_count):
    step = 64
    shifts = jnp.arange(lag_count, dtype=jnp.int32) - lag_count // 2
    hi = jnp.arange(freq_count // step, dtype=jnp.int32) * step
    lo = jnp.arange(step, dtype=jnp.int32)
    scale = 2.0 * math.pi / NSAMP
    angle_hi = jnp.mod(hi[:, None] * shifts[None, :], NSAMP).astype(jnp.float32) * scale
    angle_lo = jnp.mod(lo[:, None] * shifts[None, :], NSAMP).astype(jnp.float32) * scale
    cos_hi, sin_hi = jnp.cos(angle_hi)[:, None, :], jnp.sin(angle_hi)[:, None, :]
    cos_lo, sin_lo = jnp.cos(angle_lo)[None, :, :], jnp.sin(angle_lo)[None, :, :]
    factor = 1.0 / math.sqrt(2.0 * freq_count)
    cosines = (cos_hi * cos_lo - sin_hi * sin_lo) * factor
    sines = (sin_hi * cos_lo + cos_hi * sin_lo) * (-factor)
    cosines = cosines.reshape(freq_count, lag_count).astype(jnp.bfloat16)
    sines = sines.reshape(freq_count, lag_count).astype(jnp.bfloat16)
    return jnp.stack([cosines, sines], axis=0).reshape(2 * freq_count, lag_count)


def cross_kernel(
    place_ref, rec_ref, own_ref, sib_ref, tab_hbm, out_ref, srcf, recf, rtails, stails, cross,
    tab_ref, tab_sem, *, windows, freqs, group, chunk
):
    step = pl.program_id(0)
    rcv_count, per = rec_ref.shape[0], rec_ref.shape[1]
    chips = own_ref.shape[0]
    nsrc = 2 * chips * per
    body = windows * 2 * freqs
    width = 2 * freqs

    def place(block, dst, values, tails, source_side):
        rows = slice(dst * per, (dst + 1) * per)
        mask = block[:, body : body + PAD].astype(jnp.float32)
        tails[rows, :] = mask
        for w in range(windows):
            m = mask[:, w : w + 1]
            a = block[:, w * width : w * width + freqs].astype(jnp.float32) * m
            b = block[:, w * width + freqs : (w + 1) * width].astype(jnp.float32) * m
            if source_side:
                terms = (a, b - a, a + b)
            else:
                terms = (a - b, a, b)
            for t, term in enumerate(terms):
                start = (3 * w + t) * freqs
                values[rows, start : start + freqs] = term

    @pl.when(step == 0)
    def _():
        pltpu.make_async_copy(tab_hbm, tab_ref, tab_sem).start()

    @pl.when(step == 0)
    def _():
        rcv_index, chip, core = place_ref[0], place_ref[1], place_ref[2]
        for dst in range(rcv_count):
            k = (rcv_index - dst + rcv_count) % rcv_count
            place(rec_ref[k], dst, recf, rtails, False)
        for zz in range(chips):
            k = (chip - zz + chips) % chips
            own_block = own_ref[k]
            sib_block = sib_ref[k]
            for cc in range(2):
                same = core == cc
                block = jnp.where(same, own_block, sib_block)
                place(block, zz * 2 + cc, srcf, stails, True)

    smask = stails[...]

    def per_receiver(j, carry):
        i = step * group + j
        rtail = rtails[pl.ds(i, 1), :]
        count = jnp.sum(smask * rtail, axis=1, keepdims=True)
        inverse = 1.0 / jnp.maximum(count, 1.0)
        rows = pl.ds(pl.multiple_of(j * nsrc, nsrc), nsrc)
        for c in range(freqs // chunk):
            k1 = jnp.zeros((nsrc, chunk), jnp.float32)
            k2 = jnp.zeros((nsrc, chunk), jnp.float32)
            k3 = jnp.zeros((nsrc, chunk), jnp.float32)
            for w in range(windows):
                at = [(3 * w + t) * freqs + c * chunk for t in range(3)]
                sa = srcf[:, at[0] : at[0] + chunk]
                sd = srcf[:, at[1] : at[1] + chunk]
                se = srcf[:, at[2] : at[2] + chunk]
                ru = recf[pl.ds(i, 1), at[0] : at[0] + chunk]
                ra = recf[pl.ds(i, 1), at[1] : at[1] + chunk]
                rb = recf[pl.ds(i, 1), at[2] : at[2] + chunk]
                k1 = k1 + sa * ru
                k2 = k2 + ra * sd
                k3 = k3 + rb * se
            real = (k1 + k3) * inverse
            imag = (k1 + k2) * inverse
            cross[rows, c * chunk : (c + 1) * chunk] = real.astype(jnp.bfloat16)
            cross[rows, freqs + c * chunk : freqs + (c + 1) * chunk] = imag.astype(jnp.bfloat16)
        return carry

    lax.fori_loop(0, group, per_receiver, 0)

    @pl.when(step == 0)
    def _():
        pltpu.make_async_copy(tab_hbm, tab_ref, tab_sem).wait()

    out_ref[...] = jnp.dot(
        cross[...], tab_ref[...], preferred_element_type=jnp.float32
    ).astype(jnp.bfloat16)


def correlate(place, rec_stack, own_stack, sib_stack, table, windows, freqs):
    rcv_count, per, width = rec_stack.shape
    chips = own_stack.shape[0]
    nrec = rcv_count * per
    nsrc = 2 * chips * per
    lags = table.shape[1]
    group = 8
    kernel = functools.partial(
        cross_kernel, windows=windows, freqs=freqs, group=group, chunk=256
    )
    full3 = lambda g, p: (0, 0, 0)
    out = pl.pallas_call(
        kernel,
        grid_spec=pltpu.PrefetchScalarGridSpec(
            num_scalar_prefetch=1,
            grid=(nrec // group,),
            in_specs=[
                pl.BlockSpec(rec_stack.shape, full3),
                pl.BlockSpec(own_stack.shape, full3),
                pl.BlockSpec(sib_stack.shape, full3),
                pl.BlockSpec(memory_space=pl.ANY),
            ],
            out_specs=pl.BlockSpec((group * nsrc, lags), lambda g, p: (g, 0)),
            scratch_shapes=[
                pltpu.VMEM((nsrc, windows * 3 * freqs), jnp.float32),
                pltpu.VMEM((nrec, windows * 3 * freqs), jnp.float32),
                pltpu.VMEM((nrec, PAD), jnp.float32),
                pltpu.VMEM((nsrc, PAD), jnp.float32),
                pltpu.VMEM((group * nsrc, 2 * freqs), jnp.bfloat16),
                pltpu.VMEM(table.shape, jnp.bfloat16),
                pltpu.SemaphoreType.DMA(()),
            ],
        ),
        out_shape=jax.ShapeDtypeStruct((nrec * nsrc, lags), jnp.bfloat16),
        compiler_params=pltpu.CompilerParams(dimension_semantics=("arbitrary",)),
    )(place, rec_stack, own_stack, sib_stack, table)
    return out.reshape(nrec, nsrc, lags)


def shifted(x, axis, count, stride):
    parts = [x]
    for shift in range(1, count // stride):
        pairs = [(j, (j + stride * shift) % count) for j in range(count)]
        parts.append(lax.ppermute(x, axis, perm=pairs))
    return jnp.stack(parts)


def local(spectra, valid, rcv_count, src_count):
    channels, windows, _, freqs = spectra.shape
    table = lag_table(freqs, LAGS)
    packed = whiten_pack(spectra, valid)
    rec_stack = shifted(packed, "rcv", rcv_count, 1)
    own_stack = shifted(packed, "src", src_count, 2)
    table, rec_stack, own_stack = lax.optimization_barrier((table, rec_stack, own_stack))
    sib_stack = lax.ppermute(own_stack, "src", perm=[(j, j ^ 1) for j in range(src_count)])
    src_index = lax.axis_index("src")
    place = jnp.stack(
        [lax.axis_index("rcv"), src_index // 2, src_index % 2]
    ).astype(jnp.int32)
    return correlate(place, rec_stack, own_stack, sib_stack, table, windows, freqs)


def solution(mesh):
    return jax.shard_map(
        functools.partial(local, rcv_count=mesh.shape["rcv"], src_count=mesh.shape["src"]),
        mesh=mesh,
        in_specs=(P(("src", "rcv"), None, None, None), P(("src", "rcv"), None)),
        out_specs=P("src", "rcv", None),
        check_vma=False,
    )
```

```python
import functools
import math

import jax
import jax.numpy as jnp
from jax import lax
from jax.experimental import pallas as pl
from jax.experimental.pallas import tpu as pltpu
from jax.sharding import PartitionSpec as P

LAGS = 512
BAND = 32
NSAMP = 7500
PAD = 128

epsilon = 1e-06


def split3(x):
    hi = x.astype(jnp.bfloat16)
    rest = x - hi.astype(jnp.float32)
    mid = rest.astype(jnp.bfloat16)
    lo = (rest - mid.astype(jnp.float32)).astype(jnp.bfloat16)
    return hi, mid, lo


def exact_dot(x, ones):
    return sum(jnp.dot(part, ones, preferred_element_type=jnp.float32) for part in split3(x))


def whiten_kernel(x_ref, v_ref, out_ref, sq_ref, *, channels, windows, freqs):
    bands = freqs // BAND
    band_of = lax.broadcasted_iota(jnp.int32, (freqs, bands), 0) // BAND
    to_band = (band_of == lax.broadcasted_iota(jnp.int32, (freqs, bands), 1)).astype(jnp.bfloat16)
    band_row = lax.broadcasted_iota(jnp.int32, (bands, freqs), 1) // BAND
    from_band = (band_row == lax.broadcasted_iota(jnp.int32, (bands, freqs), 0)).astype(
        jnp.bfloat16
    )
    for c in range(channels):
        for w in range(windows):
            x = x_ref[c, w].astype(jnp.float32)
            row = c * windows + w
            sq_ref[row : row + 1, :] = x[0:1] ** 2 + x[1:2] ** 2
    power = exact_dot(sq_ref[...], to_band) / (2.0 * BAND)
    factor = exact_dot(1.0 / jnp.sqrt(power + epsilon), from_band)
    width = 2 * freqs
    for c in range(channels):
        for w in range(windows):
            x = x_ref[c, w].astype(jnp.float32)
            row = c * windows + w
            scale = factor[row : row + 1, :]
            out_ref[c : c + 1, w * width : w * width + freqs] = (x[0:1] * scale).astype(
                jnp.bfloat16
            )
            out_ref[c : c + 1, w * width + freqs : (w + 1) * width] = (x[1:2] * scale).astype(
                jnp.bfloat16
            )
    body = windows * width
    valid = v_ref[...].astype(jnp.float32)
    lane = lax.broadcasted_iota(jnp.int32, (channels, PAD), 1)
    tail = jnp.zeros((channels, PAD), jnp.float32)
    for w in range(windows):
        tail = jnp.where(lane == w, valid[:, w : w + 1], tail)
    out_ref[:, body : body + PAD] = tail.astype(jnp.bfloat16)


def whiten_pack(spectra, valid):
    channels, windows, _, freqs = spectra.shape
    kernel = functools.partial(whiten_kernel, channels=channels, windows=windows, freqs=freqs)
    return pl.pallas_call(
        kernel,
        out_shape=jax.ShapeDtypeStruct((channels, windows * 2 * freqs + PAD), jnp.bfloat16),
        scratch_shapes=[pltpu.VMEM((channels * windows, freqs), jnp.float32)],
    )(spectra, valid)


def lag_table(freq_count, lag_count):
    step = 64
    shifts = jnp.arange(lag_count, dtype=jnp.int32) - lag_count // 2
    hi = jnp.arange(freq_count // step, dtype=jnp.int32) * step
    lo = jnp.arange(step, dtype=jnp.int32)
    scale = 2.0 * math.pi / NSAMP
    angle_hi = jnp.mod(hi[:, None] * shifts[None, :], NSAMP).astype(jnp.float32) * scale
    angle_lo = jnp.mod(lo[:, None] * shifts[None, :], NSAMP).astype(jnp.float32) * scale
    cos_hi, sin_hi = jnp.cos(angle_hi)[:, None, :], jnp.sin(angle_hi)[:, None, :]
    cos_lo, sin_lo = jnp.cos(angle_lo)[None, :, :], jnp.sin(angle_lo)[None, :, :]
    factor = 1.0 / math.sqrt(2.0 * freq_count)
    cosines = (cos_hi * cos_lo - sin_hi * sin_lo) * factor
    sines = (sin_hi * cos_lo + cos_hi * sin_lo) * (-factor)
    cosines = cosines.reshape(freq_count, lag_count).astype(jnp.bfloat16)
    sines = sines.reshape(freq_count, lag_count).astype(jnp.bfloat16)
    return jnp.stack([cosines, sines], axis=0).reshape(2 * freq_count, lag_count)


def cross_kernel(
    place_ref, rec_ref, own_ref, sib_ref, tab_hbm, out_ref, srcf, recf, rtails, stails, cross,
    tab_ref, tab_sem, *, windows, freqs, group, chunk
):
    step = pl.program_id(0)
    rcv_count, per = rec_ref.shape[0], rec_ref.shape[1]
    chips = own_ref.shape[0]
    nsrc = 2 * chips * per
    body = windows * 2 * freqs
    width = 2 * freqs

    def place(block, dst, values, tails, source_side):
        rows = slice(dst * per, (dst + 1) * per)
        mask = block[:, body : body + PAD].astype(jnp.float32)
        tails[rows, :] = mask
        for w in range(windows):
            m = mask[:, w : w + 1]
            a = block[:, w * width : w * width + freqs].astype(jnp.float32) * m
            b = block[:, w * width + freqs : (w + 1) * width].astype(jnp.float32) * m
            if source_side:
                terms = (a, b - a, a + b)
            else:
                terms = (a - b, a, b)
            for t, term in enumerate(terms):
                start = (3 * w + t) * freqs
                values[rows, start : start + freqs] = term

    @pl.when(step == 0)
    def _():
        pltpu.make_async_copy(tab_hbm, tab_ref, tab_sem).start()

    @pl.when(step == 0)
    def _():
        core = place_ref[0]
        for dst in range(rcv_count):
            place(rec_ref[dst], dst, recf, rtails, False)
        for zz in range(chips):
            own_block = own_ref[zz]
            sib_block = sib_ref[zz]
            for cc in range(2):
                same = core == cc
                block = jnp.where(same, own_block, sib_block)
                place(block, zz * 2 + cc, srcf, stails, True)

    smask = stails[...]

    def per_receiver(j, carry):
        i = step * group + j
        rtail = rtails[pl.ds(i, 1), :]
        count = jnp.sum(smask * rtail, axis=1, keepdims=True)
        inverse = 1.0 / jnp.maximum(count, 1.0)
        rows = pl.ds(pl.multiple_of(j * nsrc, nsrc), nsrc)
        for c in range(freqs // chunk):
            k1 = jnp.zeros((nsrc, chunk), jnp.float32)
            k2 = jnp.zeros((nsrc, chunk), jnp.float32)
            k3 = jnp.zeros((nsrc, chunk), jnp.float32)
            for w in range(windows):
                at = [(3 * w + t) * freqs + c * chunk for t in range(3)]
                sa = srcf[:, at[0] : at[0] + chunk]
                sd = srcf[:, at[1] : at[1] + chunk]
                se = srcf[:, at[2] : at[2] + chunk]
                ru = recf[pl.ds(i, 1), at[0] : at[0] + chunk]
                ra = recf[pl.ds(i, 1), at[1] : at[1] + chunk]
                rb = recf[pl.ds(i, 1), at[2] : at[2] + chunk]
                k1 = k1 + sa * ru
                k2 = k2 + ra * sd
                k3 = k3 + rb * se
            real = (k1 + k3) * inverse
            imag = (k1 + k2) * inverse
            cross[rows, c * chunk : (c + 1) * chunk] = real.astype(jnp.bfloat16)
            cross[rows, freqs + c * chunk : freqs + (c + 1) * chunk] = imag.astype(jnp.bfloat16)
        return carry

    lax.fori_loop(0, group, per_receiver, 0)

    @pl.when(step == 0)
    def _():
        pltpu.make_async_copy(tab_hbm, tab_ref, tab_sem).wait()

    out_ref[...] = jnp.dot(
        cross[...], tab_ref[...], preferred_element_type=jnp.float32
    ).astype(jnp.bfloat16)


def correlate(place, rec_stack, own_stack, sib_stack, table, windows, freqs):
    rcv_count, per, width = rec_stack.shape
    chips = own_stack.shape[0]
    nrec = rcv_count * per
    nsrc = 2 * chips * per
    lags = table.shape[1]
    group = 8
    kernel = functools.partial(
        cross_kernel, windows=windows, freqs=freqs, group=group, chunk=256
    )
    full3 = lambda g, p: (0, 0, 0)
    out = pl.pallas_call(
        kernel,
        grid_spec=pltpu.PrefetchScalarGridSpec(
            num_scalar_prefetch=1,
            grid=(nrec // group,),
            in_specs=[
                pl.BlockSpec(rec_stack.shape, full3),
                pl.BlockSpec(own_stack.shape, full3),
                pl.BlockSpec(sib_stack.shape, full3),
                pl.BlockSpec(memory_space=pl.ANY),
            ],
            out_specs=pl.BlockSpec((group * nsrc, lags), lambda g, p: (g, 0)),
            scratch_shapes=[
                pltpu.VMEM((nsrc, windows * 3 * freqs), jnp.float32),
                pltpu.VMEM((nrec, windows * 3 * freqs), jnp.float32),
                pltpu.VMEM((nrec, PAD), jnp.float32),
                pltpu.VMEM((nsrc, PAD), jnp.float32),
                pltpu.VMEM((group * nsrc, 2 * freqs), jnp.bfloat16),
                pltpu.VMEM(table.shape, jnp.bfloat16),
                pltpu.SemaphoreType.DMA(()),
            ],
        ),
        out_shape=jax.ShapeDtypeStruct((nrec * nsrc, lags), jnp.bfloat16),
        compiler_params=pltpu.CompilerParams(dimension_semantics=("arbitrary",)),
    )(place, rec_stack, own_stack, sib_stack, table)
    return out.reshape(nrec, nsrc, lags)


def doubling(x, axis, count, first):
    index = lax.axis_index(axis)
    blocks = x[None]
    bit = first
    while bit < count:
        other = lax.ppermute(blocks, axis, perm=[(j, j ^ bit) for j in range(count)])
        low = (index & bit) == 0
        blocks = jnp.concatenate(
            [jnp.where(low, blocks, other), jnp.where(low, other, blocks)], axis=0
        )
        bit *= 2
    return blocks


def local(spectra, valid, rcv_count, src_count):
    channels, windows, _, freqs = spectra.shape
    table = lag_table(freqs, LAGS)
    packed = whiten_pack(spectra, valid)
    rec_stack = doubling(packed, "rcv", rcv_count, 1)
    own_stack = doubling(packed, "src", src_count, 2)
    table, rec_stack, own_stack = lax.optimization_barrier((table, rec_stack, own_stack))
    sib_stack = lax.ppermute(own_stack, "src", perm=[(j, j ^ 1) for j in range(src_count)])
    core = lax.axis_index("src") % 2
    place = jnp.stack([core]).astype(jnp.int32)
    return correlate(place, rec_stack, own_stack, sib_stack, table, windows, freqs)


def solution(mesh):
    return jax.shard_map(
        functools.partial(local, rcv_count=mesh.shape["rcv"], src_count=mesh.shape["src"]),
        mesh=mesh,
        in_specs=(P(("src", "rcv"), None, None, None), P(("src", "rcv"), None)),
        out_specs=P("src", "rcv", None),
        check_vma=False,
    )
```

```python
import functools
import math

import jax
import jax.numpy as jnp
from jax import lax
from jax.experimental import pallas as pl
from jax.experimental.pallas import tpu as pltpu
from jax.sharding import PartitionSpec as P

LAGS = 512
BAND = 32
NSAMP = 7500
PAD = 128

epsilon = 1e-06


def split3(x):
    hi = x.astype(jnp.bfloat16)
    rest = x - hi.astype(jnp.float32)
    mid = rest.astype(jnp.bfloat16)
    lo = (rest - mid.astype(jnp.float32)).astype(jnp.bfloat16)
    return hi, mid, lo


def exact_dot(x, ones):
    return sum(jnp.dot(part, ones, preferred_element_type=jnp.float32) for part in split3(x))


def whiten_kernel(x_ref, v_ref, out_ref, sq_ref, *, channels, windows, freqs):
    bands = freqs // BAND
    band_of = lax.broadcasted_iota(jnp.int32, (freqs, bands), 0) // BAND
    to_band = (band_of == lax.broadcasted_iota(jnp.int32, (freqs, bands), 1)).astype(jnp.bfloat16)
    band_row = lax.broadcasted_iota(jnp.int32, (bands, freqs), 1) // BAND
    from_band = (band_row == lax.broadcasted_iota(jnp.int32, (bands, freqs), 0)).astype(
        jnp.bfloat16
    )
    for c in range(channels):
        for w in range(windows):
            x = x_ref[c, w].astype(jnp.float32)
            row = c * windows + w
            sq_ref[row : row + 1, :] = x[0:1] ** 2 + x[1:2] ** 2
    power = exact_dot(sq_ref[...], to_band) / (2.0 * BAND)
    factor = exact_dot(1.0 / jnp.sqrt(power + epsilon), from_band)
    width = 2 * freqs
    for c in range(channels):
        for w in range(windows):
            x = x_ref[c, w].astype(jnp.float32)
            row = c * windows + w
            scale = factor[row : row + 1, :]
            out_ref[c : c + 1, w * width : w * width + freqs] = (x[0:1] * scale).astype(
                jnp.bfloat16
            )
            out_ref[c : c + 1, w * width + freqs : (w + 1) * width] = (x[1:2] * scale).astype(
                jnp.bfloat16
            )
    body = windows * width
    valid = v_ref[...].astype(jnp.float32)
    lane = lax.broadcasted_iota(jnp.int32, (channels, PAD), 1)
    tail = jnp.zeros((channels, PAD), jnp.float32)
    for w in range(windows):
        tail = jnp.where(lane == w, valid[:, w : w + 1], tail)
    out_ref[:, body : body + PAD] = tail.astype(jnp.bfloat16)


def whiten_pack(spectra, valid):
    channels, windows, _, freqs = spectra.shape
    kernel = functools.partial(whiten_kernel, channels=channels, windows=windows, freqs=freqs)
    return pl.pallas_call(
        kernel,
        out_shape=jax.ShapeDtypeStruct((channels, windows * 2 * freqs + PAD), jnp.bfloat16),
        scratch_shapes=[pltpu.VMEM((channels * windows, freqs), jnp.float32)],
    )(spectra, valid)


def lag_table(freq_count, lag_count):
    step = 64
    shifts = jnp.arange(lag_count, dtype=jnp.int32) - lag_count // 2
    hi = jnp.arange(freq_count // step, dtype=jnp.int32) * step
    lo = jnp.arange(step, dtype=jnp.int32)
    scale = 2.0 * math.pi / NSAMP
    angle_hi = jnp.mod(hi[:, None] * shifts[None, :], NSAMP).astype(jnp.float32) * scale
    angle_lo = jnp.mod(lo[:, None] * shifts[None, :], NSAMP).astype(jnp.float32) * scale
    cos_hi, sin_hi = jnp.cos(angle_hi)[:, None, :], jnp.sin(angle_hi)[:, None, :]
    cos_lo, sin_lo = jnp.cos(angle_lo)[None, :, :], jnp.sin(angle_lo)[None, :, :]
    factor = 1.0 / math.sqrt(2.0 * freq_count)
    cosines = (cos_hi * cos_lo - sin_hi * sin_lo) * factor
    sines = (sin_hi * cos_lo + cos_hi * sin_lo) * (-factor)
    cosines = cosines.reshape(freq_count, lag_count).astype(jnp.bfloat16)
    sines = sines.reshape(freq_count, lag_count).astype(jnp.bfloat16)
    return jnp.stack([cosines, sines], axis=0).reshape(2 * freq_count, lag_count)


def cross_kernel(
    place_ref, rec_ref, own_ref, sib_ref, tab_hbm, out_ref, srcf, recf, rtails, stails, cross,
    tab_ref, tab_sem, *, windows, freqs, group, chunk
):
    step = pl.program_id(0)
    rcv_count, per = rec_ref.shape[0], rec_ref.shape[1]
    chips = own_ref.shape[0]
    nsrc = 2 * chips * per
    body = windows * 2 * freqs
    width = 2 * freqs

    def place(block, dst, values, tails, source_side):
        rows = slice(dst * per, (dst + 1) * per)
        mask = block[:, body : body + PAD].astype(jnp.float32)
        tails[rows, :] = mask
        for w in range(windows):
            m = mask[:, w : w + 1]
            a = block[:, w * width : w * width + freqs].astype(jnp.float32) * m
            b = block[:, w * width + freqs : (w + 1) * width].astype(jnp.float32) * m
            if source_side:
                terms = (a, b - a, a + b)
            else:
                terms = (a - b, a, b)
            for t, term in enumerate(terms):
                start = (3 * w + t) * freqs
                values[rows, start : start + freqs] = term

    @pl.when(step == 0)
    def _():
        pltpu.make_async_copy(tab_hbm, tab_ref, tab_sem).start()

    @pl.when(step == 0)
    def _():
        rcv_index, chip, core = place_ref[0], place_ref[1], place_ref[2]
        for rot in range(rcv_count):

            @pl.when(rcv_index == rot)
            def _():
                for dst in range(rcv_count):
                    place(rec_ref[(rot - dst) % rcv_count], dst, recf, rtails, False)

        for rot in range(chips):
            for mine in range(2):

                @pl.when((chip == rot) & (core == mine))
                def _():
                    for zz in range(chips):
                        k = (rot - zz) % chips
                        place(own_ref[k], zz * 2 + mine, srcf, stails, True)
                        place(sib_ref[k], zz * 2 + 1 - mine, srcf, stails, True)

    smask = stails[...]

    def per_receiver(j, carry):
        i = step * group + j
        rtail = rtails[pl.ds(i, 1), :]
        count = jnp.sum(smask * rtail, axis=1, keepdims=True)
        inverse = 1.0 / jnp.maximum(count, 1.0)
        rows = pl.ds(pl.multiple_of(j * nsrc, nsrc), nsrc)
        for c in range(freqs // chunk):
            k1 = jnp.zeros((nsrc, chunk), jnp.float32)
            k2 = jnp.zeros((nsrc, chunk), jnp.float32)
            k3 = jnp.zeros((nsrc, chunk), jnp.float32)
            for w in range(windows):
                at = [(3 * w + t) * freqs + c * chunk for t in range(3)]
                sa = srcf[:, at[0] : at[0] + chunk]
                sd = srcf[:, at[1] : at[1] + chunk]
                se = srcf[:, at[2] : at[2] + chunk]
                ru = recf[pl.ds(i, 1), at[0] : at[0] + chunk]
                ra = recf[pl.ds(i, 1), at[1] : at[1] + chunk]
                rb = recf[pl.ds(i, 1), at[2] : at[2] + chunk]
                k1 = k1 + sa * ru
                k2 = k2 + ra * sd
                k3 = k3 + rb * se
            real = (k1 + k3) * inverse
            imag = (k1 + k2) * inverse
            cross[rows, c * chunk : (c + 1) * chunk] = real.astype(jnp.bfloat16)
            cross[rows, freqs + c * chunk : freqs + (c + 1) * chunk] = imag.astype(jnp.bfloat16)
        return carry

    lax.fori_loop(0, group, per_receiver, 0)

    @pl.when(step == 0)
    def _():
        pltpu.make_async_copy(tab_hbm, tab_ref, tab_sem).wait()

    out_ref[...] = jnp.dot(
        cross[...], tab_ref[...], preferred_element_type=jnp.float32
    ).astype(jnp.bfloat16)


def correlate(place, rec_stack, own_stack, sib_stack, table, windows, freqs):
    rcv_count, per, width = rec_stack.shape
    chips = own_stack.shape[0]
    nrec = rcv_count * per
    nsrc = 2 * chips * per
    lags = table.shape[1]
    group = 8
    kernel = functools.partial(
        cross_kernel, windows=windows, freqs=freqs, group=group, chunk=256
    )
    full3 = lambda g, p: (0, 0, 0)
    out = pl.pallas_call(
        kernel,
        grid_spec=pltpu.PrefetchScalarGridSpec(
            num_scalar_prefetch=1,
            grid=(nrec // group,),
            in_specs=[
                pl.BlockSpec(rec_stack.shape, full3),
                pl.BlockSpec(own_stack.shape, full3),
                pl.BlockSpec(sib_stack.shape, full3),
                pl.BlockSpec(memory_space=pl.ANY),
            ],
            out_specs=pl.BlockSpec((group * nsrc, lags), lambda g, p: (g, 0)),
            scratch_shapes=[
                pltpu.VMEM((nsrc, windows * 3 * freqs), jnp.float32),
                pltpu.VMEM((nrec, windows * 3 * freqs), jnp.float32),
                pltpu.VMEM((nrec, PAD), jnp.float32),
                pltpu.VMEM((nsrc, PAD), jnp.float32),
                pltpu.VMEM((group * nsrc, 2 * freqs), jnp.bfloat16),
                pltpu.VMEM(table.shape, jnp.bfloat16),
                pltpu.SemaphoreType.DMA(()),
            ],
        ),
        out_shape=jax.ShapeDtypeStruct((nrec * nsrc, lags), jnp.bfloat16),
        compiler_params=pltpu.CompilerParams(dimension_semantics=("arbitrary",)),
    )(place, rec_stack, own_stack, sib_stack, table)
    return out.reshape(nrec, nsrc, lags)


def shifted(x, axis, count, stride):
    parts = [x]
    for shift in range(1, count // stride):
        pairs = [(j, (j + stride * shift) % count) for j in range(count)]
        parts.append(lax.ppermute(x, axis, perm=pairs))
    return jnp.stack(parts)


def local(spectra, valid, rcv_count, src_count):
    channels, windows, _, freqs = spectra.shape
    table = lag_table(freqs, LAGS)
    packed = whiten_pack(spectra, valid)
    rec_stack = shifted(packed, "rcv", rcv_count, 1)
    own_stack = shifted(packed, "src", src_count, 2)
    table, rec_stack, own_stack = lax.optimization_barrier((table, rec_stack, own_stack))
    sib_stack = lax.ppermute(own_stack, "src", perm=[(j, j ^ 1) for j in range(src_count)])
    src_index = lax.axis_index("src")
    place = jnp.stack(
        [lax.axis_index("rcv"), src_index // 2, src_index % 2]
    ).astype(jnp.int32)
    return correlate(place, rec_stack, own_stack, sib_stack, table, windows, freqs)


def solution(mesh):
    return jax.shard_map(
        functools.partial(local, rcv_count=mesh.shape["rcv"], src_count=mesh.shape["src"]),
        mesh=mesh,
        in_specs=(P(("src", "rcv"), None, None, None), P(("src", "rcv"), None)),
        out_specs=P("src", "rcv", None),
        check_vma=False,
    )
```

```python
import functools
import math

import jax
import jax.numpy as jnp
from jax import lax
from jax.experimental import pallas as pl
from jax.experimental.pallas import tpu as pltpu
from jax.sharding import PartitionSpec as P

LAGS = 512
BAND = 32
NSAMP = 7500
PAD = 128

epsilon = 1e-06


def split3(x):
    hi = x.astype(jnp.bfloat16)
    rest = x - hi.astype(jnp.float32)
    mid = rest.astype(jnp.bfloat16)
    lo = (rest - mid.astype(jnp.float32)).astype(jnp.bfloat16)
    return hi, mid, lo


def exact_dot(x, ones):
    return sum(jnp.dot(part, ones, preferred_element_type=jnp.float32) for part in split3(x))


def whiten_kernel(x_ref, v_ref, out_ref, sq_ref, *, channels, windows, freqs):
    bands = freqs // BAND
    band_of = lax.broadcasted_iota(jnp.int32, (freqs, bands), 0) // BAND
    to_band = (band_of == lax.broadcasted_iota(jnp.int32, (freqs, bands), 1)).astype(jnp.bfloat16)
    band_row = lax.broadcasted_iota(jnp.int32, (bands, freqs), 1) // BAND
    from_band = (band_row == lax.broadcasted_iota(jnp.int32, (bands, freqs), 0)).astype(
        jnp.bfloat16
    )
    for c in range(channels):
        for w in range(windows):
            x = x_ref[c, w].astype(jnp.float32)
            row = c * windows + w
            sq_ref[row : row + 1, :] = x[0:1] ** 2 + x[1:2] ** 2
    power = exact_dot(sq_ref[...], to_band) / (2.0 * BAND)
    factor = exact_dot(1.0 / jnp.sqrt(power + epsilon), from_band)
    width = 2 * freqs
    for c in range(channels):
        for w in range(windows):
            x = x_ref[c, w].astype(jnp.float32)
            row = c * windows + w
            scale = factor[row : row + 1, :]
            out_ref[c : c + 1, w * width : w * width + freqs] = (x[0:1] * scale).astype(
                jnp.bfloat16
            )
            out_ref[c : c + 1, w * width + freqs : (w + 1) * width] = (x[1:2] * scale).astype(
                jnp.bfloat16
            )
    body = windows * width
    valid = v_ref[...].astype(jnp.float32)
    lane = lax.broadcasted_iota(jnp.int32, (channels, PAD), 1)
    tail = jnp.zeros((channels, PAD), jnp.float32)
    for w in range(windows):
        tail = jnp.where(lane == w, valid[:, w : w + 1], tail)
    out_ref[:, body : body + PAD] = tail.astype(jnp.bfloat16)


def whiten_pack(spectra, valid):
    channels, windows, _, freqs = spectra.shape
    kernel = functools.partial(whiten_kernel, channels=channels, windows=windows, freqs=freqs)
    return pl.pallas_call(
        kernel,
        out_shape=jax.ShapeDtypeStruct((channels, windows * 2 * freqs + PAD), jnp.bfloat16),
        scratch_shapes=[pltpu.VMEM((channels * windows, freqs), jnp.float32)],
    )(spectra, valid)


def lag_table(freq_count, lag_count):
    step = 64
    shifts = jnp.arange(lag_count, dtype=jnp.int32) - lag_count // 2
    hi = jnp.arange(freq_count // step, dtype=jnp.int32) * step
    lo = jnp.arange(step, dtype=jnp.int32)
    scale = 2.0 * math.pi / NSAMP
    angle_hi = jnp.mod(hi[:, None] * shifts[None, :], NSAMP).astype(jnp.float32) * scale
    angle_lo = jnp.mod(lo[:, None] * shifts[None, :], NSAMP).astype(jnp.float32) * scale
    cos_hi, sin_hi = jnp.cos(angle_hi)[:, None, :], jnp.sin(angle_hi)[:, None, :]
    cos_lo, sin_lo = jnp.cos(angle_lo)[None, :, :], jnp.sin(angle_lo)[None, :, :]
    factor = 1.0 / math.sqrt(2.0 * freq_count)
    cosines = (cos_hi * cos_lo - sin_hi * sin_lo) * factor
    sines = (sin_hi * cos_lo + cos_hi * sin_lo) * (-factor)
    cosines = cosines.reshape(freq_count, lag_count).astype(jnp.bfloat16)
    sines = sines.reshape(freq_count, lag_count).astype(jnp.bfloat16)
    return jnp.stack([cosines, sines], axis=0).reshape(2 * freq_count, lag_count)


def cross_kernel(
    place_ref, rec_ref, own_ref, sib_ref, tab_hbm, out_ref, srcf, recf, rtails, stails, cross,
    tab_ref, tab_sem, *, windows, freqs, group, chunk
):
    step = pl.program_id(0)
    rcv_count, per = rec_ref.shape[0], rec_ref.shape[1]
    chips = own_ref.shape[0]
    nsrc = 2 * chips * per
    body = windows * 2 * freqs
    width = 2 * freqs

    def place(block, dst, values, tails, source_side):
        rows = slice(dst * per, (dst + 1) * per)
        mask = block[:, body : body + PAD].astype(jnp.float32)
        tails[rows, :] = mask
        for w in range(windows):
            m = mask[:, w : w + 1]
            a = block[:, w * width : w * width + freqs].astype(jnp.float32) * m
            b = block[:, w * width + freqs : (w + 1) * width].astype(jnp.float32) * m
            if source_side:
                terms = (a, b - a, a + b)
            else:
                terms = (a - b, a, b)
            for t, term in enumerate(terms):
                start = (3 * w + t) * freqs
                values[rows, start : start + freqs] = term

    @pl.when(step == 0)
    def _():
        pltpu.make_async_copy(tab_hbm, tab_ref, tab_sem).start()

    @pl.when(step == 0)
    def _():
        rcv_index, chip, core = place_ref[0], place_ref[1], place_ref[2]
        for rot in range(rcv_count):

            @pl.when(rcv_index == rot)
            def _():
                for dst in range(rcv_count):
                    place(rec_ref[(rot - dst) % rcv_count], dst, recf, rtails, False)

        for mine in range(2):
            if True:

                @pl.when(core == mine)
                def _():
                    for zz in range(chips):
                        place(own_ref[zz], zz * 2 + mine, srcf, stails, True)
                        place(sib_ref[zz], zz * 2 + 1 - mine, srcf, stails, True)

    smask = stails[...]

    def per_receiver(j, carry):
        i = step * group + j
        rtail = rtails[pl.ds(i, 1), :]
        count = jnp.sum(smask * rtail, axis=1, keepdims=True)
        inverse = 1.0 / jnp.maximum(count, 1.0)
        rows = pl.ds(pl.multiple_of(j * nsrc, nsrc), nsrc)
        for c in range(freqs // chunk):
            k1 = jnp.zeros((nsrc, chunk), jnp.float32)
            k2 = jnp.zeros((nsrc, chunk), jnp.float32)
            k3 = jnp.zeros((nsrc, chunk), jnp.float32)
            for w in range(windows):
                at = [(3 * w + t) * freqs + c * chunk for t in range(3)]
                sa = srcf[:, at[0] : at[0] + chunk]
                sd = srcf[:, at[1] : at[1] + chunk]
                se = srcf[:, at[2] : at[2] + chunk]
                ru = recf[pl.ds(i, 1), at[0] : at[0] + chunk]
                ra = recf[pl.ds(i, 1), at[1] : at[1] + chunk]
                rb = recf[pl.ds(i, 1), at[2] : at[2] + chunk]
                k1 = k1 + sa * ru
                k2 = k2 + ra * sd
                k3 = k3 + rb * se
            real = (k1 + k3) * inverse
            imag = (k1 + k2) * inverse
            cross[rows, c * chunk : (c + 1) * chunk] = real.astype(jnp.bfloat16)
            cross[rows, freqs + c * chunk : freqs + (c + 1) * chunk] = imag.astype(jnp.bfloat16)
        return carry

    lax.fori_loop(0, group, per_receiver, 0)

    @pl.when(step == 0)
    def _():
        pltpu.make_async_copy(tab_hbm, tab_ref, tab_sem).wait()

    out_ref[...] = jnp.dot(
        cross[...], tab_ref[...], preferred_element_type=jnp.float32
    ).astype(jnp.bfloat16)


def correlate(place, rec_stack, own_stack, sib_stack, table, windows, freqs):
    rcv_count, per, width = rec_stack.shape
    chips = own_stack.shape[0]
    nrec = rcv_count * per
    nsrc = 2 * chips * per
    lags = table.shape[1]
    group = 8
    kernel = functools.partial(
        cross_kernel, windows=windows, freqs=freqs, group=group, chunk=256
    )
    full3 = lambda g, p: (0, 0, 0)
    out = pl.pallas_call(
        kernel,
        grid_spec=pltpu.PrefetchScalarGridSpec(
            num_scalar_prefetch=1,
            grid=(nrec // group,),
            in_specs=[
                pl.BlockSpec(rec_stack.shape, full3),
                pl.BlockSpec(own_stack.shape, full3),
                pl.BlockSpec(sib_stack.shape, full3),
                pl.BlockSpec(memory_space=pl.ANY),
            ],
            out_specs=pl.BlockSpec((group * nsrc, lags), lambda g, p: (g, 0)),
            scratch_shapes=[
                pltpu.VMEM((nsrc, windows * 3 * freqs), jnp.float32),
                pltpu.VMEM((nrec, windows * 3 * freqs), jnp.float32),
                pltpu.VMEM((nrec, PAD), jnp.float32),
                pltpu.VMEM((nsrc, PAD), jnp.float32),
                pltpu.VMEM((group * nsrc, 2 * freqs), jnp.bfloat16),
                pltpu.VMEM(table.shape, jnp.bfloat16),
                pltpu.SemaphoreType.DMA(()),
            ],
        ),
        out_shape=jax.ShapeDtypeStruct((nrec * nsrc, lags), jnp.bfloat16),
        compiler_params=pltpu.CompilerParams(dimension_semantics=("arbitrary",)),
    )(place, rec_stack, own_stack, sib_stack, table)
    return out.reshape(nrec, nsrc, lags)


def shifted(x, axis, count, stride):
    parts = [x]
    for shift in range(1, count // stride):
        pairs = [(j, (j + stride * shift) % count) for j in range(count)]
        parts.append(lax.ppermute(x, axis, perm=pairs))
    return jnp.stack(parts)


def forwarded(x, axis, count):
    chips = count // 2
    up = [(j, j + 2) for j in range(count - 2)]
    down = [(j + 2, j) for j in range(count - 2)]
    left, right = [x], [x]
    for _ in range(1, chips):
        left.append(lax.ppermute(left[-1], axis, perm=up))
        right.append(lax.ppermute(right[-1], axis, perm=down))
    sequence = jnp.stack(left[:0:-1] + right)
    chip = lax.axis_index(axis) // 2
    return lax.dynamic_slice_in_dim(sequence, chips - 1 - chip, chips, axis=0)


def local(spectra, valid, rcv_count, src_count):
    channels, windows, _, freqs = spectra.shape
    table = lag_table(freqs, LAGS)
    packed = whiten_pack(spectra, valid)
    rec_stack = shifted(packed, "rcv", rcv_count, 1)
    own_stack = forwarded(packed, "src", src_count)
    table, rec_stack, own_stack = lax.optimization_barrier((table, rec_stack, own_stack))
    sib_stack = lax.ppermute(own_stack, "src", perm=[(j, j ^ 1) for j in range(src_count)])
    src_index = lax.axis_index("src")
    place = jnp.stack(
        [lax.axis_index("rcv"), src_index // 2, src_index % 2]
    ).astype(jnp.int32)
    return correlate(place, rec_stack, own_stack, sib_stack, table, windows, freqs)


def solution(mesh):
    return jax.shard_map(
        functools.partial(local, rcv_count=mesh.shape["rcv"], src_count=mesh.shape["src"]),
        mesh=mesh,
        in_specs=(P(("src", "rcv"), None, None, None), P(("src", "rcv"), None)),
        out_specs=P("src", "rcv", None),
        check_vma=False,
    )
```

```python
import functools
import math

import jax
import jax.numpy as jnp
from jax import lax
from jax.experimental import pallas as pl
from jax.experimental.pallas import tpu as pltpu
from jax.sharding import PartitionSpec as P

LAGS = 512
BAND = 32
NSAMP = 7500
PAD = 128

epsilon = 1e-06


def split3(x):
    hi = x.astype(jnp.bfloat16)
    rest = x - hi.astype(jnp.float32)
    mid = rest.astype(jnp.bfloat16)
    lo = (rest - mid.astype(jnp.float32)).astype(jnp.bfloat16)
    return hi, mid, lo


def exact_dot(x, ones):
    return sum(jnp.dot(part, ones, preferred_element_type=jnp.float32) for part in split3(x))


def whiten_kernel(x_ref, v_ref, out_ref, sq_ref, *, channels, windows, freqs):
    bands = freqs // BAND
    band_of = lax.broadcasted_iota(jnp.int32, (freqs, bands), 0) // BAND
    to_band = (band_of == lax.broadcasted_iota(jnp.int32, (freqs, bands), 1)).astype(jnp.bfloat16)
    band_row = lax.broadcasted_iota(jnp.int32, (bands, freqs), 1) // BAND
    from_band = (band_row == lax.broadcasted_iota(jnp.int32, (bands, freqs), 0)).astype(
        jnp.bfloat16
    )
    for c in range(channels):
        for w in range(windows):
            x = x_ref[c, w].astype(jnp.float32)
            row = c * windows + w
            sq_ref[row : row + 1, :] = x[0:1] ** 2 + x[1:2] ** 2
    power = exact_dot(sq_ref[...], to_band) / (2.0 * BAND)
    factor = exact_dot(1.0 / jnp.sqrt(power + epsilon), from_band)
    width = 2 * freqs
    for c in range(channels):
        for w in range(windows):
            x = x_ref[c, w].astype(jnp.float32)
            row = c * windows + w
            scale = factor[row : row + 1, :]
            out_ref[c : c + 1, w * width : w * width + freqs] = (x[0:1] * scale).astype(
                jnp.bfloat16
            )
            out_ref[c : c + 1, w * width + freqs : (w + 1) * width] = (x[1:2] * scale).astype(
                jnp.bfloat16
            )
    body = windows * width
    valid = v_ref[...].astype(jnp.float32)
    lane = lax.broadcasted_iota(jnp.int32, (channels, PAD), 1)
    tail = jnp.zeros((channels, PAD), jnp.float32)
    for w in range(windows):
        tail = jnp.where(lane == w, valid[:, w : w + 1], tail)
    out_ref[:, body : body + PAD] = tail.astype(jnp.bfloat16)


def whiten_pack(spectra, valid):
    channels, windows, _, freqs = spectra.shape
    kernel = functools.partial(whiten_kernel, channels=channels, windows=windows, freqs=freqs)
    return pl.pallas_call(
        kernel,
        out_shape=jax.ShapeDtypeStruct((channels, windows * 2 * freqs + PAD), jnp.bfloat16),
        scratch_shapes=[pltpu.VMEM((channels * windows, freqs), jnp.float32)],
    )(spectra, valid)


def lag_table(freq_count, lag_count):
    step = 64
    shifts = jnp.arange(lag_count, dtype=jnp.int32) - lag_count // 2
    hi = jnp.arange(freq_count // step, dtype=jnp.int32) * step
    lo = jnp.arange(step, dtype=jnp.int32)
    scale = 2.0 * math.pi / NSAMP
    angle_hi = jnp.mod(hi[:, None] * shifts[None, :], NSAMP).astype(jnp.float32) * scale
    angle_lo = jnp.mod(lo[:, None] * shifts[None, :], NSAMP).astype(jnp.float32) * scale
    cos_hi, sin_hi = jnp.cos(angle_hi)[:, None, :], jnp.sin(angle_hi)[:, None, :]
    cos_lo, sin_lo = jnp.cos(angle_lo)[None, :, :], jnp.sin(angle_lo)[None, :, :]
    factor = 1.0 / math.sqrt(2.0 * freq_count)
    cosines = (cos_hi * cos_lo - sin_hi * sin_lo) * factor
    sines = (sin_hi * cos_lo + cos_hi * sin_lo) * (-factor)
    cosines = cosines.reshape(freq_count, lag_count).astype(jnp.bfloat16)
    sines = sines.reshape(freq_count, lag_count).astype(jnp.bfloat16)
    return jnp.stack([cosines, sines], axis=0).reshape(2 * freq_count, lag_count)


def cross_kernel(
    place_ref, rec_ref, own_ref, sib_ref, tab_hbm, out_ref, srcf, recf, rtails, stails, cross,
    tab_ref, tab_sem, *, windows, freqs, group, chunk
):
    step = pl.program_id(0)
    rcv_count, per = rec_ref.shape[0], rec_ref.shape[1]
    chips = own_ref.shape[0]
    nsrc = 2 * chips * per
    body = windows * 2 * freqs
    width = 2 * freqs

    def place(block, dst, values, tails, source_side):
        rows = slice(dst * per, (dst + 1) * per)
        mask = block[:, body : body + PAD].astype(jnp.float32)
        tails[rows, :] = mask
        for w in range(windows):
            m = mask[:, w : w + 1]
            a = block[:, w * width : w * width + freqs].astype(jnp.float32) * m
            b = block[:, w * width + freqs : (w + 1) * width].astype(jnp.float32) * m
            if source_side:
                terms = (a, b - a, a + b)
            else:
                terms = (a - b, a, b)
            for t, term in enumerate(terms):
                start = (3 * w + t) * freqs
                values[rows, start : start + freqs] = term

    @pl.when(step == 0)
    def _():
        pltpu.make_async_copy(tab_hbm, tab_ref, tab_sem).start()

    @pl.when(step == 0)
    def _():
        rcv_index, chip, core = place_ref[0], place_ref[1], place_ref[2]
        for dst in range(rcv_count):
            place(rec_ref[dst], dst, recf, rtails, False)

        for rot in range(chips):
            for mine in range(2):

                @pl.when((chip == rot) & (core == mine))
                def _():
                    for zz in range(chips):
                        k = (rot - zz) % chips
                        place(own_ref[k], zz * 2 + mine, srcf, stails, True)
                        place(sib_ref[k], zz * 2 + 1 - mine, srcf, stails, True)

    smask = stails[...]

    def per_receiver(j, carry):
        i = step * group + j
        rtail = rtails[pl.ds(i, 1), :]
        count = jnp.sum(smask * rtail, axis=1, keepdims=True)
        inverse = 1.0 / jnp.maximum(count, 1.0)
        rows = pl.ds(pl.multiple_of(j * nsrc, nsrc), nsrc)
        for c in range(freqs // chunk):
            k1 = jnp.zeros((nsrc, chunk), jnp.float32)
            k2 = jnp.zeros((nsrc, chunk), jnp.float32)
            k3 = jnp.zeros((nsrc, chunk), jnp.float32)
            for w in range(windows):
                at = [(3 * w + t) * freqs + c * chunk for t in range(3)]
                sa = srcf[:, at[0] : at[0] + chunk]
                sd = srcf[:, at[1] : at[1] + chunk]
                se = srcf[:, at[2] : at[2] + chunk]
                ru = recf[pl.ds(i, 1), at[0] : at[0] + chunk]
                ra = recf[pl.ds(i, 1), at[1] : at[1] + chunk]
                rb = recf[pl.ds(i, 1), at[2] : at[2] + chunk]
                k1 = k1 + sa * ru
                k2 = k2 + ra * sd
                k3 = k3 + rb * se
            real = (k1 + k3) * inverse
            imag = (k1 + k2) * inverse
            cross[rows, c * chunk : (c + 1) * chunk] = real.astype(jnp.bfloat16)
            cross[rows, freqs + c * chunk : freqs + (c + 1) * chunk] = imag.astype(jnp.bfloat16)
        return carry

    lax.fori_loop(0, group, per_receiver, 0)

    @pl.when(step == 0)
    def _():
        pltpu.make_async_copy(tab_hbm, tab_ref, tab_sem).wait()

    out_ref[...] = jnp.dot(
        cross[...], tab_ref[...], preferred_element_type=jnp.float32
    ).astype(jnp.bfloat16)


def correlate(place, rec_stack, own_stack, sib_stack, table, windows, freqs):
    rcv_count, per, width = rec_stack.shape
    chips = own_stack.shape[0]
    nrec = rcv_count * per
    nsrc = 2 * chips * per
    lags = table.shape[1]
    group = 8
    kernel = functools.partial(
        cross_kernel, windows=windows, freqs=freqs, group=group, chunk=256
    )
    full3 = lambda g, p: (0, 0, 0)
    out = pl.pallas_call(
        kernel,
        grid_spec=pltpu.PrefetchScalarGridSpec(
            num_scalar_prefetch=1,
            grid=(nrec // group,),
            in_specs=[
                pl.BlockSpec(rec_stack.shape, full3),
                pl.BlockSpec(own_stack.shape, full3),
                pl.BlockSpec(sib_stack.shape, full3),
                pl.BlockSpec(memory_space=pl.ANY),
            ],
            out_specs=pl.BlockSpec((group * nsrc, lags), lambda g, p: (g, 0)),
            scratch_shapes=[
                pltpu.VMEM((nsrc, windows * 3 * freqs), jnp.float32),
                pltpu.VMEM((nrec, windows * 3 * freqs), jnp.float32),
                pltpu.VMEM((nrec, PAD), jnp.float32),
                pltpu.VMEM((nsrc, PAD), jnp.float32),
                pltpu.VMEM((group * nsrc, 2 * freqs), jnp.bfloat16),
                pltpu.VMEM(table.shape, jnp.bfloat16),
                pltpu.SemaphoreType.DMA(()),
            ],
        ),
        out_shape=jax.ShapeDtypeStruct((nrec * nsrc, lags), jnp.bfloat16),
        compiler_params=pltpu.CompilerParams(dimension_semantics=("arbitrary",)),
    )(place, rec_stack, own_stack, sib_stack, table)
    return out.reshape(nrec, nsrc, lags)


def shifted(x, axis, count, stride):
    parts = [x]
    for shift in range(1, count // stride):
        pairs = [(j, (j + stride * shift) % count) for j in range(count)]
        parts.append(lax.ppermute(x, axis, perm=pairs))
    return jnp.stack(parts)


def local(spectra, valid, rcv_count, src_count):
    channels, windows, _, freqs = spectra.shape
    table = lag_table(freqs, LAGS)
    packed = whiten_pack(spectra, valid)
    copies = jnp.broadcast_to(packed[None], (rcv_count,) + packed.shape)
    rec_stack = lax.all_to_all(copies, "rcv", 0, 0, tiled=True)
    own_stack = shifted(packed, "src", src_count, 2)
    table, rec_stack, own_stack = lax.optimization_barrier((table, rec_stack, own_stack))
    sib_stack = lax.ppermute(own_stack, "src", perm=[(j, j ^ 1) for j in range(src_count)])
    src_index = lax.axis_index("src")
    place = jnp.stack(
        [lax.axis_index("rcv"), src_index // 2, src_index % 2]
    ).astype(jnp.int32)
    return correlate(place, rec_stack, own_stack, sib_stack, table, windows, freqs)


def solution(mesh):
    return jax.shard_map(
        functools.partial(local, rcv_count=mesh.shape["rcv"], src_count=mesh.shape["src"]),
        mesh=mesh,
        in_specs=(P(("src", "rcv"), None, None, None), P(("src", "rcv"), None)),
        out_specs=P("src", "rcv", None),
        check_vma=False,
    )
```

```python
import functools
import math

import jax
import jax.numpy as jnp
from jax import lax
from jax.experimental import pallas as pl
from jax.experimental.pallas import tpu as pltpu
from jax.sharding import PartitionSpec as P

LAGS = 512
BAND = 32
NSAMP = 7500
PAD = 128

epsilon = 1e-06


def split3(x):
    hi = x.astype(jnp.bfloat16)
    rest = x - hi.astype(jnp.float32)
    mid = rest.astype(jnp.bfloat16)
    lo = (rest - mid.astype(jnp.float32)).astype(jnp.bfloat16)
    return hi, mid, lo


def exact_dot(x, ones):
    return sum(jnp.dot(part, ones, preferred_element_type=jnp.float32) for part in split3(x))


def whiten_kernel(x_ref, v_ref, out_ref, sq_ref, *, channels, windows, freqs):
    bands = freqs // BAND
    band_of = lax.broadcasted_iota(jnp.int32, (freqs, bands), 0) // BAND
    to_band = (band_of == lax.broadcasted_iota(jnp.int32, (freqs, bands), 1)).astype(jnp.bfloat16)
    band_row = lax.broadcasted_iota(jnp.int32, (bands, freqs), 1) // BAND
    from_band = (band_row == lax.broadcasted_iota(jnp.int32, (bands, freqs), 0)).astype(
        jnp.bfloat16
    )
    for c in range(channels):
        for w in range(windows):
            x = x_ref[c, w].astype(jnp.float32)
            row = c * windows + w
            sq_ref[row : row + 1, :] = x[0:1] ** 2 + x[1:2] ** 2
    power = exact_dot(sq_ref[...], to_band) / (2.0 * BAND)
    factor = exact_dot(1.0 / jnp.sqrt(power + epsilon), from_band)
    width = 2 * freqs
    for c in range(channels):
        for w in range(windows):
            x = x_ref[c, w].astype(jnp.float32)
            row = c * windows + w
            scale = factor[row : row + 1, :]
            out_ref[c : c + 1, w * width : w * width + freqs] = (x[0:1] * scale).astype(
                jnp.bfloat16
            )
            out_ref[c : c + 1, w * width + freqs : (w + 1) * width] = (x[1:2] * scale).astype(
                jnp.bfloat16
            )
    body = windows * width
    valid = v_ref[...].astype(jnp.float32)
    lane = lax.broadcasted_iota(jnp.int32, (channels, PAD), 1)
    tail = jnp.zeros((channels, PAD), jnp.float32)
    for w in range(windows):
        tail = jnp.where(lane == w, valid[:, w : w + 1], tail)
    out_ref[:, body : body + PAD] = tail.astype(jnp.bfloat16)


def whiten_pack(spectra, valid):
    channels, windows, _, freqs = spectra.shape
    kernel = functools.partial(whiten_kernel, channels=channels, windows=windows, freqs=freqs)
    return pl.pallas_call(
        kernel,
        out_shape=jax.ShapeDtypeStruct((channels, windows * 2 * freqs + PAD), jnp.bfloat16),
        scratch_shapes=[pltpu.VMEM((channels * windows, freqs), jnp.float32)],
    )(spectra, valid)


def lag_table(freq_count, lag_count):
    step = 64
    shifts = jnp.arange(lag_count, dtype=jnp.int32) - lag_count // 2
    hi = jnp.arange(freq_count // step, dtype=jnp.int32) * step
    lo = jnp.arange(step, dtype=jnp.int32)
    scale = 2.0 * math.pi / NSAMP
    angle_hi = jnp.mod(hi[:, None] * shifts[None, :], NSAMP).astype(jnp.float32) * scale
    angle_lo = jnp.mod(lo[:, None] * shifts[None, :], NSAMP).astype(jnp.float32) * scale
    cos_hi, sin_hi = jnp.cos(angle_hi)[:, None, :], jnp.sin(angle_hi)[:, None, :]
    cos_lo, sin_lo = jnp.cos(angle_lo)[None, :, :], jnp.sin(angle_lo)[None, :, :]
    factor = 1.0 / math.sqrt(2.0 * freq_count)
    cosines = (cos_hi * cos_lo - sin_hi * sin_lo) * factor
    sines = (sin_hi * cos_lo + cos_hi * sin_lo) * (-factor)
    cosines = cosines.reshape(freq_count, lag_count).astype(jnp.bfloat16)
    sines = sines.reshape(freq_count, lag_count).astype(jnp.bfloat16)
    return jnp.stack([cosines, sines], axis=0).reshape(2 * freq_count, lag_count)


def cross_kernel(
    place_ref, rec_ref, own_ref, sib_ref, tab_hbm, out_ref, srcf, recf, rtails, stails, cross,
    tab_ref, tab_sem, *, windows, freqs, group, chunk
):
    step = pl.program_id(0)
    rcv_count, per = rec_ref.shape[0], rec_ref.shape[1]
    chips = own_ref.shape[0]
    nsrc = 2 * chips * per
    body = windows * 2 * freqs
    width = 2 * freqs

    def place(block, dst, values, tails, source_side):
        rows = slice(dst * per, (dst + 1) * per)
        mask = block[:, body : body + PAD].astype(jnp.float32)
        tails[rows, :] = mask
        for w in range(windows):
            m = mask[:, w : w + 1]
            a = block[:, w * width : w * width + freqs].astype(jnp.float32) * m
            b = block[:, w * width + freqs : (w + 1) * width].astype(jnp.float32) * m
            if source_side:
                terms = (a, b - a, a + b)
            else:
                terms = (a - b, a, b)
            for t, term in enumerate(terms):
                start = (3 * w + t) * freqs
                values[rows, start : start + freqs] = term

    @pl.when(step == 0)
    def _():
        pltpu.make_async_copy(tab_hbm, tab_ref, tab_sem).start()

    @pl.when(step == 0)
    def _():
        rcv_index, chip, core = place_ref[0], place_ref[1], place_ref[2]
        for rot in range(rcv_count):

            @pl.when(rcv_index == rot)
            def _():
                for dst in range(rcv_count):
                    place(rec_ref[(rot - dst) % rcv_count], dst, recf, rtails, False)

        for rot in range(chips):
            for mine in range(2):

                @pl.when((chip == rot) & (core == mine))
                def _():
                    for zz in range(chips):
                        k = (rot - zz) % chips
                        place(own_ref[k], zz * 2 + mine, srcf, stails, True)
                        place(sib_ref[k], zz * 2 + 1 - mine, srcf, stails, True)

    smask = stails[...]

    def per_receiver(j, carry):
        i = step * group + j
        rtail = rtails[pl.ds(i, 1), :]
        count = jnp.sum(smask * rtail, axis=1, keepdims=True)
        inverse = 1.0 / jnp.maximum(count, 1.0)
        rows = pl.ds(pl.multiple_of(j * nsrc, nsrc), nsrc)
        for c in range(freqs // chunk):
            k1 = jnp.zeros((nsrc, chunk), jnp.float32)
            k2 = jnp.zeros((nsrc, chunk), jnp.float32)
            k3 = jnp.zeros((nsrc, chunk), jnp.float32)
            for w in range(windows):
                at = [(3 * w + t) * freqs + c * chunk for t in range(3)]
                sa = srcf[:, at[0] : at[0] + chunk]
                sd = srcf[:, at[1] : at[1] + chunk]
                se = srcf[:, at[2] : at[2] + chunk]
                ru = recf[pl.ds(i, 1), at[0] : at[0] + chunk]
                ra = recf[pl.ds(i, 1), at[1] : at[1] + chunk]
                rb = recf[pl.ds(i, 1), at[2] : at[2] + chunk]
                k1 = k1 + sa * ru
                k2 = k2 + ra * sd
                k3 = k3 + rb * se
            real = (k1 + k3) * inverse
            imag = (k1 + k2) * inverse
            cross[rows, c * chunk : (c + 1) * chunk] = real.astype(jnp.bfloat16)
            cross[rows, freqs + c * chunk : freqs + (c + 1) * chunk] = imag.astype(jnp.bfloat16)
        return carry

    lax.fori_loop(0, group, per_receiver, 0)

    @pl.when(step == 0)
    def _():
        pltpu.make_async_copy(tab_hbm, tab_ref, tab_sem).wait()

    out_ref[...] = jnp.dot(
        cross[...], tab_ref[...], preferred_element_type=jnp.float32
    ).astype(jnp.bfloat16)


def correlate(place, rec_stack, own_stack, sib_stack, table, windows, freqs):
    rcv_count, per, width = rec_stack.shape
    chips = own_stack.shape[0]
    nrec = rcv_count * per
    nsrc = 2 * chips * per
    lags = table.shape[1]
    group = 8
    kernel = functools.partial(
        cross_kernel, windows=windows, freqs=freqs, group=group, chunk=256
    )
    full3 = lambda g, p: (0, 0, 0)
    out = pl.pallas_call(
        kernel,
        grid_spec=pltpu.PrefetchScalarGridSpec(
            num_scalar_prefetch=1,
            grid=(nrec // group,),
            in_specs=[
                pl.BlockSpec(rec_stack.shape, full3),
                pl.BlockSpec(own_stack.shape, full3),
                pl.BlockSpec(sib_stack.shape, full3),
                pl.BlockSpec(memory_space=pl.ANY),
            ],
            out_specs=pl.BlockSpec((group * nsrc, lags), lambda g, p: (g, 0)),
            scratch_shapes=[
                pltpu.VMEM((nsrc, windows * 3 * freqs), jnp.float32),
                pltpu.VMEM((nrec, windows * 3 * freqs), jnp.float32),
                pltpu.VMEM((nrec, PAD), jnp.float32),
                pltpu.VMEM((nsrc, PAD), jnp.float32),
                pltpu.VMEM((group * nsrc, 2 * freqs), jnp.bfloat16),
                pltpu.VMEM(table.shape, jnp.bfloat16),
                pltpu.SemaphoreType.DMA(()),
            ],
        ),
        out_shape=jax.ShapeDtypeStruct((nrec * nsrc, lags), jnp.bfloat16),
        compiler_params=pltpu.CompilerParams(dimension_semantics=("arbitrary",)),
    )(place, rec_stack, own_stack, sib_stack, table)
    return out.reshape(nrec, nsrc, lags)


def shifted(x, axis, count, stride):
    parts = [x]
    for shift in range(1, count // stride):
        pairs = [(j, (j + stride * shift) % count) for j in range(count)]
        parts.append(lax.ppermute(x, axis, perm=pairs))
    stack = jnp.zeros((len(parts),) + x.shape, x.dtype)
    for k, part in enumerate(parts):
        stack = lax.dynamic_update_slice_in_dim(stack, part[None], k, axis=0)
    return stack


def local(spectra, valid, rcv_count, src_count):
    channels, windows, _, freqs = spectra.shape
    table = lag_table(freqs, LAGS)
    packed = whiten_pack(spectra, valid)
    rec_stack = shifted(packed, "rcv", rcv_count, 1)
    own_stack = shifted(packed, "src", src_count, 2)
    table, rec_stack, own_stack = lax.optimization_barrier((table, rec_stack, own_stack))
    sib_stack = lax.ppermute(own_stack, "src", perm=[(j, j ^ 1) for j in range(src_count)])
    src_index = lax.axis_index("src")
    place = jnp.stack(
        [lax.axis_index("rcv"), src_index // 2, src_index % 2]
    ).astype(jnp.int32)
    return correlate(place, rec_stack, own_stack, sib_stack, table, windows, freqs)


def solution(mesh):
    return jax.shard_map(
        functools.partial(local, rcv_count=mesh.shape["rcv"], src_count=mesh.shape["src"]),
        mesh=mesh,
        in_specs=(P(("src", "rcv"), None, None, None), P(("src", "rcv"), None)),
        out_specs=P("src", "rcv", None),
        check_vma=False,
    )
```

```python
import functools
import math

import jax
import jax.numpy as jnp
from jax import lax
from jax.experimental import pallas as pl
from jax.experimental.pallas import tpu as pltpu
from jax.sharding import PartitionSpec as P

LAGS = 512
BAND = 32
NSAMP = 7500
PAD = 128

epsilon = 1e-06


def split3(x):
    hi = x.astype(jnp.bfloat16)
    rest = x - hi.astype(jnp.float32)
    mid = rest.astype(jnp.bfloat16)
    lo = (rest - mid.astype(jnp.float32)).astype(jnp.bfloat16)
    return hi, mid, lo


def exact_dot(x, ones):
    return sum(jnp.dot(part, ones, preferred_element_type=jnp.float32) for part in split3(x))


def whiten_kernel(x_ref, v_ref, out_ref, sq_ref, *, channels, windows, freqs):
    bands = freqs // BAND
    band_of = lax.broadcasted_iota(jnp.int32, (freqs, bands), 0) // BAND
    to_band = (band_of == lax.broadcasted_iota(jnp.int32, (freqs, bands), 1)).astype(jnp.bfloat16)
    band_row = lax.broadcasted_iota(jnp.int32, (bands, freqs), 1) // BAND
    from_band = (band_row == lax.broadcasted_iota(jnp.int32, (bands, freqs), 0)).astype(
        jnp.bfloat16
    )
    for c in range(channels):
        for w in range(windows):
            x = x_ref[c, w].astype(jnp.float32)
            row = c * windows + w
            sq_ref[row : row + 1, :] = x[0:1] ** 2 + x[1:2] ** 2
    power = exact_dot(sq_ref[...], to_band) / (2.0 * BAND)
    factor = exact_dot(1.0 / jnp.sqrt(power + epsilon), from_band)
    width = 2 * freqs
    for c in range(channels):
        for w in range(windows):
            x = x_ref[c, w].astype(jnp.float32)
            row = c * windows + w
            scale = factor[row : row + 1, :]
            out_ref[c : c + 1, w * width : w * width + freqs] = (x[0:1] * scale).astype(
                jnp.bfloat16
            )
            out_ref[c : c + 1, w * width + freqs : (w + 1) * width] = (x[1:2] * scale).astype(
                jnp.bfloat16
            )
    body = windows * width
    valid = v_ref[...].astype(jnp.float32)
    lane = lax.broadcasted_iota(jnp.int32, (channels, PAD), 1)
    tail = jnp.zeros((channels, PAD), jnp.float32)
    for w in range(windows):
        tail = jnp.where(lane == w, valid[:, w : w + 1], tail)
    out_ref[:, body : body + PAD] = tail.astype(jnp.bfloat16)


def whiten_pack(spectra, valid):
    channels, windows, _, freqs = spectra.shape
    kernel = functools.partial(whiten_kernel, channels=channels, windows=windows, freqs=freqs)
    return pl.pallas_call(
        kernel,
        out_shape=jax.ShapeDtypeStruct((channels, windows * 2 * freqs + PAD), jnp.bfloat16),
        scratch_shapes=[pltpu.VMEM((channels * windows, freqs), jnp.float32)],
    )(spectra, valid)


def lag_table(freq_count, lag_count):
    step = 64
    shifts = jnp.arange(lag_count, dtype=jnp.int32) - lag_count // 2
    hi = jnp.arange(freq_count // step, dtype=jnp.int32) * step
    lo = jnp.arange(step, dtype=jnp.int32)
    scale = 2.0 * math.pi / NSAMP
    angle_hi = jnp.mod(hi[:, None] * shifts[None, :], NSAMP).astype(jnp.float32) * scale
    angle_lo = jnp.mod(lo[:, None] * shifts[None, :], NSAMP).astype(jnp.float32) * scale
    cos_hi, sin_hi = jnp.cos(angle_hi)[:, None, :], jnp.sin(angle_hi)[:, None, :]
    cos_lo, sin_lo = jnp.cos(angle_lo)[None, :, :], jnp.sin(angle_lo)[None, :, :]
    factor = 1.0 / math.sqrt(2.0 * freq_count)
    cosines = (cos_hi * cos_lo - sin_hi * sin_lo) * factor
    sines = (sin_hi * cos_lo + cos_hi * sin_lo) * (-factor)
    cosines = cosines.reshape(freq_count, lag_count).astype(jnp.bfloat16)
    sines = sines.reshape(freq_count, lag_count).astype(jnp.bfloat16)
    return jnp.stack([cosines, sines], axis=0).reshape(2 * freq_count, lag_count)


def cross_kernel(
    place_ref, rec_ref, own_ref, sib_ref, tab_hbm, out_ref, srcf, recf, rtails, stails, cross,
    tab_ref, tab_sem, *, windows, freqs, group, chunk
):
    step = pl.program_id(0)
    rcv_count, per = rec_ref.shape[0], rec_ref.shape[1]
    chips = own_ref.shape[0]
    nsrc = 2 * chips * per
    body = windows * 2 * freqs
    width = 2 * freqs

    def place(block, dst, values, tails, source_side):
        rows = slice(dst * per, (dst + 1) * per)
        mask = block[:, body : body + PAD].astype(jnp.float32)
        tails[rows, :] = mask
        for w in range(windows):
            m = mask[:, w : w + 1]
            a = block[:, w * width : w * width + freqs].astype(jnp.float32) * m
            b = block[:, w * width + freqs : (w + 1) * width].astype(jnp.float32) * m
            if source_side:
                terms = (a, b - a, a + b)
            else:
                terms = (a - b, a, b)
            for t, term in enumerate(terms):
                start = (3 * w + t) * freqs
                values[rows, start : start + freqs] = term

    @pl.when(step == 0)
    def _():
        pltpu.make_async_copy(tab_hbm, tab_ref, tab_sem).start()

    @pl.when(step == 0)
    def _():
        rcv_index, chip, core = place_ref[0], place_ref[1], place_ref[2]
        for rot in range(rcv_count):

            @pl.when(rcv_index == rot)
            def _():
                for dst in range(rcv_count):
                    place(rec_ref[(rot - dst) % rcv_count], dst, recf, rtails, False)

        for rot in range(chips):
            for mine in range(2):

                @pl.when((chip == rot) & (core == mine))
                def _():
                    for zz in range(chips):
                        k = (rot - zz) % chips
                        place(own_ref[k], zz * 2 + mine, srcf, stails, True)
                        place(sib_ref[k], zz * 2 + 1 - mine, srcf, stails, True)

    smask = stails[...]

    def per_receiver(j, carry):
        i = step * group + j
        rtail = rtails[pl.ds(i, 1), :]
        count = jnp.sum(smask * rtail, axis=1, keepdims=True)
        inverse = 1.0 / jnp.maximum(count, 1.0)
        rows = pl.ds(pl.multiple_of(j * nsrc, nsrc), nsrc)
        for c in range(freqs // chunk):
            k1 = jnp.zeros((nsrc, chunk), jnp.float32)
            k2 = jnp.zeros((nsrc, chunk), jnp.float32)
            k3 = jnp.zeros((nsrc, chunk), jnp.float32)
            for w in range(windows):
                at = [(3 * w + t) * freqs + c * chunk for t in range(3)]
                sa = srcf[:, at[0] : at[0] + chunk]
                sd = srcf[:, at[1] : at[1] + chunk]
                se = srcf[:, at[2] : at[2] + chunk]
                ru = recf[pl.ds(i, 1), at[0] : at[0] + chunk]
                ra = recf[pl.ds(i, 1), at[1] : at[1] + chunk]
                rb = recf[pl.ds(i, 1), at[2] : at[2] + chunk]
                k1 = k1 + sa * ru
                k2 = k2 + ra * sd
                k3 = k3 + rb * se
            real = (k1 + k3) * inverse
            imag = (k1 + k2) * inverse
            cross[rows, c * chunk : (c + 1) * chunk] = real.astype(jnp.bfloat16)
            cross[rows, freqs + c * chunk : freqs + (c + 1) * chunk] = imag.astype(jnp.bfloat16)
        return carry

    lax.fori_loop(0, group, per_receiver, 0)

    @pl.when(step == 0)
    def _():
        pltpu.make_async_copy(tab_hbm, tab_ref, tab_sem).wait()

    out_ref[...] = jnp.dot(
        cross[...], tab_ref[...], preferred_element_type=jnp.float32
    ).astype(jnp.bfloat16)


def correlate(place, rec_stack, own_stack, sib_stack, table, windows, freqs):
    rcv_count, per, width = rec_stack.shape
    chips = own_stack.shape[0]
    nrec = rcv_count * per
    nsrc = 2 * chips * per
    lags = table.shape[1]
    group = 8
    kernel = functools.partial(
        cross_kernel, windows=windows, freqs=freqs, group=group, chunk=256
    )
    full3 = lambda g, p: (0, 0, 0)
    out = pl.pallas_call(
        kernel,
        grid_spec=pltpu.PrefetchScalarGridSpec(
            num_scalar_prefetch=1,
            grid=(nrec // group,),
            in_specs=[
                pl.BlockSpec(rec_stack.shape, full3),
                pl.BlockSpec(own_stack.shape, full3),
                pl.BlockSpec(sib_stack.shape, full3),
                pl.BlockSpec(memory_space=pl.ANY),
            ],
            out_specs=pl.BlockSpec((group * nsrc, lags), lambda g, p: (g, 0)),
            scratch_shapes=[
                pltpu.VMEM((nsrc, windows * 3 * freqs), jnp.float32),
                pltpu.VMEM((nrec, windows * 3 * freqs), jnp.float32),
                pltpu.VMEM((nrec, PAD), jnp.float32),
                pltpu.VMEM((nsrc, PAD), jnp.float32),
                pltpu.VMEM((group * nsrc, 2 * freqs), jnp.bfloat16),
                pltpu.VMEM(table.shape, jnp.bfloat16),
                pltpu.SemaphoreType.DMA(()),
            ],
        ),
        out_shape=jax.ShapeDtypeStruct((nrec * nsrc, lags), jnp.bfloat16),
        compiler_params=pltpu.CompilerParams(dimension_semantics=("arbitrary",)),
    )(place, rec_stack, own_stack, sib_stack, table)
    return out.reshape(nrec, nsrc, lags)


def shifted(x, axis, count, stride):
    parts = [x]
    for shift in range(1, count // stride):
        pairs = [(j, (j + stride * shift) % count) for j in range(count)]
        parts.append(lax.ppermute(x, axis, perm=pairs))
    return parts


def in_place_stack(parts):
    stack = jnp.zeros((len(parts),) + parts[0].shape, parts[0].dtype)
    for k, part in enumerate(parts):
        stack = lax.dynamic_update_slice_in_dim(stack, part[None], k, axis=0)
    return stack


def local(spectra, valid, rcv_count, src_count):
    channels, windows, _, freqs = spectra.shape
    table = lag_table(freqs, LAGS)
    packed = whiten_pack(spectra, valid)
    rec_stack = shifted(packed, "rcv", rcv_count, 1)
    own_stack = shifted(packed, "src", src_count, 2)
    table, rec_stack, own_stack = lax.optimization_barrier((table, rec_stack, own_stack))
    rec_stack = in_place_stack(rec_stack)
    own_stack = in_place_stack(own_stack)
    sib_stack = lax.ppermute(own_stack, "src", perm=[(j, j ^ 1) for j in range(src_count)])
    src_index = lax.axis_index("src")
    place = jnp.stack(
        [lax.axis_index("rcv"), src_index // 2, src_index % 2]
    ).astype(jnp.int32)
    return correlate(place, rec_stack, own_stack, sib_stack, table, windows, freqs)


def solution(mesh):
    return jax.shard_map(
        functools.partial(local, rcv_count=mesh.shape["rcv"], src_count=mesh.shape["src"]),
        mesh=mesh,
        in_specs=(P(("src", "rcv"), None, None, None), P(("src", "rcv"), None)),
        out_specs=P("src", "rcv", None),
        check_vma=False,
    )
```

```python
import functools
import math

import jax
import jax.numpy as jnp
from jax import lax
from jax.experimental import pallas as pl
from jax.experimental.pallas import tpu as pltpu
from jax.sharding import PartitionSpec as P

LAGS = 512
BAND = 32
NSAMP = 7500
PAD = 128

epsilon = 1e-06


def split3(x):
    hi = x.astype(jnp.bfloat16)
    rest = x - hi.astype(jnp.float32)
    mid = rest.astype(jnp.bfloat16)
    lo = (rest - mid.astype(jnp.float32)).astype(jnp.bfloat16)
    return hi, mid, lo


def exact_dot(x, ones):
    return sum(jnp.dot(part, ones, preferred_element_type=jnp.float32) for part in split3(x))


def whiten_kernel(x_ref, v_ref, out_ref, sq_ref, *, channels, windows, freqs):
    bands = freqs // BAND
    band_of = lax.broadcasted_iota(jnp.int32, (freqs, bands), 0) // BAND
    to_band = (band_of == lax.broadcasted_iota(jnp.int32, (freqs, bands), 1)).astype(jnp.bfloat16)
    band_row = lax.broadcasted_iota(jnp.int32, (bands, freqs), 1) // BAND
    from_band = (band_row == lax.broadcasted_iota(jnp.int32, (bands, freqs), 0)).astype(
        jnp.bfloat16
    )
    for c in range(channels):
        for w in range(windows):
            x = x_ref[c, w].astype(jnp.float32)
            row = c * windows + w
            sq_ref[row : row + 1, :] = x[0:1] ** 2 + x[1:2] ** 2
    power = exact_dot(sq_ref[...], to_band) / (2.0 * BAND)
    factor = exact_dot(1.0 / jnp.sqrt(power + epsilon), from_band)
    width = 2 * freqs
    for c in range(channels):
        for w in range(windows):
            x = x_ref[c, w].astype(jnp.float32)
            row = c * windows + w
            scale = factor[row : row + 1, :]
            out_ref[c : c + 1, w * width : w * width + freqs] = (x[0:1] * scale).astype(
                jnp.bfloat16
            )
            out_ref[c : c + 1, w * width + freqs : (w + 1) * width] = (x[1:2] * scale).astype(
                jnp.bfloat16
            )
    body = windows * width
    valid = v_ref[...].astype(jnp.float32)
    lane = lax.broadcasted_iota(jnp.int32, (channels, PAD), 1)
    tail = jnp.zeros((channels, PAD), jnp.float32)
    for w in range(windows):
        tail = jnp.where(lane == w, valid[:, w : w + 1], tail)
    out_ref[:, body : body + PAD] = tail.astype(jnp.bfloat16)


def whiten_pack(spectra, valid):
    channels, windows, _, freqs = spectra.shape
    kernel = functools.partial(whiten_kernel, channels=channels, windows=windows, freqs=freqs)
    return pl.pallas_call(
        kernel,
        out_shape=jax.ShapeDtypeStruct((channels, windows * 2 * freqs + PAD), jnp.bfloat16),
        scratch_shapes=[pltpu.VMEM((channels * windows, freqs), jnp.float32)],
    )(spectra, valid)


def lag_table(freq_count, lag_count):
    step = 64
    shifts = jnp.arange(lag_count, dtype=jnp.int32) - lag_count // 2
    hi = jnp.arange(freq_count // step, dtype=jnp.int32) * step
    lo = jnp.arange(step, dtype=jnp.int32)
    scale = 2.0 * math.pi / NSAMP
    angle_hi = jnp.mod(hi[:, None] * shifts[None, :], NSAMP).astype(jnp.float32) * scale
    angle_lo = jnp.mod(lo[:, None] * shifts[None, :], NSAMP).astype(jnp.float32) * scale
    cos_hi, sin_hi = jnp.cos(angle_hi)[:, None, :], jnp.sin(angle_hi)[:, None, :]
    cos_lo, sin_lo = jnp.cos(angle_lo)[None, :, :], jnp.sin(angle_lo)[None, :, :]
    factor = 1.0 / math.sqrt(2.0 * freq_count)
    cosines = (cos_hi * cos_lo - sin_hi * sin_lo) * factor
    sines = (sin_hi * cos_lo + cos_hi * sin_lo) * (-factor)
    cosines = cosines.reshape(freq_count, lag_count).astype(jnp.bfloat16)
    sines = sines.reshape(freq_count, lag_count).astype(jnp.bfloat16)
    return jnp.stack([cosines, sines], axis=0).reshape(2 * freq_count, lag_count)


def cross_kernel(
    place_ref, rec_ref, own_ref, sib_ref, tab_hbm, out_ref, srcf, recf, rtails, stails, cross,
    tab_ref, tab_sem, *, windows, freqs, group, chunk
):
    step = pl.program_id(0)
    rcv_count, per = rec_ref.shape[0], rec_ref.shape[1]
    chips = own_ref.shape[0]
    nsrc = 2 * chips * per
    body = windows * 2 * freqs
    width = 2 * freqs

    def place(block, dst, values, tails, source_side):
        rows = slice(dst * per, (dst + 1) * per)
        mask = block[:, body : body + PAD].astype(jnp.float32)
        tails[rows, :] = mask
        for w in range(windows):
            m = mask[:, w : w + 1]
            a = block[:, w * width : w * width + freqs].astype(jnp.float32) * m
            b = block[:, w * width + freqs : (w + 1) * width].astype(jnp.float32) * m
            if source_side:
                terms = (a, b - a, a + b)
            else:
                terms = (a - b, a, b)
            for t, term in enumerate(terms):
                start = (3 * w + t) * freqs
                values[rows, start : start + freqs] = term

    @pl.when(step == 0)
    def _():
        pltpu.make_async_copy(tab_hbm, tab_ref, tab_sem).start()

    @pl.when(step == 0)
    def _():
        rcv_index, chip, core = place_ref[0], place_ref[1], place_ref[2]
        for rot in range(rcv_count):

            @pl.when(rcv_index == rot)
            def _():
                for dst in range(rcv_count):
                    place(rec_ref[(rot - dst) % rcv_count], dst, recf, rtails, False)

        for rot in range(chips):
            for mine in range(2):

                @pl.when((chip == rot) & (core == mine))
                def _():
                    for zz in range(chips):
                        k = (rot - zz) % chips
                        place(own_ref[k], zz * 2 + mine, srcf, stails, True)
                        place(sib_ref[k], zz * 2 + 1 - mine, srcf, stails, True)

    smask = stails[...]

    def per_receiver(j, carry):
        i = step * group + j
        rtail = rtails[pl.ds(i, 1), :]
        count = jnp.sum(smask * rtail, axis=1, keepdims=True)
        inverse = 1.0 / jnp.maximum(count, 1.0)
        rows = pl.ds(pl.multiple_of(j * nsrc, nsrc), nsrc)
        for c in range(freqs // chunk):
            k1 = jnp.zeros((nsrc, chunk), jnp.float32)
            k2 = jnp.zeros((nsrc, chunk), jnp.float32)
            k3 = jnp.zeros((nsrc, chunk), jnp.float32)
            for w in range(windows):
                at = [(3 * w + t) * freqs + c * chunk for t in range(3)]
                sa = srcf[:, at[0] : at[0] + chunk]
                sd = srcf[:, at[1] : at[1] + chunk]
                se = srcf[:, at[2] : at[2] + chunk]
                ru = recf[pl.ds(i, 1), at[0] : at[0] + chunk]
                ra = recf[pl.ds(i, 1), at[1] : at[1] + chunk]
                rb = recf[pl.ds(i, 1), at[2] : at[2] + chunk]
                k1 = k1 + sa * ru
                k2 = k2 + ra * sd
                k3 = k3 + rb * se
            real = (k1 + k3) * inverse
            imag = (k1 + k2) * inverse
            cross[rows, c * chunk : (c + 1) * chunk] = real.astype(jnp.bfloat16)
            cross[rows, freqs + c * chunk : freqs + (c + 1) * chunk] = imag.astype(jnp.bfloat16)
        return carry

    lax.fori_loop(0, group, per_receiver, 0)

    @pl.when(step == 0)
    def _():
        pltpu.make_async_copy(tab_hbm, tab_ref, tab_sem).wait()

    out_ref[...] = jnp.dot(
        cross[...], tab_ref[...], preferred_element_type=jnp.float32
    ).astype(jnp.bfloat16)


def correlate(place, rec_stack, own_stack, sib_stack, table, windows, freqs):
    rcv_count, per, width = rec_stack.shape
    chips = own_stack.shape[0]
    nrec = rcv_count * per
    nsrc = 2 * chips * per
    lags = table.shape[1]
    group = 8
    kernel = functools.partial(
        cross_kernel, windows=windows, freqs=freqs, group=group, chunk=256
    )
    full3 = lambda g, p: (0, 0, 0)
    out = pl.pallas_call(
        kernel,
        grid_spec=pltpu.PrefetchScalarGridSpec(
            num_scalar_prefetch=1,
            grid=(nrec // group,),
            in_specs=[
                pl.BlockSpec(rec_stack.shape, full3),
                pl.BlockSpec(own_stack.shape, full3),
                pl.BlockSpec(sib_stack.shape, full3),
                pl.BlockSpec(memory_space=pl.ANY),
            ],
            out_specs=pl.BlockSpec((group * nsrc, lags), lambda g, p: (g, 0)),
            scratch_shapes=[
                pltpu.VMEM((nsrc, windows * 3 * freqs), jnp.float32),
                pltpu.VMEM((nrec, windows * 3 * freqs), jnp.float32),
                pltpu.VMEM((nrec, PAD), jnp.float32),
                pltpu.VMEM((nsrc, PAD), jnp.float32),
                pltpu.VMEM((group * nsrc, 2 * freqs), jnp.bfloat16),
                pltpu.VMEM(table.shape, jnp.bfloat16),
                pltpu.SemaphoreType.DMA(()),
            ],
        ),
        out_shape=jax.ShapeDtypeStruct((nrec * nsrc, lags), jnp.bfloat16),
        compiler_params=pltpu.CompilerParams(dimension_semantics=("arbitrary",)),
    )(place, rec_stack, own_stack, sib_stack, table)
    return out.reshape(nrec, nsrc, lags)


def shifted(x, axis, count, stride):
    parts = [x]
    for shift in range(1, count // stride):
        pairs = [(j, (j + stride * shift) % count) for j in range(count)]
        parts.append(lax.ppermute(x, axis, perm=pairs))
    return parts


def in_place_stack(parts):
    stack = jnp.zeros((len(parts),) + parts[0].shape, parts[0].dtype)
    for k, part in enumerate(parts):
        stack = lax.dynamic_update_slice_in_dim(stack, part[None], k, axis=0)
    return stack


def local(spectra, valid, rcv_count, src_count):
    channels, windows, _, freqs = spectra.shape
    table = lag_table(freqs, LAGS)
    packed = whiten_pack(spectra, valid)
    rec_stack = shifted(packed, "rcv", rcv_count, 1)
    own_stack = shifted(packed, "src", src_count, 2)
    sibling = [(j, j ^ 1) for j in range(src_count)]
    sib_stack = [lax.ppermute(part, "src", perm=sibling) for part in own_stack]
    table, rec_stack, own_stack, sib_stack = lax.optimization_barrier(
        (table, rec_stack, own_stack, sib_stack)
    )
    rec_stack = in_place_stack(rec_stack)
    own_stack = in_place_stack(own_stack)
    sib_stack = in_place_stack(sib_stack)
    src_index = lax.axis_index("src")
    place = jnp.stack(
        [lax.axis_index("rcv"), src_index // 2, src_index % 2]
    ).astype(jnp.int32)
    return correlate(place, rec_stack, own_stack, sib_stack, table, windows, freqs)


def solution(mesh):
    return jax.shard_map(
        functools.partial(local, rcv_count=mesh.shape["rcv"], src_count=mesh.shape["src"]),
        mesh=mesh,
        in_specs=(P(("src", "rcv"), None, None, None), P(("src", "rcv"), None)),
        out_specs=P("src", "rcv", None),
        check_vma=False,
    )
```

```python
import functools
import math

import jax
import jax.numpy as jnp
from jax import lax
from jax.experimental import pallas as pl
from jax.experimental.pallas import tpu as pltpu
from jax.sharding import PartitionSpec as P

LAGS = 512
BAND = 32
NSAMP = 7500
PAD = 128

epsilon = 1e-06


def split3(x):
    hi = x.astype(jnp.bfloat16)
    rest = x - hi.astype(jnp.float32)
    mid = rest.astype(jnp.bfloat16)
    lo = (rest - mid.astype(jnp.float32)).astype(jnp.bfloat16)
    return hi, mid, lo


def exact_dot(x, ones):
    return sum(jnp.dot(part, ones, preferred_element_type=jnp.float32) for part in split3(x))


def whiten_kernel(x_ref, v_ref, out_ref, sq_ref, *, channels, windows, freqs):
    bands = freqs // BAND
    band_of = lax.broadcasted_iota(jnp.int32, (freqs, bands), 0) // BAND
    to_band = (band_of == lax.broadcasted_iota(jnp.int32, (freqs, bands), 1)).astype(jnp.bfloat16)
    band_row = lax.broadcasted_iota(jnp.int32, (bands, freqs), 1) // BAND
    from_band = (band_row == lax.broadcasted_iota(jnp.int32, (bands, freqs), 0)).astype(
        jnp.bfloat16
    )
    for c in range(channels):
        for w in range(windows):
            x = x_ref[c, w].astype(jnp.float32)
            row = c * windows + w
            sq_ref[row : row + 1, :] = x[0:1] ** 2 + x[1:2] ** 2
    power = exact_dot(sq_ref[...], to_band) / (2.0 * BAND)
    factor = exact_dot(1.0 / jnp.sqrt(power + epsilon), from_band)
    width = 2 * freqs
    for c in range(channels):
        for w in range(windows):
            x = x_ref[c, w].astype(jnp.float32)
            row = c * windows + w
            scale = factor[row : row + 1, :]
            out_ref[c : c + 1, w * width : w * width + freqs] = (x[0:1] * scale).astype(
                jnp.bfloat16
            )
            out_ref[c : c + 1, w * width + freqs : (w + 1) * width] = (x[1:2] * scale).astype(
                jnp.bfloat16
            )
    body = windows * width
    valid = v_ref[...].astype(jnp.float32)
    lane = lax.broadcasted_iota(jnp.int32, (channels, PAD), 1)
    tail = jnp.zeros((channels, PAD), jnp.float32)
    for w in range(windows):
        tail = jnp.where(lane == w, valid[:, w : w + 1], tail)
    out_ref[:, body : body + PAD] = tail.astype(jnp.bfloat16)


def whiten_pack(spectra, valid):
    channels, windows, _, freqs = spectra.shape
    kernel = functools.partial(whiten_kernel, channels=channels, windows=windows, freqs=freqs)
    return pl.pallas_call(
        kernel,
        out_shape=jax.ShapeDtypeStruct((channels, windows * 2 * freqs + PAD), jnp.bfloat16),
        scratch_shapes=[pltpu.VMEM((channels * windows, freqs), jnp.float32)],
    )(spectra, valid)


def lag_table(freq_count, lag_count):
    step = 64
    shifts = jnp.arange(lag_count, dtype=jnp.int32) - lag_count // 2
    hi = jnp.arange(freq_count // step, dtype=jnp.int32) * step
    lo = jnp.arange(step, dtype=jnp.int32)
    scale = 2.0 * math.pi / NSAMP
    angle_hi = jnp.mod(hi[:, None] * shifts[None, :], NSAMP).astype(jnp.float32) * scale
    angle_lo = jnp.mod(lo[:, None] * shifts[None, :], NSAMP).astype(jnp.float32) * scale
    cos_hi, sin_hi = jnp.cos(angle_hi)[:, None, :], jnp.sin(angle_hi)[:, None, :]
    cos_lo, sin_lo = jnp.cos(angle_lo)[None, :, :], jnp.sin(angle_lo)[None, :, :]
    factor = 1.0 / math.sqrt(2.0 * freq_count)
    cosines = (cos_hi * cos_lo - sin_hi * sin_lo) * factor
    sines = (sin_hi * cos_lo + cos_hi * sin_lo) * (-factor)
    cosines = cosines.reshape(freq_count, lag_count).astype(jnp.bfloat16)
    sines = sines.reshape(freq_count, lag_count).astype(jnp.bfloat16)
    return cosines, sines


def cross_kernel(
    place_ref, rec_ref, own_ref, sib_ref, cos_hbm, sin_hbm, out_ref, srcf, recf, rtails, stails,
    cross, cos_ref, sin_ref, cos_sem, sin_sem, *, windows, freqs, group, chunk
):
    step = pl.program_id(0)
    rcv_count, per = rec_ref.shape[0], rec_ref.shape[1]
    chips = own_ref.shape[0]
    nsrc = 2 * chips * per
    body = windows * 2 * freqs
    width = 2 * freqs

    def place(block, dst, values, tails, source_side):
        rows = slice(dst * per, (dst + 1) * per)
        mask = block[:, body : body + PAD].astype(jnp.float32)
        tails[rows, :] = mask
        for w in range(windows):
            m = mask[:, w : w + 1]
            a = block[:, w * width : w * width + freqs].astype(jnp.float32) * m
            b = block[:, w * width + freqs : (w + 1) * width].astype(jnp.float32) * m
            if source_side:
                terms = (a, b - a, a + b)
            else:
                terms = (a - b, a, b)
            for t, term in enumerate(terms):
                start = (3 * w + t) * freqs
                values[rows, start : start + freqs] = term

    @pl.when(step == 0)
    def _():
        pltpu.make_async_copy(cos_hbm, cos_ref, cos_sem).start()
        pltpu.make_async_copy(sin_hbm, sin_ref, sin_sem).start()

    @pl.when(step == 0)
    def _():
        rcv_index, chip, core = place_ref[0], place_ref[1], place_ref[2]
        for rot in range(rcv_count):

            @pl.when(rcv_index == rot)
            def _():
                for dst in range(rcv_count):
                    place(rec_ref[(rot - dst) % rcv_count], dst, recf, rtails, False)

        for rot in range(chips):
            for mine in range(2):

                @pl.when((chip == rot) & (core == mine))
                def _():
                    for zz in range(chips):
                        k = (rot - zz) % chips
                        place(own_ref[k], zz * 2 + mine, srcf, stails, True)
                        place(sib_ref[k], zz * 2 + 1 - mine, srcf, stails, True)

    smask = stails[...]

    def per_receiver(j, carry):
        i = step * group + j
        rtail = rtails[pl.ds(i, 1), :]
        count = jnp.sum(smask * rtail, axis=1, keepdims=True)
        inverse = 1.0 / jnp.maximum(count, 1.0)
        rows = pl.ds(pl.multiple_of(j * nsrc, nsrc), nsrc)
        for c in range(freqs // chunk):
            k1 = jnp.zeros((nsrc, chunk), jnp.float32)
            k2 = jnp.zeros((nsrc, chunk), jnp.float32)
            k3 = jnp.zeros((nsrc, chunk), jnp.float32)
            for w in range(windows):
                at = [(3 * w + t) * freqs + c * chunk for t in range(3)]
                sa = srcf[:, at[0] : at[0] + chunk]
                sd = srcf[:, at[1] : at[1] + chunk]
                se = srcf[:, at[2] : at[2] + chunk]
                ru = recf[pl.ds(i, 1), at[0] : at[0] + chunk]
                ra = recf[pl.ds(i, 1), at[1] : at[1] + chunk]
                rb = recf[pl.ds(i, 1), at[2] : at[2] + chunk]
                k1 = k1 + sa * ru
                k2 = k2 + ra * sd
                k3 = k3 + rb * se
            real = (k1 + k3) * inverse
            imag = (k1 + k2) * inverse
            cross[rows, c * chunk : (c + 1) * chunk] = real.astype(jnp.bfloat16)
            cross[rows, freqs + c * chunk : freqs + (c + 1) * chunk] = imag.astype(jnp.bfloat16)
        return carry

    lax.fori_loop(0, group, per_receiver, 0)

    @pl.when(step == 0)
    def _():
        pltpu.make_async_copy(cos_hbm, cos_ref, cos_sem).wait()
        pltpu.make_async_copy(sin_hbm, sin_ref, sin_sem).wait()

    real = jnp.dot(cross[:, :freqs], cos_ref[...], preferred_element_type=jnp.float32)
    imag = jnp.dot(cross[:, freqs:], sin_ref[...], preferred_element_type=jnp.float32)
    out_ref[...] = (real + imag).astype(jnp.bfloat16)


def correlate(place, rec_stack, own_stack, sib_stack, tables, windows, freqs):
    rcv_count, per, width = rec_stack.shape
    chips = own_stack.shape[0]
    nrec = rcv_count * per
    nsrc = 2 * chips * per
    lags = tables[0].shape[1]
    group = 8
    kernel = functools.partial(
        cross_kernel, windows=windows, freqs=freqs, group=group, chunk=256
    )
    full3 = lambda g, p: (0, 0, 0)
    out = pl.pallas_call(
        kernel,
        grid_spec=pltpu.PrefetchScalarGridSpec(
            num_scalar_prefetch=1,
            grid=(nrec // group,),
            in_specs=[
                pl.BlockSpec(rec_stack.shape, full3),
                pl.BlockSpec(own_stack.shape, full3),
                pl.BlockSpec(sib_stack.shape, full3),
                pl.BlockSpec(memory_space=pl.ANY),
                pl.BlockSpec(memory_space=pl.ANY),
            ],
            out_specs=pl.BlockSpec((group * nsrc, lags), lambda g, p: (g, 0)),
            scratch_shapes=[
                pltpu.VMEM((nsrc, windows * 3 * freqs), jnp.float32),
                pltpu.VMEM((nrec, windows * 3 * freqs), jnp.float32),
                pltpu.VMEM((nrec, PAD), jnp.float32),
                pltpu.VMEM((nsrc, PAD), jnp.float32),
                pltpu.VMEM((group * nsrc, 2 * freqs), jnp.bfloat16),
                pltpu.VMEM(tables[0].shape, jnp.bfloat16),
                pltpu.VMEM(tables[1].shape, jnp.bfloat16),
                pltpu.SemaphoreType.DMA(()),
                pltpu.SemaphoreType.DMA(()),
            ],
        ),
        out_shape=jax.ShapeDtypeStruct((nrec * nsrc, lags), jnp.bfloat16),
        compiler_params=pltpu.CompilerParams(dimension_semantics=("arbitrary",)),
    )(place, rec_stack, own_stack, sib_stack, *tables)
    return out.reshape(nrec, nsrc, lags)


def shifted(x, axis, count, stride):
    parts = [x]
    for shift in range(1, count // stride):
        pairs = [(j, (j + stride * shift) % count) for j in range(count)]
        parts.append(lax.ppermute(x, axis, perm=pairs))
    return parts


def in_place_stack(parts):
    stack = jnp.zeros((len(parts),) + parts[0].shape, parts[0].dtype)
    for k, part in enumerate(parts):
        stack = lax.dynamic_update_slice_in_dim(stack, part[None], k, axis=0)
    return stack


def local(spectra, valid, rcv_count, src_count):
    channels, windows, _, freqs = spectra.shape
    table = lag_table(freqs, LAGS)
    packed = whiten_pack(spectra, valid)
    rec_stack = shifted(packed, "rcv", rcv_count, 1)
    own_stack = shifted(packed, "src", src_count, 2)
    sibling = [(j, j ^ 1) for j in range(src_count)]
    sib_stack = [lax.ppermute(part, "src", perm=sibling) for part in own_stack]
    table, rec_stack, own_stack, sib_stack = lax.optimization_barrier(
        (table, rec_stack, own_stack, sib_stack)
    )
    rec_stack = in_place_stack(rec_stack)
    own_stack = in_place_stack(own_stack)
    sib_stack = in_place_stack(sib_stack)
    src_index = lax.axis_index("src")
    place = jnp.stack(
        [lax.axis_index("rcv"), src_index // 2, src_index % 2]
    ).astype(jnp.int32)
    return correlate(place, rec_stack, own_stack, sib_stack, table, windows, freqs)


def solution(mesh):
    return jax.shard_map(
        functools.partial(local, rcv_count=mesh.shape["rcv"], src_count=mesh.shape["src"]),
        mesh=mesh,
        in_specs=(P(("src", "rcv"), None, None, None), P(("src", "rcv"), None)),
        out_specs=P("src", "rcv", None),
        check_vma=False,
    )
```

```python
import functools
import math

import jax
import jax.numpy as jnp
from jax import lax
from jax.experimental import pallas as pl
from jax.experimental.pallas import tpu as pltpu
from jax.sharding import PartitionSpec as P

LAGS = 512
BAND = 32
NSAMP = 7500
PAD = 128

epsilon = 1e-06


def split3(x):
    hi = x.astype(jnp.bfloat16)
    rest = x - hi.astype(jnp.float32)
    mid = rest.astype(jnp.bfloat16)
    lo = (rest - mid.astype(jnp.float32)).astype(jnp.bfloat16)
    return hi, mid, lo


def exact_dot(x, ones):
    return sum(jnp.dot(part, ones, preferred_element_type=jnp.float32) for part in split3(x))


def whiten_kernel(x_ref, v_ref, out_ref, sq_ref, *, channels, windows, freqs):
    bands = freqs // BAND
    band_of = lax.broadcasted_iota(jnp.int32, (freqs, bands), 0) // BAND
    to_band = (band_of == lax.broadcasted_iota(jnp.int32, (freqs, bands), 1)).astype(jnp.bfloat16)
    band_row = lax.broadcasted_iota(jnp.int32, (bands, freqs), 1) // BAND
    from_band = (band_row == lax.broadcasted_iota(jnp.int32, (bands, freqs), 0)).astype(
        jnp.bfloat16
    )
    for c in range(channels):
        for w in range(windows):
            x = x_ref[c, w].astype(jnp.float32)
            row = c * windows + w
            sq_ref[row : row + 1, :] = x[0:1] ** 2 + x[1:2] ** 2
    power = exact_dot(sq_ref[...], to_band) / (2.0 * BAND)
    factor = exact_dot(1.0 / jnp.sqrt(power + epsilon), from_band)
    width = 2 * freqs
    for c in range(channels):
        for w in range(windows):
            x = x_ref[c, w].astype(jnp.float32)
            row = c * windows + w
            scale = factor[row : row + 1, :]
            out_ref[c : c + 1, w * width : w * width + freqs] = (x[0:1] * scale).astype(
                jnp.bfloat16
            )
            out_ref[c : c + 1, w * width + freqs : (w + 1) * width] = (x[1:2] * scale).astype(
                jnp.bfloat16
            )
    body = windows * width
    valid = v_ref[...].astype(jnp.float32)
    lane = lax.broadcasted_iota(jnp.int32, (channels, PAD), 1)
    tail = jnp.zeros((channels, PAD), jnp.float32)
    for w in range(windows):
        tail = jnp.where(lane == w, valid[:, w : w + 1], tail)
    out_ref[:, body : body + PAD] = tail.astype(jnp.bfloat16)


def whiten_pack(spectra, valid):
    channels, windows, _, freqs = spectra.shape
    kernel = functools.partial(whiten_kernel, channels=channels, windows=windows, freqs=freqs)
    return pl.pallas_call(
        kernel,
        out_shape=jax.ShapeDtypeStruct((channels, windows * 2 * freqs + PAD), jnp.bfloat16),
        scratch_shapes=[pltpu.VMEM((channels * windows, freqs), jnp.float32)],
    )(spectra, valid)


def lag_table(freq_count, lag_count):
    step = 64
    shifts = jnp.arange(lag_count, dtype=jnp.int32) - lag_count // 2
    hi = jnp.arange(freq_count // step, dtype=jnp.int32) * step
    lo = jnp.arange(step, dtype=jnp.int32)
    scale = 2.0 * math.pi / NSAMP
    angle_hi = jnp.mod(hi[:, None] * shifts[None, :], NSAMP).astype(jnp.float32) * scale
    angle_lo = jnp.mod(lo[:, None] * shifts[None, :], NSAMP).astype(jnp.float32) * scale
    cos_hi, sin_hi = jnp.cos(angle_hi)[:, None, :], jnp.sin(angle_hi)[:, None, :]
    cos_lo, sin_lo = jnp.cos(angle_lo)[None, :, :], jnp.sin(angle_lo)[None, :, :]
    factor = 1.0 / math.sqrt(2.0 * freq_count)
    cosines = (cos_hi * cos_lo - sin_hi * sin_lo) * factor
    sines = (sin_hi * cos_lo + cos_hi * sin_lo) * (-factor)
    cosines = cosines.reshape(freq_count, lag_count).astype(jnp.bfloat16)
    sines = sines.reshape(freq_count, lag_count).astype(jnp.bfloat16)
    return jnp.stack([cosines, sines], axis=0).reshape(2 * freq_count, lag_count)


def cross_kernel(
    rec_ref, own_ref, sib_ref, tab_hbm, out_ref, srcf, recf, rtails, stails, cross,
    tab_ref, tab_sem, *, windows, freqs, group, chunk
):
    step = pl.program_id(0)
    rcv_count, per = rec_ref.shape[0], rec_ref.shape[1]
    chips = own_ref.shape[0]
    nsrc = 2 * chips * per
    body = windows * 2 * freqs
    width = 2 * freqs

    def place(block, dst, values, tails, source_side):
        rows = slice(dst * per, (dst + 1) * per)
        mask = block[:, body : body + PAD].astype(jnp.float32)
        tails[rows, :] = mask
        for w in range(windows):
            m = mask[:, w : w + 1]
            a = block[:, w * width : w * width + freqs].astype(jnp.float32) * m
            b = block[:, w * width + freqs : (w + 1) * width].astype(jnp.float32) * m
            if source_side:
                terms = (a, b - a, a + b)
            else:
                terms = (a - b, a, b)
            for t, term in enumerate(terms):
                start = (3 * w + t) * freqs
                values[rows, start : start + freqs] = term

    @pl.when(step == 0)
    def _():
        pltpu.make_async_copy(tab_hbm, tab_ref, tab_sem).start()

    @pl.when(step == 0)
    def _():
        src_index = lax.axis_index("src")
        rcv_index, chip, core = lax.axis_index("rcv"), src_index // 2, src_index % 2
        for rot in range(rcv_count):

            @pl.when(rcv_index == rot)
            def _():
                for dst in range(rcv_count):
                    place(rec_ref[(rot - dst) % rcv_count], dst, recf, rtails, False)

        for rot in range(chips):
            for mine in range(2):

                @pl.when((chip == rot) & (core == mine))
                def _():
                    for zz in range(chips):
                        k = (rot - zz) % chips
                        place(own_ref[k], zz * 2 + mine, srcf, stails, True)
                        place(sib_ref[k], zz * 2 + 1 - mine, srcf, stails, True)

    smask = stails[...]

    def per_receiver(j, carry):
        i = step * group + j
        rtail = rtails[pl.ds(i, 1), :]
        count = jnp.sum(smask * rtail, axis=1, keepdims=True)
        inverse = 1.0 / jnp.maximum(count, 1.0)
        rows = pl.ds(pl.multiple_of(j * nsrc, nsrc), nsrc)
        for c in range(freqs // chunk):
            k1 = jnp.zeros((nsrc, chunk), jnp.float32)
            k2 = jnp.zeros((nsrc, chunk), jnp.float32)
            k3 = jnp.zeros((nsrc, chunk), jnp.float32)
            for w in range(windows):
                at = [(3 * w + t) * freqs + c * chunk for t in range(3)]
                sa = srcf[:, at[0] : at[0] + chunk]
                sd = srcf[:, at[1] : at[1] + chunk]
                se = srcf[:, at[2] : at[2] + chunk]
                ru = recf[pl.ds(i, 1), at[0] : at[0] + chunk]
                ra = recf[pl.ds(i, 1), at[1] : at[1] + chunk]
                rb = recf[pl.ds(i, 1), at[2] : at[2] + chunk]
                k1 = k1 + sa * ru
                k2 = k2 + ra * sd
                k3 = k3 + rb * se
            real = (k1 + k3) * inverse
            imag = (k1 + k2) * inverse
            cross[rows, c * chunk : (c + 1) * chunk] = real.astype(jnp.bfloat16)
            cross[rows, freqs + c * chunk : freqs + (c + 1) * chunk] = imag.astype(jnp.bfloat16)
        return carry

    lax.fori_loop(0, group, per_receiver, 0)

    @pl.when(step == 0)
    def _():
        pltpu.make_async_copy(tab_hbm, tab_ref, tab_sem).wait()

    out_ref[...] = jnp.dot(
        cross[...], tab_ref[...], preferred_element_type=jnp.float32
    ).astype(jnp.bfloat16)


def correlate(rec_stack, own_stack, sib_stack, table, windows, freqs):
    rcv_count, per, width = rec_stack.shape
    chips = own_stack.shape[0]
    nrec = rcv_count * per
    nsrc = 2 * chips * per
    lags = table.shape[1]
    group = 8
    kernel = functools.partial(
        cross_kernel, windows=windows, freqs=freqs, group=group, chunk=256
    )
    full3 = lambda g: (0, 0, 0)
    out = pl.pallas_call(
        kernel,
        grid_spec=pl.GridSpec(
            grid=(nrec // group,),
            in_specs=[
                pl.BlockSpec(rec_stack.shape, full3),
                pl.BlockSpec(own_stack.shape, full3),
                pl.BlockSpec(sib_stack.shape, full3),
                pl.BlockSpec(memory_space=pl.ANY),
            ],
            out_specs=pl.BlockSpec((group * nsrc, lags), lambda g: (g, 0)),
            scratch_shapes=[
                pltpu.VMEM((nsrc, windows * 3 * freqs), jnp.float32),
                pltpu.VMEM((nrec, windows * 3 * freqs), jnp.float32),
                pltpu.VMEM((nrec, PAD), jnp.float32),
                pltpu.VMEM((nsrc, PAD), jnp.float32),
                pltpu.VMEM((group * nsrc, 2 * freqs), jnp.bfloat16),
                pltpu.VMEM(table.shape, jnp.bfloat16),
                pltpu.SemaphoreType.DMA(()),
            ],
        ),
        out_shape=jax.ShapeDtypeStruct((nrec * nsrc, lags), jnp.bfloat16),
        compiler_params=pltpu.CompilerParams(dimension_semantics=("arbitrary",)),
    )(rec_stack, own_stack, sib_stack, table)
    return out.reshape(nrec, nsrc, lags)


def shifted(x, axis, count, stride):
    parts = [x]
    for shift in range(1, count // stride):
        pairs = [(j, (j + stride * shift) % count) for j in range(count)]
        parts.append(lax.ppermute(x, axis, perm=pairs))
    return parts


def in_place_stack(parts):
    stack = jnp.zeros((len(parts),) + parts[0].shape, parts[0].dtype)
    for k, part in enumerate(parts):
        stack = lax.dynamic_update_slice_in_dim(stack, part[None], k, axis=0)
    return stack


def local(spectra, valid, rcv_count, src_count):
    channels, windows, _, freqs = spectra.shape
    table = lag_table(freqs, LAGS)
    packed = whiten_pack(spectra, valid)
    rec_stack = shifted(packed, "rcv", rcv_count, 1)
    own_stack = shifted(packed, "src", src_count, 2)
    sibling = [(j, j ^ 1) for j in range(src_count)]
    sib_stack = [lax.ppermute(part, "src", perm=sibling) for part in own_stack]
    table, rec_stack, own_stack, sib_stack = lax.optimization_barrier(
        (table, rec_stack, own_stack, sib_stack)
    )
    rec_stack = in_place_stack(rec_stack)
    own_stack = in_place_stack(own_stack)
    sib_stack = in_place_stack(sib_stack)
    return correlate(rec_stack, own_stack, sib_stack, table, windows, freqs)


def solution(mesh):
    return jax.shard_map(
        functools.partial(local, rcv_count=mesh.shape["rcv"], src_count=mesh.shape["src"]),
        mesh=mesh,
        in_specs=(P(("src", "rcv"), None, None, None), P(("src", "rcv"), None)),
        out_specs=P("src", "rcv", None),
        check_vma=False,
    )
```

```python
import functools
import math

import jax
import jax.numpy as jnp
from jax import lax
from jax.experimental import pallas as pl
from jax.experimental.pallas import tpu as pltpu
from jax.sharding import PartitionSpec as P

LAGS = 512
BAND = 32
NSAMP = 7500
PAD = 128

epsilon = 1e-06


def split3(x):
    hi = x.astype(jnp.bfloat16)
    rest = x - hi.astype(jnp.float32)
    mid = rest.astype(jnp.bfloat16)
    lo = (rest - mid.astype(jnp.float32)).astype(jnp.bfloat16)
    return hi, mid, lo


def exact_dot(x, ones):
    return sum(jnp.dot(part, ones, preferred_element_type=jnp.float32) for part in split3(x))


def whiten_kernel(x_ref, v_ref, out_ref, sq_ref, *, channels, windows, freqs):
    bands = freqs // BAND
    band_of = lax.broadcasted_iota(jnp.int32, (freqs, bands), 0) // BAND
    to_band = (band_of == lax.broadcasted_iota(jnp.int32, (freqs, bands), 1)).astype(jnp.bfloat16)
    band_row = lax.broadcasted_iota(jnp.int32, (bands, freqs), 1) // BAND
    from_band = (band_row == lax.broadcasted_iota(jnp.int32, (bands, freqs), 0)).astype(
        jnp.bfloat16
    )
    for c in range(channels):
        for w in range(windows):
            x = x_ref[c, w].astype(jnp.float32)
            row = c * windows + w
            sq_ref[row : row + 1, :] = x[0:1] ** 2 + x[1:2] ** 2
    power = exact_dot(sq_ref[...], to_band) / (2.0 * BAND)
    factor = exact_dot(1.0 / jnp.sqrt(power + epsilon), from_band)
    width = 2 * freqs
    for c in range(channels):
        for w in range(windows):
            x = x_ref[c, w].astype(jnp.float32)
            row = c * windows + w
            scale = factor[row : row + 1, :]
            out_ref[c : c + 1, w * width : w * width + freqs] = (x[0:1] * scale).astype(
                jnp.bfloat16
            )
            out_ref[c : c + 1, w * width + freqs : (w + 1) * width] = (x[1:2] * scale).astype(
                jnp.bfloat16
            )
    body = windows * width
    valid = v_ref[...].astype(jnp.float32)
    lane = lax.broadcasted_iota(jnp.int32, (channels, PAD), 1)
    tail = jnp.zeros((channels, PAD), jnp.float32)
    for w in range(windows):
        tail = jnp.where(lane == w, valid[:, w : w + 1], tail)
    out_ref[:, body : body + PAD] = tail.astype(jnp.bfloat16)


def whiten_pack(spectra, valid):
    channels, windows, _, freqs = spectra.shape
    kernel = functools.partial(whiten_kernel, channels=channels, windows=windows, freqs=freqs)
    return pl.pallas_call(
        kernel,
        out_shape=jax.ShapeDtypeStruct((channels, windows * 2 * freqs + PAD), jnp.bfloat16),
        scratch_shapes=[pltpu.VMEM((channels * windows, freqs), jnp.float32)],
    )(spectra, valid)


def lag_table(freq_count, lag_count):
    step = 64
    shifts = jnp.arange(lag_count, dtype=jnp.int32) - lag_count // 2
    hi = jnp.arange(freq_count // step, dtype=jnp.int32) * step
    lo = jnp.arange(step, dtype=jnp.int32)
    scale = 2.0 * math.pi / NSAMP
    angle_hi = jnp.mod(hi[:, None] * shifts[None, :], NSAMP).astype(jnp.float32) * scale
    angle_lo = jnp.mod(lo[:, None] * shifts[None, :], NSAMP).astype(jnp.float32) * scale
    cos_hi, sin_hi = jnp.cos(angle_hi)[:, None, :], jnp.sin(angle_hi)[:, None, :]
    cos_lo, sin_lo = jnp.cos(angle_lo)[None, :, :], jnp.sin(angle_lo)[None, :, :]
    factor = 1.0 / math.sqrt(2.0 * freq_count)
    cosines = (cos_hi * cos_lo - sin_hi * sin_lo) * factor
    sines = (sin_hi * cos_lo + cos_hi * sin_lo) * (-factor)
    cosines = cosines.reshape(freq_count, lag_count).astype(jnp.bfloat16)
    sines = sines.reshape(freq_count, lag_count).astype(jnp.bfloat16)
    return cosines, sines


def cross_kernel(
    rec_ref, own_ref, sib_ref, cos_hbm, sin_hbm, out_ref, srcf, recf, rtails, stails,
    cross, cos_ref, sin_ref, cos_sem, sin_sem, *, windows, freqs, group, chunk
):
    step = pl.program_id(0)
    rcv_count, per = rec_ref.shape[0], rec_ref.shape[1]
    chips = own_ref.shape[0]
    nsrc = 2 * chips * per
    body = windows * 2 * freqs
    width = 2 * freqs

    def place(block, dst, values, tails, source_side):
        rows = slice(dst * per, (dst + 1) * per)
        mask = block[:, body : body + PAD].astype(jnp.float32)
        tails[rows, :] = mask
        for w in range(windows):
            m = mask[:, w : w + 1]
            a = block[:, w * width : w * width + freqs].astype(jnp.float32) * m
            b = block[:, w * width + freqs : (w + 1) * width].astype(jnp.float32) * m
            if source_side:
                terms = (a, b - a, a + b)
            else:
                terms = (a - b, a, b)
            for t, term in enumerate(terms):
                start = (3 * w + t) * freqs
                values[rows, start : start + freqs] = term

    @pl.when(step == 0)
    def _():
        pltpu.make_async_copy(cos_hbm, cos_ref, cos_sem).start()
        pltpu.make_async_copy(sin_hbm, sin_ref, sin_sem).start()

    @pl.when(step == 0)
    def _():
        src_index = lax.axis_index("src")
        rcv_index, chip, core = lax.axis_index("rcv"), src_index // 2, src_index % 2
        for rot in range(rcv_count):

            @pl.when(rcv_index == rot)
            def _():
                for dst in range(rcv_count):
                    place(rec_ref[(rot - dst) % rcv_count], dst, recf, rtails, False)

        for rot in range(chips):
            for mine in range(2):

                @pl.when((chip == rot) & (core == mine))
                def _():
                    for zz in range(chips):
                        k = (rot - zz) % chips
                        place(own_ref[k], zz * 2 + mine, srcf, stails, True)
                        place(sib_ref[k], zz * 2 + 1 - mine, srcf, stails, True)

    smask = stails[...]

    def per_receiver(j, carry):
        i = step * group + j
        rtail = rtails[pl.ds(i, 1), :]
        count = jnp.sum(smask * rtail, axis=1, keepdims=True)
        inverse = 1.0 / jnp.maximum(count, 1.0)
        rows = pl.ds(pl.multiple_of(j * nsrc, nsrc), nsrc)
        for c in range(freqs // chunk):
            k1 = jnp.zeros((nsrc, chunk), jnp.float32)
            k2 = jnp.zeros((nsrc, chunk), jnp.float32)
            k3 = jnp.zeros((nsrc, chunk), jnp.float32)
            for w in range(windows):
                at = [(3 * w + t) * freqs + c * chunk for t in range(3)]
                sa = srcf[:, at[0] : at[0] + chunk]
                sd = srcf[:, at[1] : at[1] + chunk]
                se = srcf[:, at[2] : at[2] + chunk]
                ru = recf[pl.ds(i, 1), at[0] : at[0] + chunk]
                ra = recf[pl.ds(i, 1), at[1] : at[1] + chunk]
                rb = recf[pl.ds(i, 1), at[2] : at[2] + chunk]
                k1 = k1 + sa * ru
                k2 = k2 + ra * sd
                k3 = k3 + rb * se
            real = (k1 + k3) * inverse
            imag = (k1 + k2) * inverse
            cross[rows, c * chunk : (c + 1) * chunk] = real.astype(jnp.bfloat16)
            cross[rows, freqs + c * chunk : freqs + (c + 1) * chunk] = imag.astype(jnp.bfloat16)
        return carry

    lax.fori_loop(0, group, per_receiver, 0)

    @pl.when(step == 0)
    def _():
        pltpu.make_async_copy(cos_hbm, cos_ref, cos_sem).wait()
        pltpu.make_async_copy(sin_hbm, sin_ref, sin_sem).wait()

    real = jnp.dot(cross[:, :freqs], cos_ref[...], preferred_element_type=jnp.float32)
    imag = jnp.dot(cross[:, freqs:], sin_ref[...], preferred_element_type=jnp.float32)
    out_ref[...] = (real + imag).astype(jnp.bfloat16)


def correlate(rec_stack, own_stack, sib_stack, tables, windows, freqs):
    rcv_count, per, width = rec_stack.shape
    chips = own_stack.shape[0]
    nrec = rcv_count * per
    nsrc = 2 * chips * per
    lags = tables[0].shape[1]
    group = 8
    kernel = functools.partial(
        cross_kernel, windows=windows, freqs=freqs, group=group, chunk=256
    )
    full3 = lambda g: (0, 0, 0)
    out = pl.pallas_call(
        kernel,
        grid_spec=pl.GridSpec(
            grid=(nrec // group,),
            in_specs=[
                pl.BlockSpec(rec_stack.shape, full3),
                pl.BlockSpec(own_stack.shape, full3),
                pl.BlockSpec(sib_stack.shape, full3),
                pl.BlockSpec(memory_space=pl.ANY),
                pl.BlockSpec(memory_space=pl.ANY),
            ],
            out_specs=pl.BlockSpec((group * nsrc, lags), lambda g: (g, 0)),
            scratch_shapes=[
                pltpu.VMEM((nsrc, windows * 3 * freqs), jnp.float32),
                pltpu.VMEM((nrec, windows * 3 * freqs), jnp.float32),
                pltpu.VMEM((nrec, PAD), jnp.float32),
                pltpu.VMEM((nsrc, PAD), jnp.float32),
                pltpu.VMEM((group * nsrc, 2 * freqs), jnp.bfloat16),
                pltpu.VMEM(tables[0].shape, jnp.bfloat16),
                pltpu.VMEM(tables[1].shape, jnp.bfloat16),
                pltpu.SemaphoreType.DMA(()),
                pltpu.SemaphoreType.DMA(()),
            ],
        ),
        out_shape=jax.ShapeDtypeStruct((nrec * nsrc, lags), jnp.bfloat16),
        compiler_params=pltpu.CompilerParams(dimension_semantics=("arbitrary",)),
    )(rec_stack, own_stack, sib_stack, *tables)
    return out.reshape(nrec, nsrc, lags)


def shifted(x, axis, count, stride):
    parts = [x]
    for shift in range(1, count // stride):
        pairs = [(j, (j + stride * shift) % count) for j in range(count)]
        parts.append(lax.ppermute(x, axis, perm=pairs))
    return parts


def in_place_stack(parts):
    stack = jnp.zeros((len(parts),) + parts[0].shape, parts[0].dtype)
    for k, part in enumerate(parts):
        stack = lax.dynamic_update_slice_in_dim(stack, part[None], k, axis=0)
    return stack


def local(spectra, valid, rcv_count, src_count):
    channels, windows, _, freqs = spectra.shape
    table = lag_table(freqs, LAGS)
    packed = whiten_pack(spectra, valid)
    rec_stack = shifted(packed, "rcv", rcv_count, 1)
    own_stack = shifted(packed, "src", src_count, 2)
    sibling = [(j, j ^ 1) for j in range(src_count)]
    sib_stack = [lax.ppermute(part, "src", perm=sibling) for part in own_stack]
    table, rec_stack, own_stack, sib_stack = lax.optimization_barrier(
        (table, rec_stack, own_stack, sib_stack)
    )
    rec_stack = in_place_stack(rec_stack)
    own_stack = in_place_stack(own_stack)
    sib_stack = in_place_stack(sib_stack)
    return correlate(rec_stack, own_stack, sib_stack, table, windows, freqs)


def solution(mesh):
    return jax.shard_map(
        functools.partial(local, rcv_count=mesh.shape["rcv"], src_count=mesh.shape["src"]),
        mesh=mesh,
        in_specs=(P(("src", "rcv"), None, None, None), P(("src", "rcv"), None)),
        out_specs=P("src", "rcv", None),
        check_vma=False,
    )
```

```python
import functools
import math

import jax
import jax.numpy as jnp
from jax import lax
from jax.experimental import pallas as pl
from jax.experimental.pallas import tpu as pltpu
from jax.sharding import PartitionSpec as P

LAGS = 512
BAND = 32
NSAMP = 7500
PAD = 128

epsilon = 1e-06


def split3(x):
    hi = x.astype(jnp.bfloat16)
    rest = x - hi.astype(jnp.float32)
    mid = rest.astype(jnp.bfloat16)
    lo = (rest - mid.astype(jnp.float32)).astype(jnp.bfloat16)
    return hi, mid, lo


def exact_dot(x, ones):
    return sum(jnp.dot(part, ones, preferred_element_type=jnp.float32) for part in split3(x))


def whiten_kernel(x_ref, v_ref, out_ref, sq_ref, *, channels, windows, freqs):
    bands = freqs // BAND
    band_of = lax.broadcasted_iota(jnp.int32, (freqs, bands), 0) // BAND
    to_band = (band_of == lax.broadcasted_iota(jnp.int32, (freqs, bands), 1)).astype(jnp.bfloat16)
    band_row = lax.broadcasted_iota(jnp.int32, (bands, freqs), 1) // BAND
    from_band = (band_row == lax.broadcasted_iota(jnp.int32, (bands, freqs), 0)).astype(
        jnp.bfloat16
    )
    for c in range(channels):
        for w in range(windows):
            x = x_ref[c, w].astype(jnp.float32)
            row = c * windows + w
            sq_ref[row : row + 1, :] = x[0:1] ** 2 + x[1:2] ** 2
    power = exact_dot(sq_ref[...], to_band) / (2.0 * BAND)
    factor = exact_dot(1.0 / jnp.sqrt(power + epsilon), from_band)
    width = 2 * freqs
    for c in range(channels):
        for w in range(windows):
            x = x_ref[c, w].astype(jnp.float32)
            row = c * windows + w
            scale = factor[row : row + 1, :]
            out_ref[c : c + 1, w * width : w * width + freqs] = (x[0:1] * scale).astype(
                jnp.bfloat16
            )
            out_ref[c : c + 1, w * width + freqs : (w + 1) * width] = (x[1:2] * scale).astype(
                jnp.bfloat16
            )
    body = windows * width
    valid = v_ref[...].astype(jnp.float32)
    lane = lax.broadcasted_iota(jnp.int32, (channels, PAD), 1)
    tail = jnp.zeros((channels, PAD), jnp.float32)
    for w in range(windows):
        tail = jnp.where(lane == w, valid[:, w : w + 1], tail)
    out_ref[:, body : body + PAD] = tail.astype(jnp.bfloat16)


def whiten_pack(spectra, valid):
    channels, windows, _, freqs = spectra.shape
    kernel = functools.partial(whiten_kernel, channels=channels, windows=windows, freqs=freqs)
    return pl.pallas_call(
        kernel,
        out_shape=jax.ShapeDtypeStruct((channels, windows * 2 * freqs + PAD), jnp.bfloat16),
        scratch_shapes=[pltpu.VMEM((channels * windows, freqs), jnp.float32)],
    )(spectra, valid)


def lag_table(freq_count, lag_count):
    step = 64
    shifts = jnp.arange(lag_count, dtype=jnp.int32) - lag_count // 2
    hi = jnp.arange(freq_count // step, dtype=jnp.int32) * step
    lo = jnp.arange(step, dtype=jnp.int32)
    scale = 2.0 * math.pi / NSAMP
    angle_hi = jnp.mod(hi[:, None] * shifts[None, :], NSAMP).astype(jnp.float32) * scale
    angle_lo = jnp.mod(lo[:, None] * shifts[None, :], NSAMP).astype(jnp.float32) * scale
    cos_hi, sin_hi = jnp.cos(angle_hi)[:, None, :], jnp.sin(angle_hi)[:, None, :]
    cos_lo, sin_lo = jnp.cos(angle_lo)[None, :, :], jnp.sin(angle_lo)[None, :, :]
    return cos_hi[:, 0], sin_hi[:, 0], cos_lo[0], sin_lo[0]


def cross_kernel(
    rec_ref, own_ref, sib_ref, chi_ref, shi_ref, clo_ref, slo_ref, out_ref, srcf, recf, rtails,
    stails, cross, tab_ref, *, windows, freqs, group, chunk
):
    step = pl.program_id(0)
    rcv_count, per = rec_ref.shape[0], rec_ref.shape[1]
    chips = own_ref.shape[0]
    nsrc = 2 * chips * per
    body = windows * 2 * freqs
    width = 2 * freqs

    def place(block, dst, values, tails, source_side):
        rows = slice(dst * per, (dst + 1) * per)
        mask = block[:, body : body + PAD].astype(jnp.float32)
        tails[rows, :] = mask
        for w in range(windows):
            m = mask[:, w : w + 1]
            a = block[:, w * width : w * width + freqs].astype(jnp.float32) * m
            b = block[:, w * width + freqs : (w + 1) * width].astype(jnp.float32) * m
            if source_side:
                terms = (a, b - a, a + b)
            else:
                terms = (a - b, a, b)
            for t, term in enumerate(terms):
                start = (3 * w + t) * freqs
                values[rows, start : start + freqs] = term

    @pl.when(step == 0)
    def _():
        factor = 1.0 / math.sqrt(2.0 * freqs)
        span = clo_ref.shape[0]
        clo = clo_ref[...]
        slo = slo_ref[...]

        def fill(h, carry):
            ch = chi_ref[pl.ds(h, 1), :]
            sh = shi_ref[pl.ds(h, 1), :]
            rows = pl.ds(pl.multiple_of(h * span, span), span)
            tab_ref[rows, :] = ((ch * clo - sh * slo) * factor).astype(jnp.bfloat16)
            rows = pl.ds(pl.multiple_of(freqs + h * span, span), span)
            tab_ref[rows, :] = ((sh * clo + ch * slo) * (-factor)).astype(jnp.bfloat16)
            return carry

        lax.fori_loop(0, chi_ref.shape[0], fill, 0)

    @pl.when(step == 0)
    def _():
        src_index = lax.axis_index("src")
        rcv_index, chip, core = lax.axis_index("rcv"), src_index // 2, src_index % 2
        for rot in range(rcv_count):

            @pl.when(rcv_index == rot)
            def _():
                for dst in range(rcv_count):
                    place(rec_ref[(rot - dst) % rcv_count], dst, recf, rtails, False)

        for rot in range(chips):
            for mine in range(2):

                @pl.when((chip == rot) & (core == mine))
                def _():
                    for zz in range(chips):
                        k = (rot - zz) % chips
                        place(own_ref[k], zz * 2 + mine, srcf, stails, True)
                        place(sib_ref[k], zz * 2 + 1 - mine, srcf, stails, True)

    smask = stails[...]

    def per_receiver(j, carry):
        i = step * group + j
        rtail = rtails[pl.ds(i, 1), :]
        count = jnp.sum(smask * rtail, axis=1, keepdims=True)
        inverse = 1.0 / jnp.maximum(count, 1.0)
        rows = pl.ds(pl.multiple_of(j * nsrc, nsrc), nsrc)
        for c in range(freqs // chunk):
            k1 = jnp.zeros((nsrc, chunk), jnp.float32)
            k2 = jnp.zeros((nsrc, chunk), jnp.float32)
            k3 = jnp.zeros((nsrc, chunk), jnp.float32)
            for w in range(windows):
                at = [(3 * w + t) * freqs + c * chunk for t in range(3)]
                sa = srcf[:, at[0] : at[0] + chunk]
                sd = srcf[:, at[1] : at[1] + chunk]
                se = srcf[:, at[2] : at[2] + chunk]
                ru = recf[pl.ds(i, 1), at[0] : at[0] + chunk]
                ra = recf[pl.ds(i, 1), at[1] : at[1] + chunk]
                rb = recf[pl.ds(i, 1), at[2] : at[2] + chunk]
                k1 = k1 + sa * ru
                k2 = k2 + ra * sd
                k3 = k3 + rb * se
            real = (k1 + k3) * inverse
            imag = (k1 + k2) * inverse
            cross[rows, c * chunk : (c + 1) * chunk] = real.astype(jnp.bfloat16)
            cross[rows, freqs + c * chunk : freqs + (c + 1) * chunk] = imag.astype(jnp.bfloat16)
        return carry

    lax.fori_loop(0, group, per_receiver, 0)

    out_ref[...] = jnp.dot(
        cross[...], tab_ref[...], preferred_element_type=jnp.float32
    ).astype(jnp.bfloat16)


def correlate(rec_stack, own_stack, sib_stack, angles, windows, freqs):
    rcv_count, per, width = rec_stack.shape
    chips = own_stack.shape[0]
    nrec = rcv_count * per
    nsrc = 2 * chips * per
    lags = angles[0].shape[1]
    group = 8
    kernel = functools.partial(
        cross_kernel, windows=windows, freqs=freqs, group=group, chunk=256
    )
    full3 = lambda g: (0, 0, 0)
    out = pl.pallas_call(
        kernel,
        grid_spec=pl.GridSpec(
            grid=(nrec // group,),
            in_specs=[
                pl.BlockSpec(rec_stack.shape, full3),
                pl.BlockSpec(own_stack.shape, full3),
                pl.BlockSpec(sib_stack.shape, full3),
            ]
            + [pl.BlockSpec(a.shape, lambda g: (0, 0)) for a in angles],
            out_specs=pl.BlockSpec((group * nsrc, lags), lambda g: (g, 0)),
            scratch_shapes=[
                pltpu.VMEM((nsrc, windows * 3 * freqs), jnp.float32),
                pltpu.VMEM((nrec, windows * 3 * freqs), jnp.float32),
                pltpu.VMEM((nrec, PAD), jnp.float32),
                pltpu.VMEM((nsrc, PAD), jnp.float32),
                pltpu.VMEM((group * nsrc, 2 * freqs), jnp.bfloat16),
                pltpu.VMEM((2 * freqs, lags), jnp.bfloat16),
            ],
        ),
        out_shape=jax.ShapeDtypeStruct((nrec * nsrc, lags), jnp.bfloat16),
        compiler_params=pltpu.CompilerParams(dimension_semantics=("arbitrary",)),
    )(rec_stack, own_stack, sib_stack, *angles)
    return out.reshape(nrec, nsrc, lags)


def shifted(x, axis, count, stride):
    parts = [x]
    for shift in range(1, count // stride):
        pairs = [(j, (j + stride * shift) % count) for j in range(count)]
        parts.append(lax.ppermute(x, axis, perm=pairs))
    return parts


def in_place_stack(parts):
    stack = jnp.zeros((len(parts),) + parts[0].shape, parts[0].dtype)
    for k, part in enumerate(parts):
        stack = lax.dynamic_update_slice_in_dim(stack, part[None], k, axis=0)
    return stack


def local(spectra, valid, rcv_count, src_count):
    channels, windows, _, freqs = spectra.shape
    table = lag_table(freqs, LAGS)
    packed = whiten_pack(spectra, valid)
    rec_stack = shifted(packed, "rcv", rcv_count, 1)
    own_stack = shifted(packed, "src", src_count, 2)
    sibling = [(j, j ^ 1) for j in range(src_count)]
    sib_stack = [lax.ppermute(part, "src", perm=sibling) for part in own_stack]
    table, rec_stack, own_stack, sib_stack = lax.optimization_barrier(
        (table, rec_stack, own_stack, sib_stack)
    )
    rec_stack = in_place_stack(rec_stack)
    own_stack = in_place_stack(own_stack)
    sib_stack = in_place_stack(sib_stack)
    return correlate(rec_stack, own_stack, sib_stack, table, windows, freqs)


def solution(mesh):
    return jax.shard_map(
        functools.partial(local, rcv_count=mesh.shape["rcv"], src_count=mesh.shape["src"]),
        mesh=mesh,
        in_specs=(P(("src", "rcv"), None, None, None), P(("src", "rcv"), None)),
        out_specs=P("src", "rcv", None),
        check_vma=False,
    )
```

```python
import functools
import math

import jax
import jax.numpy as jnp
from jax import lax
from jax.experimental import pallas as pl
from jax.experimental.pallas import tpu as pltpu
from jax.sharding import PartitionSpec as P

LAGS = 512
BAND = 32
NSAMP = 7500
PAD = 128

epsilon = 1e-06


def split3(x):
    hi = x.astype(jnp.bfloat16)
    rest = x - hi.astype(jnp.float32)
    mid = rest.astype(jnp.bfloat16)
    lo = (rest - mid.astype(jnp.float32)).astype(jnp.bfloat16)
    return hi, mid, lo


def exact_dot(x, ones):
    return sum(jnp.dot(part, ones, preferred_element_type=jnp.float32) for part in split3(x))


def whiten_kernel(x_ref, v_ref, out_ref, sq_ref, *, channels, windows, freqs):
    bands = freqs // BAND
    band_of = lax.broadcasted_iota(jnp.int32, (freqs, bands), 0) // BAND
    to_band = (band_of == lax.broadcasted_iota(jnp.int32, (freqs, bands), 1)).astype(jnp.bfloat16)
    band_row = lax.broadcasted_iota(jnp.int32, (bands, freqs), 1) // BAND
    from_band = (band_row == lax.broadcasted_iota(jnp.int32, (bands, freqs), 0)).astype(
        jnp.bfloat16
    )
    for c in range(channels):
        for w in range(windows):
            x = x_ref[c, w].astype(jnp.float32)
            row = c * windows + w
            sq_ref[row : row + 1, :] = x[0:1] ** 2 + x[1:2] ** 2
    power = exact_dot(sq_ref[...], to_band) / (2.0 * BAND)
    factor = exact_dot(1.0 / jnp.sqrt(power + epsilon), from_band)
    width = 2 * freqs
    for c in range(channels):
        for w in range(windows):
            x = x_ref[c, w].astype(jnp.float32)
            row = c * windows + w
            scale = factor[row : row + 1, :]
            out_ref[c : c + 1, w * width : w * width + freqs] = (x[0:1] * scale).astype(
                jnp.bfloat16
            )
            out_ref[c : c + 1, w * width + freqs : (w + 1) * width] = (x[1:2] * scale).astype(
                jnp.bfloat16
            )
    body = windows * width
    valid = v_ref[...].astype(jnp.float32)
    lane = lax.broadcasted_iota(jnp.int32, (channels, PAD), 1)
    tail = jnp.zeros((channels, PAD), jnp.float32)
    for w in range(windows):
        tail = jnp.where(lane == w, valid[:, w : w + 1], tail)
    out_ref[:, body : body + PAD] = tail.astype(jnp.bfloat16)


def whiten_pack(spectra, valid):
    channels, windows, _, freqs = spectra.shape
    kernel = functools.partial(whiten_kernel, channels=channels, windows=windows, freqs=freqs)
    return pl.pallas_call(
        kernel,
        out_shape=jax.ShapeDtypeStruct((channels, windows * 2 * freqs + PAD), jnp.bfloat16),
        scratch_shapes=[pltpu.VMEM((channels * windows, freqs), jnp.float32)],
    )(spectra, valid)


def lag_table(freq_count, lag_count):
    step = 64
    shifts = jnp.arange(lag_count, dtype=jnp.int32) - lag_count // 2
    hi = jnp.arange(freq_count // step, dtype=jnp.int32) * step
    lo = jnp.arange(step, dtype=jnp.int32)
    scale = 2.0 * math.pi / NSAMP
    angle_hi = jnp.mod(hi[:, None] * shifts[None, :], NSAMP).astype(jnp.float32) * scale
    angle_lo = jnp.mod(lo[:, None] * shifts[None, :], NSAMP).astype(jnp.float32) * scale
    cos_hi, sin_hi = jnp.cos(angle_hi)[:, None, :], jnp.sin(angle_hi)[:, None, :]
    cos_lo, sin_lo = jnp.cos(angle_lo)[None, :, :], jnp.sin(angle_lo)[None, :, :]
    factor = 1.0 / math.sqrt(2.0 * freq_count)
    cosines = (cos_hi * cos_lo - sin_hi * sin_lo) * factor
    sines = (sin_hi * cos_lo + cos_hi * sin_lo) * (-factor)
    cosines = cosines.reshape(freq_count, lag_count).astype(jnp.bfloat16)
    sines = sines.reshape(freq_count, lag_count).astype(jnp.bfloat16)
    return jnp.stack([cosines, sines], axis=0).reshape(2 * freq_count, lag_count)


def cross_kernel(
    rec_ref, own_ref, sib_ref, tab_hbm, out_ref, srcf, recf, rtails, stails, cross,
    tab_ref, tab_sem, *, windows, freqs, group, chunk
):
    step = pl.program_id(0)
    rcv_count, per = rec_ref.shape[0], rec_ref.shape[1]
    chips = own_ref.shape[0]
    nsrc = 2 * chips * per
    body = windows * 2 * freqs
    width = 2 * freqs

    def place(block, dst, values, tails, source_side):
        rows = slice(dst * per, (dst + 1) * per)
        mask = block[:, body : body + PAD].astype(jnp.float32)
        tails[rows, :] = mask
        for w in range(windows):
            m = mask[:, w : w + 1]
            a = block[:, w * width : w * width + freqs].astype(jnp.float32) * m
            b = block[:, w * width + freqs : (w + 1) * width].astype(jnp.float32) * m
            if source_side:
                terms = (a, b - a, a + b)
            else:
                terms = (a - b, a, b)
            for t, term in enumerate(terms):
                start = (3 * w + t) * freqs
                values[rows, start : start + freqs] = term

    @pl.when(step == 0)
    def _():
        pltpu.make_async_copy(tab_hbm, tab_ref, tab_sem).start()

    @pl.when(step == 0)
    def _():
        src_index = lax.axis_index("src")
        rcv_index, chip, core = lax.axis_index("rcv"), src_index // 2, src_index % 2
        for rot in range(rcv_count):

            @pl.when(rcv_index == rot)
            def _():
                for dst in range(rcv_count):
                    place(rec_ref[(rot - dst) % rcv_count], dst, recf, rtails, False)

        for rot in range(chips):
            for mine in range(2):

                @pl.when((chip == rot) & (core == mine))
                def _():
                    for zz in range(chips):
                        k = (rot - zz) % chips
                        place(own_ref[k], zz * 2 + mine, srcf, stails, True)
                        place(sib_ref[k], zz * 2 + 1 - mine, srcf, stails, True)

    smask = stails[...]

    def per_receiver(j, carry):
        i = step * group + j
        rtail = rtails[pl.ds(i, 1), :]
        count = jnp.sum(smask * rtail, axis=1, keepdims=True)
        inverse = 1.0 / jnp.maximum(count, 1.0)
        rows = pl.ds(pl.multiple_of(j * nsrc, nsrc), nsrc)
        for c in range(freqs // chunk):
            k1 = jnp.zeros((nsrc, chunk), jnp.float32)
            k2 = jnp.zeros((nsrc, chunk), jnp.float32)
            k3 = jnp.zeros((nsrc, chunk), jnp.float32)
            for w in range(windows):
                at = [(3 * w + t) * freqs + c * chunk for t in range(3)]
                sa = srcf[:, at[0] : at[0] + chunk]
                sd = srcf[:, at[1] : at[1] + chunk]
                se = srcf[:, at[2] : at[2] + chunk]
                ru = recf[pl.ds(i, 1), at[0] : at[0] + chunk]
                ra = recf[pl.ds(i, 1), at[1] : at[1] + chunk]
                rb = recf[pl.ds(i, 1), at[2] : at[2] + chunk]
                k1 = k1 + sa * ru
                k2 = k2 + ra * sd
                k3 = k3 + rb * se
            real = (k1 + k3) * inverse
            imag = (k1 + k2) * inverse
            cross[rows, c * chunk : (c + 1) * chunk] = real.astype(jnp.bfloat16)
            cross[rows, freqs + c * chunk : freqs + (c + 1) * chunk] = imag.astype(jnp.bfloat16)
        return carry

    lax.fori_loop(0, group, per_receiver, 0)

    @pl.when(step == 0)
    def _():
        pltpu.make_async_copy(tab_hbm, tab_ref, tab_sem).wait()

    out_ref[...] = jnp.dot(
        cross[...], tab_ref[...], preferred_element_type=jnp.float32
    ).astype(jnp.bfloat16)


def correlate(rec_stack, own_stack, sib_stack, table, windows, freqs):
    rcv_count, per, width = rec_stack.shape
    chips = own_stack.shape[0]
    nrec = rcv_count * per
    nsrc = 2 * chips * per
    lags = table.shape[1]
    group = nrec if nrec <= 16 else 8
    kernel = functools.partial(
        cross_kernel, windows=windows, freqs=freqs, group=group, chunk=256
    )
    full3 = lambda g: (0, 0, 0)
    out = pl.pallas_call(
        kernel,
        grid_spec=pl.GridSpec(
            grid=(nrec // group,),
            in_specs=[
                pl.BlockSpec(rec_stack.shape, full3),
                pl.BlockSpec(own_stack.shape, full3),
                pl.BlockSpec(sib_stack.shape, full3),
                pl.BlockSpec(memory_space=pl.ANY),
            ],
            out_specs=pl.BlockSpec((group * nsrc, lags), lambda g: (g, 0)),
            scratch_shapes=[
                pltpu.VMEM((nsrc, windows * 3 * freqs), jnp.float32),
                pltpu.VMEM((nrec, windows * 3 * freqs), jnp.float32),
                pltpu.VMEM((nrec, PAD), jnp.float32),
                pltpu.VMEM((nsrc, PAD), jnp.float32),
                pltpu.VMEM((group * nsrc, 2 * freqs), jnp.bfloat16),
                pltpu.VMEM(table.shape, jnp.bfloat16),
                pltpu.SemaphoreType.DMA(()),
            ],
        ),
        out_shape=jax.ShapeDtypeStruct((nrec * nsrc, lags), jnp.bfloat16),
        compiler_params=pltpu.CompilerParams(dimension_semantics=("arbitrary",)),
    )(rec_stack, own_stack, sib_stack, table)
    return out.reshape(nrec, nsrc, lags)


def shifted(x, axis, count, stride):
    parts = [x]
    for shift in range(1, count // stride):
        pairs = [(j, (j + stride * shift) % count) for j in range(count)]
        parts.append(lax.ppermute(x, axis, perm=pairs))
    return parts


def in_place_stack(parts):
    stack = jnp.zeros((len(parts),) + parts[0].shape, parts[0].dtype)
    for k, part in enumerate(parts):
        stack = lax.dynamic_update_slice_in_dim(stack, part[None], k, axis=0)
    return stack


def local(spectra, valid, rcv_count, src_count):
    channels, windows, _, freqs = spectra.shape
    table = lag_table(freqs, LAGS)
    packed = whiten_pack(spectra, valid)
    rec_stack = shifted(packed, "rcv", rcv_count, 1)
    own_stack = shifted(packed, "src", src_count, 2)
    sibling = [(j, j ^ 1) for j in range(src_count)]
    sib_stack = [lax.ppermute(part, "src", perm=sibling) for part in own_stack]
    table, rec_stack, own_stack, sib_stack = lax.optimization_barrier(
        (table, rec_stack, own_stack, sib_stack)
    )
    rec_stack = in_place_stack(rec_stack)
    own_stack = in_place_stack(own_stack)
    sib_stack = in_place_stack(sib_stack)
    return correlate(rec_stack, own_stack, sib_stack, table, windows, freqs)


def solution(mesh):
    return jax.shard_map(
        functools.partial(local, rcv_count=mesh.shape["rcv"], src_count=mesh.shape["src"]),
        mesh=mesh,
        in_specs=(P(("src", "rcv"), None, None, None), P(("src", "rcv"), None)),
        out_specs=P("src", "rcv", None),
        check_vma=False,
    )
```
